32 devices in a mesh: groups: 2 (over y), tm: 4 (over z), comp: 2 (over core), panel: 2 (over x).
Axes of the slice: x: 2, y: 2, z: 4, core: 2. Of those that a mesh axis runs over, the one named last changes fastest.
Arguments:
- orbit_angles: float32 [2, 8192], P(None, ('groups', 'tm')), parts along dimension 1, may hold values from -3.15 to 3.15, as said below
- gap_mask: int32 [8192], P(('groups', 'tm')), parts along dimension 0, may hold values 0 or 1
- column_index: int32 [2, 512], P(None, 'panel'), may hold values from -280 to 280, as said below
- lat_coeffs: bfloat16 [2, 640, 512], P('comp', None, 'panel'), may hold values from -6 to 6
- psd_table: int32 [2, 2049], P('comp'), may hold values from 1024 to 32752, as said below
Outputs:
- normals: float32 [1024, 512], P(('groups', 'tm'), 'panel'), parts along dimension 0
The draws below stay inside these ranges and needn't reach their ends.
There are 2 independent parts, one for each index of `groups`. The reference program is written for one: setup_inputs(seed, part) draws one part's arguments, and reference() takes and returns one part's arrays. A program takes and returns all parts, laid end to end along the dimension named above; an argument that names none is the same for every part. Nothing has to cross between parts.
Inputs may be any that keep to these rules, and one draw needn't show every extreme that they name: orbit_angles holds colatitude in its first row and longitude in its second. `column_index`: the first row holds each unknown's degree, the second its order; a degree is at least 2 and at least the order's magnitude; a negative order stands for the sine term in longitude. `psd_table`: entry g of a component's row is its noise power at frequency g (and 4096 - g), times 8192.
All inputs are finite; a program needn't handle non-finite values. No bound on the sum of `gap_mask` on one device may be relied on, other than what follows from the above.
Results may differ from the reference program's by a relative error of at most 0.0016.
Values may be sent and summed in bfloat16 or wider, within the bound.
No kernel may reach another device: no remote copies, remote signals or barrier semaphores. Data moves between devices by JAX's collectives and lax.ppermute only.
A program may use at most 64 MiB of HBM per device.

```python
import math
import jax
import jax.numpy as jnp
from jax import lax

DEG = 280
KLAT = 320
UNKNOWNS = 512
TIME_DEV = 1024
SAMPLES = 4096
COMPS = 2


def draw_orbit_angles(key, part):
    key_orbit, key_earth, key_node, key_jitter = jax.random.split(key, 4)
    epochs = jnp.arange(SAMPLES, dtype=jnp.int32)
    period = 5383
    incline = 1.6878
    orbit_start = jax.random.randint(key_orbit, (), 0, period)
    earth_start = jax.random.randint(key_earth, (), 0, 86164)
    ascending = jax.random.uniform(key_node, (), jnp.float32, -math.pi, math.pi)
    lat_argument = ((epochs + orbit_start) % period).astype(jnp.float32) * (2.0 * math.pi / period)
    earth_turn = ((epochs + earth_start) % 86164).astype(jnp.float32) * (2.0 * math.pi / 86164.0)
    colatitude = jnp.arccos(jnp.sin(incline) * jnp.sin(lat_argument))
    colatitude = colatitude + 0.002 * jax.random.normal(key_jitter, (SAMPLES,), jnp.float32)
    raw_lon = ascending - earth_turn + jnp.arctan2(jnp.cos(incline) * jnp.sin(lat_argument), jnp.cos(lat_argument))
    longitude = jnp.arctan2(jnp.sin(raw_lon), jnp.cos(raw_lon))
    return jnp.stack([colatitude, longitude]).astype(jnp.float32)


def draw_column_index(key, part):
    key_order, key_degree, key_pick = jax.random.split(key, 3)
    orders = jax.random.randint(key_order, (UNKNOWNS,), -DEG, DEG + 1)
    lowest = jnp.maximum(jnp.abs(orders), 2)
    spans = DEG + 1 - lowest
    degree = lowest + jax.random.randint(key_degree, (UNKNOWNS,), 0, 1048576) % spans
    picked = jax.random.permutation(key_pick, UNKNOWNS)
    orders = orders.at[picked[0]].set(DEG).at[picked[1]].set(-DEG)
    degree = degree.at[picked[0]].set(DEG).at[picked[1]].set(DEG)
    return jnp.stack([degree, orders]).astype(jnp.int32)


def draw_psd_table(key, part):
    key_mant, key_expo = jax.random.split(key)
    grid_shape = (COMPS, SAMPLES // 2 + 1)
    mantissa = jax.random.randint(key_mant, grid_shape, 1024, 2048)
    exponent = jax.random.randint(key_expo, grid_shape, 0, 5)
    return jnp.left_shift(mantissa, exponent).astype(jnp.int32)


def set_ends(result, own_key, smallest, largest):
    longest = result.shape.index(max(result.shape))
    spots = []
    for shift in (0, 1):
        where = [jax.random.randint(jax.random.fold_in(own_key, axis), (), 0, length) for axis, length in enumerate(result.shape)]
        where[longest] = (where[longest] + shift) % result.shape[longest]
        spots.append(tuple(where))
    return result.at[spots[0]].set(smallest).at[spots[1]].set(largest)


def shard_levels(rng, dims, pieces, low, high):
    factor_of = 1.0
    for axis_at, shards_of in pieces:
        heights = jax.random.uniform(jax.random.fold_in(jax.random.fold_in(rng, 6), axis_at), (shards_of,), jnp.float32, low / len(pieces), high / len(pieces))
        factor_of = factor_of * jnp.repeat(jnp.exp(heights), dims[axis_at] // shards_of).reshape((-1,) + (1,) * (len(dims) - 1 - axis_at))
    return factor_of


def bell_draw(own_key, extent, deviation, reach, cuts=(), held_as=jnp.bfloat16):
    level = shard_levels(own_key, extent, cuts, -0.22, 0.18) if cuts else 1.0
    result = jax.random.normal(own_key, extent, jnp.float32) * deviation * level
    return jnp.minimum(jnp.maximum(result, -reach), reach).astype(held_as)


def setup_inputs(seed: int = 0, part: int = 0) -> dict:
    keys = jax.random.split(jax.random.key(seed), 6)
    own_keys = jax.random.split(jax.random.fold_in(keys[5], part), 6)
    orbit_angles = draw_orbit_angles(jax.random.fold_in(jax.random.fold_in(keys[5], part), 71), part)
    gap_mask = set_ends((jax.random.randint(own_keys[1], (SAMPLES,), 0, 16) < 15).astype(jnp.int32), jax.random.fold_in(own_keys[1], 1), 0, 1)
    column_index = draw_column_index(jax.random.fold_in(keys[5], 71), part)
    lat_coeffs = bell_draw(keys[3], (COMPS, 2 * KLAT, UNKNOWNS), 1.0, 6.0, ((0, 2), (2, 2)))
    psd_table = draw_psd_table(jax.random.fold_in(keys[5], 71), part)
    return dict(orbit_angles=orbit_angles, gap_mask=gap_mask, column_index=column_index, lat_coeffs=lat_coeffs, psd_table=psd_table)


def synthesize(angles, keep_rows, column_index, coeffs):
    terms_lat = coeffs.shape[0] // 2
    colatitude = angles[0]
    longit = angles[1]
    wavenumbers = jnp.arange(terms_lat, dtype=jnp.float32)
    phases = colatitude[:, None] * wavenumbers[None, :]
    basis_rows = jnp.concatenate([jnp.cos(phases), jnp.sin(phases)], axis=1).astype(jnp.bfloat16)
    degree = column_index[0]
    orders = column_index[1]
    levels = jnp.arange(2 * terms_lat, dtype=jnp.int32) % terms_lat
    allowed = levels[:, None] <= degree[None, :]
    masked = jnp.where(allowed, coeffs, jnp.zeros_like(coeffs))
    latitude = jnp.dot(basis_rows, masked, preferred_element_type=jnp.float32)
    lon_phase = longit[:, None] * jnp.abs(orders).astype(jnp.float32)[None, :]
    lon_wave = jnp.where(orders[None, :] >= 0, jnp.cos(lon_phase), jnp.sin(lon_phase))
    norm_scale = 1.0 / jnp.sqrt(degree.astype(jnp.float32) + 1.0)
    return latitude * lon_wave * (keep_rows[:, None] * norm_scale[None, :])

def reference(orbit_angles, gap_mask, column_index, lat_coeffs, psd_table):
    samples = orbit_angles.shape[1]
    keep_rows = gap_mask.astype(jnp.float32)
    frequency = jnp.arange(samples, dtype=jnp.int32)
    folded = jnp.minimum(frequency, samples - frequency)
    starts = jnp.arange(samples // TIME_DEV, dtype=jnp.int32) * TIME_DEV
    normals = jnp.zeros((UNKNOWNS, UNKNOWNS), jnp.float32)
    for comp_index in range(COMPS):
        coeffs = lat_coeffs[comp_index]

        def block_design(start_row):
            angles = lax.dynamic_slice_in_dim(orbit_angles, start_row, TIME_DEV, 1)
            keep_part = lax.dynamic_slice_in_dim(keep_rows, start_row, TIME_DEV, 0)
            return synthesize(angles, keep_part, column_index, coeffs)
        design = lax.map(block_design, starts).reshape(samples, UNKNOWNS)
        spectrum = jnp.fft.fft(design, axis=0) / samples
        spec_real = jnp.real(spectrum).astype(jnp.bfloat16)
        spec_imag = jnp.imag(spectrum).astype(jnp.bfloat16)
        inverse_psd = 8192.0 / psd_table[comp_index][folded].astype(jnp.float32)
        weighted_real = (spec_real.astype(jnp.float32) * inverse_psd[:, None]).astype(jnp.bfloat16)
        weighted_imag = (spec_imag.astype(jnp.float32) * inverse_psd[:, None]).astype(jnp.bfloat16)
        normals = normals + jnp.dot(spec_real.T, weighted_real, preferred_element_type=jnp.float32)
        normals = normals + jnp.dot(spec_imag.T, weighted_imag, preferred_element_type=jnp.float32)
    return normals
```

```python
import math

import jax
import jax.numpy as jnp
from jax import lax
from jax.sharding import PartitionSpec as P

SPLIT = 64


def synthesize(angles, keep_rows, column_index, coeffs):
    terms_lat = coeffs.shape[0] // 2
    colatitude = angles[0]
    longit = angles[1]
    wavenumbers = jnp.arange(terms_lat, dtype=jnp.float32)
    phases = colatitude[:, None] * wavenumbers[None, :]
    basis_rows = jnp.concatenate([jnp.cos(phases), jnp.sin(phases)], axis=1).astype(jnp.bfloat16)
    degree = column_index[0]
    orders = column_index[1]
    levels = jnp.arange(2 * terms_lat, dtype=jnp.int32) % terms_lat
    allowed = levels[:, None] <= degree[None, :]
    masked = jnp.where(allowed, coeffs, jnp.zeros_like(coeffs))
    latitude = jnp.dot(basis_rows, masked, preferred_element_type=jnp.float32)
    lon_phase = longit[:, None] * jnp.abs(orders).astype(jnp.float32)[None, :]
    lon_wave = jnp.where(orders[None, :] >= 0, jnp.cos(lon_phase), jnp.sin(lon_phase))
    norm_scale = 1.0 / jnp.sqrt(degree.astype(jnp.float32) + 1.0)
    return latitude * lon_wave * (keep_rows[:, None] * norm_scale[None, :])


def phase_tables(row_index, col_index, length):
    product = row_index[:, None] * col_index[None, :] % length
    angle_grid = product.astype(jnp.float32) * (2.0 * math.pi / length)
    return (jnp.cos(angle_grid), jnp.sin(angle_grid))


def dft_tables(length):
    indices = jnp.arange(length, dtype=jnp.int32)
    return phase_tables(indices, indices, length)


def rotate(real_part, imag_part, outer_index, inner_index, length):
    index_grid = outer_index[:, None] * inner_index[None, :] % length
    angle_grid = index_grid.astype(jnp.float32) * (2.0 * math.pi / length)
    cosine = jnp.cos(angle_grid)[:, :, None]
    sine_grid = jnp.sin(angle_grid)[:, :, None]
    return (real_part * cosine + imag_part * sine_grid, imag_part * cosine - real_part * sine_grid)


def precise_dot(left_side, right_side):
    return jnp.dot(
        left_side, right_side, precision=lax.Precision.HIGHEST, preferred_element_type=jnp.float32
    )


def transform(cos_table, sin_table, real_part, imag_part):
    new_real = precise_dot(cos_table, real_part) + precise_dot(sin_table, imag_part)
    new_imag = precise_dot(cos_table, imag_part) - precise_dot(sin_table, real_part)
    return (new_real, new_imag)


def four_step(real_in, imag_in, samples):
    length = real_in.shape[0]
    columns = real_in.shape[1]
    outer_count = SPLIT
    inner_count = length // SPLIT
    real_part = real_in.reshape(outer_count, inner_count * columns)
    imag_part = imag_in.reshape(outer_count, inner_count * columns)
    cos_outer, sin_outer = dft_tables(outer_count)
    real_part, imag_part = transform(cos_outer, sin_outer, real_part, imag_part)
    real_part = real_part.reshape(outer_count, inner_count, columns)
    imag_part = imag_part.reshape(outer_count, inner_count, columns)
    real_part, imag_part = rotate(
        real_part,
        imag_part,
        jnp.arange(outer_count, dtype=jnp.int32),
        jnp.arange(inner_count, dtype=jnp.int32),
        length,
    )
    real_part = jnp.transpose(real_part, (1, 0, 2)).reshape(inner_count, outer_count * columns)
    imag_part = jnp.transpose(imag_part, (1, 0, 2)).reshape(inner_count, outer_count * columns)
    cos_inner, sin_inner = dft_tables(inner_count)
    real_part, imag_part = transform(cos_inner, sin_inner, real_part, imag_part)
    return (
        real_part.reshape(length, columns) / samples,
        imag_part.reshape(length, columns) / samples,
    )


def local_transform(received, samples):
    real_part, imag_part = four_step(received[0, 0], received[1, 0], samples)
    return (real_part.astype(jnp.bfloat16), imag_part.astype(jnp.bfloat16))


def inverse_weights(psd_row, position, devices_tm, epochs, samples):
    half = samples // 2
    mirrored = jnp.concatenate([psd_row[: half + 1], psd_row[1:half][::-1]])
    picked = lax.dynamic_slice_in_dim(mirrored.reshape(epochs, devices_tm), position, 1, axis=1)
    return 8192.0 / picked[:, 0].astype(jnp.float32)


def panel_spectra(spectra):
    panels = lax.axis_size("panel")
    blocks = [spectra]
    for shift in range(1, panels):
        pairs = [(src, (src + shift) % panels) for src in range(panels)]
        blocks.append(lax.ppermute(spectra, "panel", pairs))
    return blocks


def comp_sum(value):
    comps = lax.axis_size("comp")
    if comps == 1:
        return value
    if comps != 2:
        return lax.psum(value, "comp")
    other = lax.ppermute(value, "comp", [(0, 1), (1, 0)])
    return value + other


def body(orbit_angles, gap_mask, column_index, lat_coeffs, psd_table):
    devices_tm = lax.axis_size("tm")
    panels = lax.axis_size("panel")
    epochs = orbit_angles.shape[1]
    block_len = epochs // devices_tm
    samples = epochs * devices_tm
    columns = lat_coeffs.shape[2]
    coeffs = lat_coeffs[0]
    keep_rows = gap_mask.astype(jnp.float32)
    packed = jnp.concatenate([orbit_angles, keep_rows[None]], axis=0)
    packed = packed.reshape(3, devices_tm, block_len).transpose(1, 0, 2)
    received = lax.all_to_all(packed, "tm", 0, 0, tiled=True)
    flat_orbit = received.transpose(1, 0, 2).reshape(3, devices_tm * block_len)
    spread = synthesize(flat_orbit[0:2], flat_orbit[2], column_index, coeffs).reshape(
        devices_tm, block_len, columns
    )
    position = lax.axis_index("tm")
    local_epoch = position * block_len + jnp.arange(block_len, dtype=jnp.int32)
    cos_outer, sin_outer = dft_tables(devices_tm)
    flat_design = spread.reshape(devices_tm, block_len * columns)
    real_part = precise_dot(cos_outer, flat_design).reshape(devices_tm, block_len, columns)
    imag_part = -precise_dot(sin_outer, flat_design).reshape(devices_tm, block_len, columns)
    real_part, imag_part = rotate(
        real_part, imag_part, jnp.arange(devices_tm, dtype=jnp.int32), local_epoch, samples
    )
    twisted = jnp.stack([real_part, imag_part], axis=1)
    gathered = lax.all_to_all(twisted, "tm", 0, 0, tiled=True)
    gathered = gathered.transpose(1, 0, 2, 3).reshape(2, devices_tm * block_len, columns)
    real_part, imag_part = four_step(gathered[0], gathered[1], samples)
    spectra = jnp.stack([real_part.astype(jnp.bfloat16), imag_part.astype(jnp.bfloat16)])
    inverse_psd = inverse_weights(psd_table[0], position, devices_tm, epochs, samples)
    weighted = (spectra.astype(jnp.float32) * inverse_psd[None, :, None]).astype(jnp.bfloat16)
    contract = (((0, 1), (0, 1)), ((), ()))
    products = [
        lax.dot_general(block, weighted, contract, preferred_element_type=jnp.float32)
        for block in panel_spectra(spectra)
    ]
    by_shift = jnp.stack(products)
    panel = lax.axis_index("panel")
    order = (panel - jnp.arange(panels, dtype=jnp.int32)) % panels
    partial_value = jnp.take(by_shift, order, axis=0).reshape(panels * columns, columns)
    rows = partial_value.shape[0] // devices_tm
    pieces = lax.all_to_all(
        partial_value.reshape(devices_tm, rows, columns), "tm", 0, 0, tiled=True
    )
    return comp_sum(jnp.sum(pieces, axis=0))


def solution(mesh):
    return jax.shard_map(
        body,
        mesh=mesh,
        in_specs=(
            P(None, ("groups", "tm")),
            P(("groups", "tm")),
            P(None, "panel"),
            P("comp", None, "panel"),
            P("comp", None),
        ),
        out_specs=P(("groups", "tm"), "panel"),
        check_vma=False,
    )
```

```python
import math

import jax
import jax.numpy as jnp
from jax import lax
from jax.sharding import PartitionSpec as P

SPLIT = 64
CHUNKS = 2


def synthesize(angles, keep_rows, column_index, coeffs):
    terms_lat = coeffs.shape[0] // 2
    colatitude = angles[0]
    longit = angles[1]
    wavenumbers = jnp.arange(terms_lat, dtype=jnp.float32)
    phases = colatitude[:, None] * wavenumbers[None, :]
    basis_rows = jnp.concatenate([jnp.cos(phases), jnp.sin(phases)], axis=1).astype(jnp.bfloat16)
    degree = column_index[0]
    orders = column_index[1]
    levels = jnp.arange(2 * terms_lat, dtype=jnp.int32) % terms_lat
    allowed = levels[:, None] <= degree[None, :]
    masked = jnp.where(allowed, coeffs, jnp.zeros_like(coeffs))
    latitude = jnp.dot(basis_rows, masked, preferred_element_type=jnp.float32)
    lon_phase = longit[:, None] * jnp.abs(orders).astype(jnp.float32)[None, :]
    lon_wave = jnp.where(orders[None, :] >= 0, jnp.cos(lon_phase), jnp.sin(lon_phase))
    norm_scale = 1.0 / jnp.sqrt(degree.astype(jnp.float32) + 1.0)
    return latitude * lon_wave * (keep_rows[:, None] * norm_scale[None, :])


def phase_tables(row_index, col_index, length):
    product = row_index[:, None] * col_index[None, :] % length
    angle_grid = product.astype(jnp.float32) * (2.0 * math.pi / length)
    return (jnp.cos(angle_grid), jnp.sin(angle_grid))


def dft_tables(length):
    indices = jnp.arange(length, dtype=jnp.int32)
    return phase_tables(indices, indices, length)


def rotate(real_part, imag_part, outer_index, inner_index, length):
    index_grid = outer_index[:, None] * inner_index[None, :] % length
    angle_grid = index_grid.astype(jnp.float32) * (2.0 * math.pi / length)
    cosine = jnp.cos(angle_grid)[:, :, None]
    sine_grid = jnp.sin(angle_grid)[:, :, None]
    return (real_part * cosine + imag_part * sine_grid, imag_part * cosine - real_part * sine_grid)


def precise_dot(left_side, right_side):
    return jnp.dot(
        left_side, right_side, precision=lax.Precision.HIGHEST, preferred_element_type=jnp.float32
    )


def transform(cos_table, sin_table, real_part, imag_part):
    new_real = precise_dot(cos_table, real_part) + precise_dot(sin_table, imag_part)
    new_imag = precise_dot(cos_table, imag_part) - precise_dot(sin_table, real_part)
    return (new_real, new_imag)


def four_step(real_in, imag_in, samples):
    length = real_in.shape[0]
    columns = real_in.shape[1]
    outer_count = SPLIT
    inner_count = length // SPLIT
    real_part = real_in.reshape(outer_count, inner_count * columns)
    imag_part = imag_in.reshape(outer_count, inner_count * columns)
    cos_outer, sin_outer = dft_tables(outer_count)
    real_part, imag_part = transform(cos_outer, sin_outer, real_part, imag_part)
    real_part = real_part.reshape(outer_count, inner_count, columns)
    imag_part = imag_part.reshape(outer_count, inner_count, columns)
    real_part, imag_part = rotate(
        real_part,
        imag_part,
        jnp.arange(outer_count, dtype=jnp.int32),
        jnp.arange(inner_count, dtype=jnp.int32),
        length,
    )
    real_part = jnp.transpose(real_part, (1, 0, 2)).reshape(inner_count, outer_count * columns)
    imag_part = jnp.transpose(imag_part, (1, 0, 2)).reshape(inner_count, outer_count * columns)
    cos_inner, sin_inner = dft_tables(inner_count)
    real_part, imag_part = transform(cos_inner, sin_inner, real_part, imag_part)
    return (
        real_part.reshape(length, columns) / samples,
        imag_part.reshape(length, columns) / samples,
    )


def local_transform(received, samples):
    real_part, imag_part = four_step(received[0, 0], received[1, 0], samples)
    return (real_part.astype(jnp.bfloat16), imag_part.astype(jnp.bfloat16))


def inverse_weights(psd_row, position, devices_tm, epochs, samples):
    half = samples // 2
    mirrored = jnp.concatenate([psd_row[: half + 1], psd_row[1:half][::-1]])
    picked = lax.dynamic_slice_in_dim(mirrored.reshape(epochs, devices_tm), position, 1, axis=1)
    return 8192.0 / picked[:, 0].astype(jnp.float32)


def panel_spectra(spectra):
    panels = lax.axis_size("panel")
    blocks = [spectra]
    for shift in range(1, panels):
        pairs = [(src, (src + shift) % panels) for src in range(panels)]
        blocks.append(lax.ppermute(spectra, "panel", pairs))
    return blocks


def comp_sum(value):
    comps = lax.axis_size("comp")
    if comps == 1:
        return value
    if comps != 2:
        return lax.psum(value, "comp")
    other = lax.ppermute(value, "comp", [(0, 1), (1, 0)])
    return value + other


def chunk_spectra(flat_orbit, column_index, coeffs, position, samples):
    devices_tm = lax.axis_size("tm")
    block_len = flat_orbit.shape[1] // devices_tm
    columns = coeffs.shape[1]
    spread = synthesize(flat_orbit[0:2], flat_orbit[2], column_index, coeffs).reshape(
        devices_tm, block_len, columns
    )
    local_epoch = position * block_len + jnp.arange(block_len, dtype=jnp.int32)
    cos_outer, sin_outer = dft_tables(devices_tm)
    flat_design = spread.reshape(devices_tm, block_len * columns)
    real_part = precise_dot(cos_outer, flat_design).reshape(devices_tm, block_len, columns)
    imag_part = -precise_dot(sin_outer, flat_design).reshape(devices_tm, block_len, columns)
    real_part, imag_part = rotate(
        real_part, imag_part, jnp.arange(devices_tm, dtype=jnp.int32), local_epoch, samples
    )
    twisted = jnp.stack([real_part, imag_part], axis=1)
    gathered = lax.all_to_all(twisted, "tm", 0, 0, tiled=True)
    gathered = gathered.transpose(1, 0, 2, 3).reshape(2, devices_tm * block_len, columns)
    real_part, imag_part = four_step(gathered[0], gathered[1], samples)
    return jnp.stack([real_part.astype(jnp.bfloat16), imag_part.astype(jnp.bfloat16)])


def body(orbit_angles, gap_mask, column_index, lat_coeffs, psd_table):
    devices_tm = lax.axis_size("tm")
    panels = lax.axis_size("panel")
    epochs = orbit_angles.shape[1]
    block_len = epochs // devices_tm
    samples = epochs * devices_tm
    columns = lat_coeffs.shape[2]
    coeffs = lat_coeffs[0]
    keep_rows = gap_mask.astype(jnp.float32)
    packed = jnp.concatenate([orbit_angles, keep_rows[None]], axis=0)
    packed = packed.reshape(3, devices_tm, block_len).transpose(1, 0, 2)
    received = lax.all_to_all(packed, "tm", 0, 0, tiled=True)
    flat_orbit = received.transpose(1, 0, 2).reshape(3, devices_tm * block_len)
    position = lax.axis_index("tm")
    inverse_psd = inverse_weights(psd_table[0], position, devices_tm, epochs, samples)
    chunks = CHUNKS if columns % (CHUNKS * 64) == 0 else 1
    width = columns // chunks
    spectra_parts = []
    moved_parts = []
    weighted_parts = []
    for chunk in range(chunks):
        cols = slice(chunk * width, (chunk + 1) * width)
        spectra = chunk_spectra(
            flat_orbit, column_index[:, cols], coeffs[:, cols], position, samples
        )
        weighted_parts.append(
            (spectra.astype(jnp.float32) * inverse_psd[None, :, None]).astype(jnp.bfloat16)
        )
        spectra_parts.append(spectra)
        moved_parts.append(panel_spectra(spectra))
    weighted = jnp.concatenate(weighted_parts, axis=2)
    contract = (((0, 1), (0, 1)), ((), ()))
    by_shift = jnp.stack(
        [
            jnp.concatenate(
                [
                    lax.dot_general(
                        moved_parts[chunk][shift], weighted, contract,
                        preferred_element_type=jnp.float32,
                    )
                    for chunk in range(chunks)
                ],
                axis=0,
            )
            for shift in range(panels)
        ]
    )
    panel = lax.axis_index("panel")
    order = (panel - jnp.arange(panels, dtype=jnp.int32)) % panels
    partial_value = jnp.take(by_shift, order, axis=0).reshape(panels * columns, columns)
    rows = partial_value.shape[0] // devices_tm
    pieces = lax.all_to_all(
        partial_value.reshape(devices_tm, rows, columns), "tm", 0, 0, tiled=True
    )
    return comp_sum(jnp.sum(pieces, axis=0))


def solution(mesh):
    return jax.shard_map(
        body,
        mesh=mesh,
        in_specs=(
            P(None, ("groups", "tm")),
            P(("groups", "tm")),
            P(None, "panel"),
            P("comp", None, "panel"),
            P("comp", None),
        ),
        out_specs=P(("groups", "tm"), "panel"),
        check_vma=False,
    )
```

```python
import math

import jax
import jax.numpy as jnp
from jax import lax
from jax.sharding import PartitionSpec as P

SPLIT = 64
CHUNKS = 4


def synthesize(angles, keep_rows, column_index, coeffs):
    terms_lat = coeffs.shape[0] // 2
    colatitude = angles[0]
    longit = angles[1]
    wavenumbers = jnp.arange(terms_lat, dtype=jnp.float32)
    phases = colatitude[:, None] * wavenumbers[None, :]
    basis_rows = jnp.concatenate([jnp.cos(phases), jnp.sin(phases)], axis=1).astype(jnp.bfloat16)
    degree = column_index[0]
    orders = column_index[1]
    levels = jnp.arange(2 * terms_lat, dtype=jnp.int32) % terms_lat
    allowed = levels[:, None] <= degree[None, :]
    masked = jnp.where(allowed, coeffs, jnp.zeros_like(coeffs))
    latitude = jnp.dot(basis_rows, masked, preferred_element_type=jnp.float32)
    lon_phase = longit[:, None] * jnp.abs(orders).astype(jnp.float32)[None, :]
    lon_wave = jnp.where(orders[None, :] >= 0, jnp.cos(lon_phase), jnp.sin(lon_phase))
    norm_scale = 1.0 / jnp.sqrt(degree.astype(jnp.float32) + 1.0)
    return latitude * lon_wave * (keep_rows[:, None] * norm_scale[None, :])


def phase_tables(row_index, col_index, length):
    product = row_index[:, None] * col_index[None, :] % length
    angle_grid = product.astype(jnp.float32) * (2.0 * math.pi / length)
    return (jnp.cos(angle_grid), jnp.sin(angle_grid))


def dft_tables(length):
    indices = jnp.arange(length, dtype=jnp.int32)
    return phase_tables(indices, indices, length)


def rotate(real_part, imag_part, outer_index, inner_index, length):
    index_grid = outer_index[:, None] * inner_index[None, :] % length
    angle_grid = index_grid.astype(jnp.float32) * (2.0 * math.pi / length)
    cosine = jnp.cos(angle_grid)[:, :, None]
    sine_grid = jnp.sin(angle_grid)[:, :, None]
    return (real_part * cosine + imag_part * sine_grid, imag_part * cosine - real_part * sine_grid)


def precise_dot(left_side, right_side):
    return jnp.dot(
        left_side, right_side, precision=lax.Precision.HIGHEST, preferred_element_type=jnp.float32
    )


def transform(cos_table, sin_table, real_part, imag_part):
    new_real = precise_dot(cos_table, real_part) + precise_dot(sin_table, imag_part)
    new_imag = precise_dot(cos_table, imag_part) - precise_dot(sin_table, real_part)
    return (new_real, new_imag)


def four_step(real_in, imag_in, samples):
    length = real_in.shape[0]
    columns = real_in.shape[1]
    outer_count = SPLIT
    inner_count = length // SPLIT
    real_part = real_in.reshape(outer_count, inner_count * columns)
    imag_part = imag_in.reshape(outer_count, inner_count * columns)
    cos_outer, sin_outer = dft_tables(outer_count)
    real_part, imag_part = transform(cos_outer, sin_outer, real_part, imag_part)
    real_part = real_part.reshape(outer_count, inner_count, columns)
    imag_part = imag_part.reshape(outer_count, inner_count, columns)
    real_part, imag_part = rotate(
        real_part,
        imag_part,
        jnp.arange(outer_count, dtype=jnp.int32),
        jnp.arange(inner_count, dtype=jnp.int32),
        length,
    )
    real_part = jnp.transpose(real_part, (1, 0, 2)).reshape(inner_count, outer_count * columns)
    imag_part = jnp.transpose(imag_part, (1, 0, 2)).reshape(inner_count, outer_count * columns)
    cos_inner, sin_inner = dft_tables(inner_count)
    real_part, imag_part = transform(cos_inner, sin_inner, real_part, imag_part)
    return (
        real_part.reshape(length, columns) / samples,
        imag_part.reshape(length, columns) / samples,
    )


def local_transform(received, samples):
    real_part, imag_part = four_step(received[0, 0], received[1, 0], samples)
    return (real_part.astype(jnp.bfloat16), imag_part.astype(jnp.bfloat16))


def inverse_weights(psd_row, position, devices_tm, epochs, samples):
    half = samples // 2
    mirrored = jnp.concatenate([psd_row[: half + 1], psd_row[1:half][::-1]])
    picked = lax.dynamic_slice_in_dim(mirrored.reshape(epochs, devices_tm), position, 1, axis=1)
    return 8192.0 / picked[:, 0].astype(jnp.float32)


def panel_spectra(spectra):
    panels = lax.axis_size("panel")
    blocks = [spectra]
    for shift in range(1, panels):
        pairs = [(src, (src + shift) % panels) for src in range(panels)]
        blocks.append(lax.ppermute(spectra, "panel", pairs))
    return blocks


def comp_sum(value):
    comps = lax.axis_size("comp")
    if comps == 1:
        return value
    if comps != 2:
        return lax.psum(value, "comp")
    other = lax.ppermute(value, "comp", [(0, 1), (1, 0)])
    return value + other


def chunk_spectra(flat_orbit, column_index, coeffs, position, samples):
    devices_tm = lax.axis_size("tm")
    block_len = flat_orbit.shape[1] // devices_tm
    columns = coeffs.shape[1]
    spread = synthesize(flat_orbit[0:2], flat_orbit[2], column_index, coeffs).reshape(
        devices_tm, block_len, columns
    )
    local_epoch = position * block_len + jnp.arange(block_len, dtype=jnp.int32)
    cos_outer, sin_outer = dft_tables(devices_tm)
    flat_design = spread.reshape(devices_tm, block_len * columns)
    real_part = precise_dot(cos_outer, flat_design).reshape(devices_tm, block_len, columns)
    imag_part = -precise_dot(sin_outer, flat_design).reshape(devices_tm, block_len, columns)
    real_part, imag_part = rotate(
        real_part, imag_part, jnp.arange(devices_tm, dtype=jnp.int32), local_epoch, samples
    )
    twisted = jnp.stack([real_part, imag_part], axis=1)
    gathered = lax.all_to_all(twisted, "tm", 0, 0, tiled=True)
    gathered = gathered.transpose(1, 0, 2, 3).reshape(2, devices_tm * block_len, columns)
    real_part, imag_part = four_step(gathered[0], gathered[1], samples)
    return jnp.stack([real_part.astype(jnp.bfloat16), imag_part.astype(jnp.bfloat16)])


def body(orbit_angles, gap_mask, column_index, lat_coeffs, psd_table):
    devices_tm = lax.axis_size("tm")
    panels = lax.axis_size("panel")
    epochs = orbit_angles.shape[1]
    block_len = epochs // devices_tm
    samples = epochs * devices_tm
    columns = lat_coeffs.shape[2]
    coeffs = lat_coeffs[0]
    keep_rows = gap_mask.astype(jnp.float32)
    packed = jnp.concatenate([orbit_angles, keep_rows[None]], axis=0)
    packed = packed.reshape(3, devices_tm, block_len).transpose(1, 0, 2)
    received = lax.all_to_all(packed, "tm", 0, 0, tiled=True)
    flat_orbit = received.transpose(1, 0, 2).reshape(3, devices_tm * block_len)
    position = lax.axis_index("tm")
    inverse_psd = inverse_weights(psd_table[0], position, devices_tm, epochs, samples)
    chunks = CHUNKS if columns % (CHUNKS * 64) == 0 else 1
    width = columns // chunks
    spectra_parts = []
    moved_parts = []
    weighted_parts = []
    for chunk in range(chunks):
        cols = slice(chunk * width, (chunk + 1) * width)
        spectra = chunk_spectra(
            flat_orbit, column_index[:, cols], coeffs[:, cols], position, samples
        )
        weighted_parts.append(
            (spectra.astype(jnp.float32) * inverse_psd[None, :, None]).astype(jnp.bfloat16)
        )
        spectra_parts.append(spectra)
        moved_parts.append(panel_spectra(spectra))
    weighted = jnp.concatenate(weighted_parts, axis=2)
    contract = (((0, 1), (0, 1)), ((), ()))
    by_shift = jnp.stack(
        [
            jnp.concatenate(
                [
                    lax.dot_general(
                        moved_parts[chunk][shift], weighted, contract,
                        preferred_element_type=jnp.float32,
                    )
                    for chunk in range(chunks)
                ],
                axis=0,
            )
            for shift in range(panels)
        ]
    )
    panel = lax.axis_index("panel")
    order = (panel - jnp.arange(panels, dtype=jnp.int32)) % panels
    partial_value = jnp.take(by_shift, order, axis=0).reshape(panels * columns, columns)
    rows = partial_value.shape[0] // devices_tm
    pieces = lax.all_to_all(
        partial_value.reshape(devices_tm, rows, columns), "tm", 0, 0, tiled=True
    )
    return comp_sum(jnp.sum(pieces, axis=0))


def solution(mesh):
    return jax.shard_map(
        body,
        mesh=mesh,
        in_specs=(
            P(None, ("groups", "tm")),
            P(("groups", "tm")),
            P(None, "panel"),
            P("comp", None, "panel"),
            P("comp", None),
        ),
        out_specs=P(("groups", "tm"), "panel"),
        check_vma=False,
    )
```

```python
import math

import jax
import jax.numpy as jnp
from jax import lax
from jax.sharding import PartitionSpec as P

SPLIT = 64


def synthesize(angles, keep_rows, column_index, coeffs):
    terms_lat = coeffs.shape[0] // 2
    colatitude = angles[0]
    longit = angles[1]
    wavenumbers = jnp.arange(terms_lat, dtype=jnp.float32)
    phases = colatitude[:, None] * wavenumbers[None, :]
    basis_rows = jnp.concatenate([jnp.cos(phases), jnp.sin(phases)], axis=1).astype(jnp.bfloat16)
    degree = column_index[0]
    orders = column_index[1]
    levels = jnp.arange(2 * terms_lat, dtype=jnp.int32) % terms_lat
    allowed = levels[:, None] <= degree[None, :]
    masked = jnp.where(allowed, coeffs, jnp.zeros_like(coeffs))
    latitude = jnp.dot(basis_rows, masked, preferred_element_type=jnp.float32)
    lon_phase = longit[:, None] * jnp.abs(orders).astype(jnp.float32)[None, :]
    lon_wave = jnp.where(orders[None, :] >= 0, jnp.cos(lon_phase), jnp.sin(lon_phase))
    norm_scale = 1.0 / jnp.sqrt(degree.astype(jnp.float32) + 1.0)
    return latitude * lon_wave * (keep_rows[:, None] * norm_scale[None, :])


def phase_tables(row_index, col_index, length):
    product = row_index[:, None] * col_index[None, :] % length
    angle_grid = product.astype(jnp.float32) * (2.0 * math.pi / length)
    return (jnp.cos(angle_grid), jnp.sin(angle_grid))


def dft_tables(length):
    indices = jnp.arange(length, dtype=jnp.int32)
    return phase_tables(indices, indices, length)


def rotate(real_part, imag_part, outer_index, inner_index, length):
    index_grid = outer_index[:, None] * inner_index[None, :] % length
    angle_grid = index_grid.astype(jnp.float32) * (2.0 * math.pi / length)
    cosine = jnp.cos(angle_grid)[:, :, None]
    sine_grid = jnp.sin(angle_grid)[:, :, None]
    return (real_part * cosine + imag_part * sine_grid, imag_part * cosine - real_part * sine_grid)


def precise_dot(left_side, right_side):
    return jnp.dot(
        left_side, right_side, precision=lax.Precision.HIGHEST, preferred_element_type=jnp.float32
    )


def transform(cos_table, sin_table, real_part, imag_part):
    new_real = precise_dot(cos_table, real_part) + precise_dot(sin_table, imag_part)
    new_imag = precise_dot(cos_table, imag_part) - precise_dot(sin_table, real_part)
    return (new_real, new_imag)


def four_step(real_in, imag_in, samples):
    length = real_in.shape[0]
    columns = real_in.shape[1]
    outer_count = SPLIT
    inner_count = length // SPLIT
    real_part = real_in.reshape(outer_count, inner_count * columns)
    imag_part = imag_in.reshape(outer_count, inner_count * columns)
    cos_outer, sin_outer = dft_tables(outer_count)
    real_part, imag_part = transform(cos_outer, sin_outer, real_part, imag_part)
    real_part = real_part.reshape(outer_count, inner_count, columns)
    imag_part = imag_part.reshape(outer_count, inner_count, columns)
    real_part, imag_part = rotate(
        real_part,
        imag_part,
        jnp.arange(outer_count, dtype=jnp.int32),
        jnp.arange(inner_count, dtype=jnp.int32),
        length,
    )
    real_part = jnp.transpose(real_part, (1, 0, 2)).reshape(inner_count, outer_count * columns)
    imag_part = jnp.transpose(imag_part, (1, 0, 2)).reshape(inner_count, outer_count * columns)
    cos_inner, sin_inner = dft_tables(inner_count)
    real_part, imag_part = transform(cos_inner, sin_inner, real_part, imag_part)
    return (
        real_part.reshape(length, columns) / samples,
        imag_part.reshape(length, columns) / samples,
    )


def local_transform(received, samples):
    real_part, imag_part = four_step(received[0, 0], received[1, 0], samples)
    return (real_part.astype(jnp.bfloat16), imag_part.astype(jnp.bfloat16))


def inverse_weights(psd_row, position, devices_tm, epochs, samples):
    half = samples // 2
    mirrored = jnp.concatenate([psd_row[: half + 1], psd_row[1:half][::-1]])
    picked = lax.dynamic_slice_in_dim(mirrored.reshape(epochs, devices_tm), position, 1, axis=1)
    return 8192.0 / picked[:, 0].astype(jnp.float32)


def panel_spectra(spectra):
    panels = lax.axis_size("panel")
    blocks = [spectra]
    for shift in range(1, panels):
        pairs = [(src, (src + shift) % panels) for src in range(panels)]
        blocks.append(lax.ppermute(spectra, "panel", pairs))
    return blocks


def comp_sum(value):
    comps = lax.axis_size("comp")
    if comps == 1:
        return value
    if comps != 2:
        return lax.psum(value, "comp")
    other = lax.ppermute(value, "comp", [(0, 1), (1, 0)])
    return value + other


def class_partials(spread, position, samples):
    devices_tm, block_len, columns = spread.shape
    index = jnp.arange(devices_tm, dtype=jnp.int32)
    cos_table, sin_table = phase_tables(index, index, devices_tm)
    real_part = jnp.sum(cos_table[:, :, None, None] * spread[None], axis=1)
    imag_part = -jnp.sum(sin_table[:, :, None, None] * spread[None], axis=1)
    local_epoch = position * block_len + jnp.arange(block_len, dtype=jnp.int32)
    real_part, imag_part = rotate(real_part, imag_part, index, local_epoch, samples)
    return jnp.stack([real_part, imag_part], axis=1)


def class_spectrum(gathered, samples):
    devices_tm, _, block_len, columns = gathered.shape
    length = devices_tm * block_len
    index = jnp.arange(devices_tm, dtype=jnp.int32)
    cos_table, sin_table = phase_tables(index, index, devices_tm)
    real_in = gathered[:, 0]
    imag_in = gathered[:, 1]
    cos_b = cos_table[:, :, None, None]
    sin_b = sin_table[:, :, None, None]
    real_part = jnp.sum(cos_b * real_in[None] + sin_b * imag_in[None], axis=1)
    imag_part = jnp.sum(cos_b * imag_in[None] - sin_b * real_in[None], axis=1)
    real_part, imag_part = rotate(
        real_part, imag_part, index, jnp.arange(block_len, dtype=jnp.int32), length
    )
    cos_inner, sin_inner = dft_tables(block_len)
    dims = (((1,), (1,)), ((), ()))

    def mat(table, value):
        return lax.dot_general(
            table, value, dims, precision=lax.Precision.HIGHEST,
            preferred_element_type=jnp.float32,
        )

    new_real = mat(cos_inner, real_part) + mat(sin_inner, imag_part)
    new_imag = mat(cos_inner, imag_part) - mat(sin_inner, real_part)
    new_real = (new_real.reshape(length, columns) / samples).astype(jnp.bfloat16)
    new_imag = (new_imag.reshape(length, columns) / samples).astype(jnp.bfloat16)
    return jnp.stack([new_real, new_imag])


def body(orbit_angles, gap_mask, column_index, lat_coeffs, psd_table):
    devices_tm = lax.axis_size("tm")
    panels = lax.axis_size("panel")
    epochs = orbit_angles.shape[1]
    block_len = epochs // devices_tm
    samples = epochs * devices_tm
    columns = lat_coeffs.shape[2]
    coeffs = lat_coeffs[0]
    keep_rows = gap_mask.astype(jnp.float32)
    packed = jnp.concatenate([orbit_angles, keep_rows[None]], axis=0)
    packed = packed.reshape(3, devices_tm, block_len).transpose(1, 0, 2)
    received = lax.all_to_all(packed, "tm", 0, 0, tiled=True)
    flat_orbit = received.transpose(1, 0, 2).reshape(3, devices_tm * block_len)
    spread = synthesize(flat_orbit[0:2], flat_orbit[2], column_index, coeffs).reshape(
        devices_tm, block_len, columns
    )
    position = lax.axis_index("tm")
    twisted = class_partials(spread, position, samples)
    gathered = lax.all_to_all(twisted, "tm", 0, 0, tiled=True)
    spectra = class_spectrum(gathered, samples)
    inverse_psd = inverse_weights(psd_table[0], position, devices_tm, epochs, samples)
    weighted = (spectra.astype(jnp.float32) * inverse_psd[None, :, None]).astype(jnp.bfloat16)
    contract = (((0, 1), (0, 1)), ((), ()))
    products = [
        lax.dot_general(block, weighted, contract, preferred_element_type=jnp.float32)
        for block in panel_spectra(spectra)
    ]
    by_shift = jnp.stack(products)
    panel = lax.axis_index("panel")
    order = (panel - jnp.arange(panels, dtype=jnp.int32)) % panels
    partial_value = jnp.take(by_shift, order, axis=0).reshape(panels * columns, columns)
    rows = partial_value.shape[0] // devices_tm
    pieces = lax.all_to_all(
        partial_value.reshape(devices_tm, rows, columns), "tm", 0, 0, tiled=True
    )
    return comp_sum(jnp.sum(pieces, axis=0))


def solution(mesh):
    return jax.shard_map(
        body,
        mesh=mesh,
        in_specs=(
            P(None, ("groups", "tm")),
            P(("groups", "tm")),
            P(None, "panel"),
            P("comp", None, "panel"),
            P("comp", None),
        ),
        out_specs=P(("groups", "tm"), "panel"),
        check_vma=False,
    )
```

```python
import math

import jax
import jax.numpy as jnp
from jax import lax
from jax.sharding import PartitionSpec as P

SPLIT = 64


def synthesize(angles, keep_rows, column_index, coeffs):
    terms_lat = coeffs.shape[0] // 2
    colatitude = angles[0]
    longit = angles[1]
    wavenumbers = jnp.arange(terms_lat, dtype=jnp.float32)
    phases = colatitude[:, None] * wavenumbers[None, :]
    basis_rows = jnp.concatenate([jnp.cos(phases), jnp.sin(phases)], axis=1).astype(jnp.bfloat16)
    degree = column_index[0]
    orders = column_index[1]
    levels = jnp.arange(2 * terms_lat, dtype=jnp.int32) % terms_lat
    allowed = levels[:, None] <= degree[None, :]
    masked = jnp.where(allowed, coeffs, jnp.zeros_like(coeffs))
    latitude = jnp.dot(basis_rows, masked, preferred_element_type=jnp.float32)
    lon_phase = longit[:, None] * jnp.abs(orders).astype(jnp.float32)[None, :]
    lon_wave = jnp.where(orders[None, :] >= 0, jnp.cos(lon_phase), jnp.sin(lon_phase))
    norm_scale = 1.0 / jnp.sqrt(degree.astype(jnp.float32) + 1.0)
    return latitude * lon_wave * (keep_rows[:, None] * norm_scale[None, :])


def phase_tables(row_index, col_index, length):
    product = row_index[:, None] * col_index[None, :] % length
    angle_grid = product.astype(jnp.float32) * (2.0 * math.pi / length)
    return (jnp.cos(angle_grid), jnp.sin(angle_grid))


def dft_tables(length):
    indices = jnp.arange(length, dtype=jnp.int32)
    return phase_tables(indices, indices, length)


def rotate(real_part, imag_part, outer_index, inner_index, length):
    index_grid = outer_index[:, None] * inner_index[None, :] % length
    angle_grid = index_grid.astype(jnp.float32) * (2.0 * math.pi / length)
    cosine = jnp.cos(angle_grid)[:, :, None]
    sine_grid = jnp.sin(angle_grid)[:, :, None]
    return (real_part * cosine + imag_part * sine_grid, imag_part * cosine - real_part * sine_grid)


def precise_dot(left_side, right_side):
    return jnp.dot(
        left_side, right_side, precision=lax.Precision.HIGHEST, preferred_element_type=jnp.float32
    )


def transform(cos_table, sin_table, real_part, imag_part):
    new_real = precise_dot(cos_table, real_part) + precise_dot(sin_table, imag_part)
    new_imag = precise_dot(cos_table, imag_part) - precise_dot(sin_table, real_part)
    return (new_real, new_imag)


def four_step(real_in, imag_in, samples):
    length = real_in.shape[0]
    columns = real_in.shape[1]
    outer_count = SPLIT
    inner_count = length // SPLIT
    real_part = real_in.reshape(outer_count, inner_count * columns)
    imag_part = imag_in.reshape(outer_count, inner_count * columns)
    cos_outer, sin_outer = dft_tables(outer_count)
    real_part, imag_part = transform(cos_outer, sin_outer, real_part, imag_part)
    real_part = real_part.reshape(outer_count, inner_count, columns)
    imag_part = imag_part.reshape(outer_count, inner_count, columns)
    real_part, imag_part = rotate(
        real_part,
        imag_part,
        jnp.arange(outer_count, dtype=jnp.int32),
        jnp.arange(inner_count, dtype=jnp.int32),
        length,
    )
    real_part = jnp.transpose(real_part, (1, 0, 2)).reshape(inner_count, outer_count * columns)
    imag_part = jnp.transpose(imag_part, (1, 0, 2)).reshape(inner_count, outer_count * columns)
    cos_inner, sin_inner = dft_tables(inner_count)
    real_part, imag_part = transform(cos_inner, sin_inner, real_part, imag_part)
    return (
        real_part.reshape(length, columns) / samples,
        imag_part.reshape(length, columns) / samples,
    )


def local_transform(received, samples):
    real_part, imag_part = four_step(received[0, 0], received[1, 0], samples)
    return (real_part.astype(jnp.bfloat16), imag_part.astype(jnp.bfloat16))


def inverse_weights(psd_row, position, devices_tm, epochs, samples):
    half = samples // 2
    mirrored = jnp.concatenate([psd_row[: half + 1], psd_row[1:half][::-1]])
    picked = lax.dynamic_slice_in_dim(mirrored.reshape(epochs, devices_tm), position, 1, axis=1)
    return 8192.0 / picked[:, 0].astype(jnp.float32)


def panel_spectra(spectra):
    panels = lax.axis_size("panel")
    blocks = [spectra]
    for shift in range(1, panels):
        pairs = [(src, (src + shift) % panels) for src in range(panels)]
        blocks.append(lax.ppermute(spectra, "panel", pairs))
    return blocks


def comp_sum(value):
    comps = lax.axis_size("comp")
    if comps == 1:
        return value
    if comps != 2:
        return lax.psum(value, "comp")
    other = lax.ppermute(value, "comp", [(0, 1), (1, 0)])
    return value + other


def class_partials(spread, position, samples):
    devices_tm, block_len, columns = spread.shape
    index = jnp.arange(devices_tm, dtype=jnp.int32)
    cos_table, sin_table = phase_tables(index, index, devices_tm)
    real_part = jnp.sum(cos_table[:, :, None, None] * spread[None], axis=1)
    imag_part = -jnp.sum(sin_table[:, :, None, None] * spread[None], axis=1)
    local_epoch = position * block_len + jnp.arange(block_len, dtype=jnp.int32)
    real_part, imag_part = rotate(real_part, imag_part, index, local_epoch, samples)
    return jnp.stack([real_part, imag_part], axis=1)


def class_spectrum(gathered, samples):
    devices_tm, _, block_len, columns = gathered.shape
    length = devices_tm * block_len
    index = jnp.arange(devices_tm, dtype=jnp.int32)
    cos_table, sin_table = phase_tables(index, index, devices_tm)
    real_in = gathered[:, 0]
    imag_in = gathered[:, 1]
    cos_b = cos_table[:, :, None, None]
    sin_b = sin_table[:, :, None, None]
    real_part = jnp.sum(cos_b * real_in[None] + sin_b * imag_in[None], axis=1)
    imag_part = jnp.sum(cos_b * imag_in[None] - sin_b * real_in[None], axis=1)
    real_part, imag_part = rotate(
        real_part, imag_part, index, jnp.arange(block_len, dtype=jnp.int32), length
    )
    cos_inner, sin_inner = dft_tables(block_len)
    dims = (((1,), (1,)), ((), ()))

    def mat(table, value):
        return lax.dot_general(
            table, value, dims, precision=lax.Precision.HIGH,
            preferred_element_type=jnp.float32,
        )

    new_real = mat(cos_inner, real_part) + mat(sin_inner, imag_part)
    new_imag = mat(cos_inner, imag_part) - mat(sin_inner, real_part)
    new_real = (new_real.reshape(length, columns) / samples).astype(jnp.bfloat16)
    new_imag = (new_imag.reshape(length, columns) / samples).astype(jnp.bfloat16)
    return jnp.stack([new_real, new_imag])


def body(orbit_angles, gap_mask, column_index, lat_coeffs, psd_table):
    devices_tm = lax.axis_size("tm")
    panels = lax.axis_size("panel")
    epochs = orbit_angles.shape[1]
    block_len = epochs // devices_tm
    samples = epochs * devices_tm
    columns = lat_coeffs.shape[2]
    coeffs = lat_coeffs[0]
    keep_rows = gap_mask.astype(jnp.float32)
    packed = jnp.concatenate([orbit_angles, keep_rows[None]], axis=0)
    packed = packed.reshape(3, devices_tm, block_len).transpose(1, 0, 2)
    received = lax.all_to_all(packed, "tm", 0, 0, tiled=True)
    flat_orbit = received.transpose(1, 0, 2).reshape(3, devices_tm * block_len)
    spread = synthesize(flat_orbit[0:2], flat_orbit[2], column_index, coeffs).reshape(
        devices_tm, block_len, columns
    )
    position = lax.axis_index("tm")
    twisted = class_partials(spread, position, samples)
    gathered = lax.all_to_all(twisted, "tm", 0, 0, tiled=True)
    spectra = class_spectrum(gathered, samples)
    inverse_psd = inverse_weights(psd_table[0], position, devices_tm, epochs, samples)
    weighted = (spectra.astype(jnp.float32) * inverse_psd[None, :, None]).astype(jnp.bfloat16)
    contract = (((0, 1), (0, 1)), ((), ()))
    products = [
        lax.dot_general(block, weighted, contract, preferred_element_type=jnp.float32)
        for block in panel_spectra(spectra)
    ]
    by_shift = jnp.stack(products)
    panel = lax.axis_index("panel")
    order = (panel - jnp.arange(panels, dtype=jnp.int32)) % panels
    partial_value = jnp.take(by_shift, order, axis=0).reshape(panels * columns, columns)
    return settle_rows(partial_value)


def settle_rows(partial_value):
    devices_tm = lax.axis_size("tm")
    comps = lax.axis_size("comp")
    rows_total, columns = partial_value.shape
    rows = rows_total // devices_tm
    if comps != 2 or columns % 256 != 0:
        pieces = lax.all_to_all(
            partial_value.reshape(devices_tm, rows, columns), "tm", 0, 0, tiled=True
        )
        return comp_sum(jnp.sum(pieces, axis=0))
    half = columns // 2
    comp = lax.axis_index("comp")
    mine = lax.dynamic_slice_in_dim(partial_value, comp * half, half, axis=1)
    theirs = lax.dynamic_slice_in_dim(partial_value, (1 - comp) * half, half, axis=1)
    summed = mine + lax.ppermute(theirs, "comp", [(0, 1), (1, 0)])
    pieces = lax.all_to_all(summed.reshape(devices_tm, rows, half), "tm", 0, 0, tiled=True)
    block = jnp.sum(pieces, axis=0)
    other = lax.ppermute(block, "comp", [(0, 1), (1, 0)])
    first = jnp.where(comp == 0, block, other)
    second = jnp.where(comp == 0, other, block)
    return jnp.concatenate([first, second], axis=1)


def solution(mesh):
    return jax.shard_map(
        body,
        mesh=mesh,
        in_specs=(
            P(None, ("groups", "tm")),
            P(("groups", "tm")),
            P(None, "panel"),
            P("comp", None, "panel"),
            P("comp", None),
        ),
        out_specs=P(("groups", "tm"), "panel"),
        check_vma=False,
    )
```

```python
import math

import jax
import jax.numpy as jnp
from jax import lax
from jax.sharding import PartitionSpec as P

SPLIT = 64


def synthesize(angles, keep_rows, column_index, coeffs):
    terms_lat = coeffs.shape[0] // 2
    colatitude = angles[0]
    longit = angles[1]
    wavenumbers = jnp.arange(terms_lat, dtype=jnp.float32)
    phases = colatitude[:, None] * wavenumbers[None, :]
    basis_rows = jnp.concatenate([jnp.cos(phases), jnp.sin(phases)], axis=1).astype(jnp.bfloat16)
    degree = column_index[0]
    orders = column_index[1]
    levels = jnp.arange(2 * terms_lat, dtype=jnp.int32) % terms_lat
    allowed = levels[:, None] <= degree[None, :]
    masked = jnp.where(allowed, coeffs, jnp.zeros_like(coeffs))
    latitude = jnp.dot(basis_rows, masked, preferred_element_type=jnp.float32)
    lon_phase = longit[:, None] * jnp.abs(orders).astype(jnp.float32)[None, :]
    lon_wave = jnp.where(orders[None, :] >= 0, jnp.cos(lon_phase), jnp.sin(lon_phase))
    norm_scale = 1.0 / jnp.sqrt(degree.astype(jnp.float32) + 1.0)
    return latitude * lon_wave * (keep_rows[:, None] * norm_scale[None, :])


def phase_tables(row_index, col_index, length):
    product = row_index[:, None] * col_index[None, :] % length
    angle_grid = product.astype(jnp.float32) * (2.0 * math.pi / length)
    return (jnp.cos(angle_grid), jnp.sin(angle_grid))


def dft_tables(length):
    indices = jnp.arange(length, dtype=jnp.int32)
    return phase_tables(indices, indices, length)


def rotate(real_part, imag_part, outer_index, inner_index, length):
    index_grid = outer_index[:, None] * inner_index[None, :] % length
    angle_grid = index_grid.astype(jnp.float32) * (2.0 * math.pi / length)
    cosine = jnp.cos(angle_grid)[:, :, None]
    sine_grid = jnp.sin(angle_grid)[:, :, None]
    return (real_part * cosine + imag_part * sine_grid, imag_part * cosine - real_part * sine_grid)


def precise_dot(left_side, right_side):
    return jnp.dot(
        left_side, right_side, precision=lax.Precision.HIGHEST, preferred_element_type=jnp.float32
    )


def transform(cos_table, sin_table, real_part, imag_part):
    new_real = precise_dot(cos_table, real_part) + precise_dot(sin_table, imag_part)
    new_imag = precise_dot(cos_table, imag_part) - precise_dot(sin_table, real_part)
    return (new_real, new_imag)


def four_step(real_in, imag_in, samples):
    length = real_in.shape[0]
    columns = real_in.shape[1]
    outer_count = SPLIT
    inner_count = length // SPLIT
    real_part = real_in.reshape(outer_count, inner_count * columns)
    imag_part = imag_in.reshape(outer_count, inner_count * columns)
    cos_outer, sin_outer = dft_tables(outer_count)
    real_part, imag_part = transform(cos_outer, sin_outer, real_part, imag_part)
    real_part = real_part.reshape(outer_count, inner_count, columns)
    imag_part = imag_part.reshape(outer_count, inner_count, columns)
    real_part, imag_part = rotate(
        real_part,
        imag_part,
        jnp.arange(outer_count, dtype=jnp.int32),
        jnp.arange(inner_count, dtype=jnp.int32),
        length,
    )
    real_part = jnp.transpose(real_part, (1, 0, 2)).reshape(inner_count, outer_count * columns)
    imag_part = jnp.transpose(imag_part, (1, 0, 2)).reshape(inner_count, outer_count * columns)
    cos_inner, sin_inner = dft_tables(inner_count)
    real_part, imag_part = transform(cos_inner, sin_inner, real_part, imag_part)
    return (
        real_part.reshape(length, columns) / samples,
        imag_part.reshape(length, columns) / samples,
    )


def local_transform(received, samples):
    real_part, imag_part = four_step(received[0, 0], received[1, 0], samples)
    return (real_part.astype(jnp.bfloat16), imag_part.astype(jnp.bfloat16))


def inverse_weights(psd_row, position, devices_tm, epochs, samples, count):
    half = samples // 2
    mirrored = jnp.concatenate([psd_row[: half + 1], psd_row[1:half][::-1]])
    picked = lax.dynamic_slice_in_dim(mirrored.reshape(epochs, devices_tm), position, 1, axis=1)
    inverse = 8192.0 / picked[:count, 0].astype(jnp.float32)
    order = jnp.arange(count, dtype=jnp.int32)
    first = jnp.where(position == 0, 1.0, 2.0)
    middle = jnp.where(position == 0, 1.0, 0.0)
    fold = jnp.where(
        order == 0, first, jnp.where(order < epochs // 2, 2.0, jnp.where(order == epochs // 2, middle, 0.0))
    )
    return inverse, fold


def panel_spectra(spectra):
    panels = lax.axis_size("panel")
    blocks = [spectra]
    for shift in range(1, panels):
        pairs = [(src, (src + shift) % panels) for src in range(panels)]
        blocks.append(lax.ppermute(spectra, "panel", pairs))
    return blocks


def comp_sum(value):
    comps = lax.axis_size("comp")
    if comps == 1:
        return value
    if comps != 2:
        return lax.psum(value, "comp")
    other = lax.ppermute(value, "comp", [(0, 1), (1, 0)])
    return value + other


def class_partials(spread, position, samples):
    devices_tm, block_len, columns = spread.shape
    index = jnp.arange(devices_tm, dtype=jnp.int32)
    cos_table, sin_table = phase_tables(index, index, devices_tm)
    real_part = jnp.sum(cos_table[:, :, None, None] * spread[None], axis=1)
    imag_part = -jnp.sum(sin_table[:, :, None, None] * spread[None], axis=1)
    local_epoch = position * block_len + jnp.arange(block_len, dtype=jnp.int32)
    real_part, imag_part = rotate(real_part, imag_part, index, local_epoch, samples)
    return jnp.stack([real_part, imag_part], axis=1)


def class_spectrum(gathered, samples):
    devices_tm, _, block_len, columns = gathered.shape
    length = devices_tm * block_len
    index = jnp.arange(devices_tm, dtype=jnp.int32)
    cos_table, sin_table = phase_tables(index, index, devices_tm)
    real_in = gathered[:, 0]
    imag_in = gathered[:, 1]
    cos_b = cos_table[:, :, None, None]
    sin_b = sin_table[:, :, None, None]
    real_part = jnp.sum(cos_b * real_in[None] + sin_b * imag_in[None], axis=1)
    imag_part = jnp.sum(cos_b * imag_in[None] - sin_b * real_in[None], axis=1)
    real_part, imag_part = rotate(
        real_part, imag_part, index, jnp.arange(block_len, dtype=jnp.int32), length
    )
    kept = block_len // 2 + 1
    cos_inner, sin_inner = phase_tables(
        jnp.arange(kept, dtype=jnp.int32), jnp.arange(block_len, dtype=jnp.int32), block_len
    )
    dims = (((1,), (1,)), ((), ()))

    def mat(table, value):
        return lax.dot_general(
            table, value, dims, precision=lax.Precision.HIGH,
            preferred_element_type=jnp.float32,
        )

    new_real = mat(cos_inner, real_part) + mat(sin_inner, imag_part)
    new_imag = mat(cos_inner, imag_part) - mat(sin_inner, real_part)
    new_real = (new_real.reshape(kept * devices_tm, columns) / samples).astype(jnp.bfloat16)
    new_imag = (new_imag.reshape(kept * devices_tm, columns) / samples).astype(jnp.bfloat16)
    return jnp.stack([new_real, new_imag])


def body(orbit_angles, gap_mask, column_index, lat_coeffs, psd_table):
    devices_tm = lax.axis_size("tm")
    panels = lax.axis_size("panel")
    epochs = orbit_angles.shape[1]
    block_len = epochs // devices_tm
    samples = epochs * devices_tm
    columns = lat_coeffs.shape[2]
    coeffs = lat_coeffs[0]
    keep_rows = gap_mask.astype(jnp.float32)
    packed = jnp.concatenate([orbit_angles, keep_rows[None]], axis=0)
    packed = packed.reshape(3, devices_tm, block_len).transpose(1, 0, 2)
    received = lax.all_to_all(packed, "tm", 0, 0, tiled=True)
    flat_orbit = received.transpose(1, 0, 2).reshape(3, devices_tm * block_len)
    spread = synthesize(flat_orbit[0:2], flat_orbit[2], column_index, coeffs).reshape(
        devices_tm, block_len, columns
    )
    position = lax.axis_index("tm")
    twisted = class_partials(spread, position, samples)
    gathered = lax.all_to_all(twisted, "tm", 0, 0, tiled=True)
    spectra = class_spectrum(gathered, samples)
    inverse_psd, fold = inverse_weights(
        psd_table[0], position, devices_tm, epochs, samples, spectra.shape[1]
    )
    weighted = (spectra.astype(jnp.float32) * inverse_psd[None, :, None]).astype(jnp.bfloat16)
    weighted = weighted * fold[None, :, None].astype(jnp.bfloat16)
    contract = (((0, 1), (0, 1)), ((), ()))
    products = [
        lax.dot_general(block, weighted, contract, preferred_element_type=jnp.float32)
        for block in panel_spectra(spectra)
    ]
    by_shift = jnp.stack(products)
    panel = lax.axis_index("panel")
    order = (panel - jnp.arange(panels, dtype=jnp.int32)) % panels
    partial_value = jnp.take(by_shift, order, axis=0).reshape(panels * columns, columns)
    return settle_rows(partial_value)


def settle_rows(partial_value):
    devices_tm = lax.axis_size("tm")
    comps = lax.axis_size("comp")
    rows_total, columns = partial_value.shape
    rows = rows_total // devices_tm
    if comps != 2 or columns % 256 != 0:
        pieces = lax.all_to_all(
            partial_value.reshape(devices_tm, rows, columns), "tm", 0, 0, tiled=True
        )
        return comp_sum(jnp.sum(pieces, axis=0))
    half = columns // 2
    comp = lax.axis_index("comp")
    mine = lax.dynamic_slice_in_dim(partial_value, comp * half, half, axis=1)
    theirs = lax.dynamic_slice_in_dim(partial_value, (1 - comp) * half, half, axis=1)
    summed = mine + lax.ppermute(theirs, "comp", [(0, 1), (1, 0)])
    pieces = lax.all_to_all(summed.reshape(devices_tm, rows, half), "tm", 0, 0, tiled=True)
    block = jnp.sum(pieces, axis=0)
    other = lax.ppermute(block, "comp", [(0, 1), (1, 0)])
    first = jnp.where(comp == 0, block, other)
    second = jnp.where(comp == 0, other, block)
    return jnp.concatenate([first, second], axis=1)


def solution(mesh):
    return jax.shard_map(
        body,
        mesh=mesh,
        in_specs=(
            P(None, ("groups", "tm")),
            P(("groups", "tm")),
            P(None, "panel"),
            P("comp", None, "panel"),
            P("comp", None),
        ),
        out_specs=P(("groups", "tm"), "panel"),
        check_vma=False,
    )
```

```python
import math

import jax
import jax.numpy as jnp
from jax import lax
from jax.sharding import PartitionSpec as P

SPLIT = 64


def synthesize(angles, keep_rows, column_index, coeffs):
    terms_lat = coeffs.shape[0] // 2
    colatitude = angles[0]
    longit = angles[1]
    wavenumbers = jnp.arange(terms_lat, dtype=jnp.float32)
    phases = colatitude[:, None] * wavenumbers[None, :]
    basis_rows = jnp.concatenate([jnp.cos(phases), jnp.sin(phases)], axis=1).astype(jnp.bfloat16)
    degree = column_index[0]
    orders = column_index[1]
    levels = jnp.arange(2 * terms_lat, dtype=jnp.int32) % terms_lat
    allowed = levels[:, None] <= degree[None, :]
    masked = jnp.where(allowed, coeffs, jnp.zeros_like(coeffs))
    latitude = jnp.dot(basis_rows, masked, preferred_element_type=jnp.float32)
    lon_phase = longit[:, None] * jnp.abs(orders).astype(jnp.float32)[None, :]
    lon_wave = jnp.where(orders[None, :] >= 0, jnp.cos(lon_phase), jnp.sin(lon_phase))
    norm_scale = 1.0 / jnp.sqrt(degree.astype(jnp.float32) + 1.0)
    return latitude * lon_wave * (keep_rows[:, None] * norm_scale[None, :])


def phase_tables(row_index, col_index, length):
    product = row_index[:, None] * col_index[None, :] % length
    angle_grid = product.astype(jnp.float32) * (2.0 * math.pi / length)
    return (jnp.cos(angle_grid), jnp.sin(angle_grid))


def dft_tables(length):
    indices = jnp.arange(length, dtype=jnp.int32)
    return phase_tables(indices, indices, length)


def rotate(real_part, imag_part, outer_index, inner_index, length):
    index_grid = outer_index[:, None] * inner_index[None, :] % length
    angle_grid = index_grid.astype(jnp.float32) * (2.0 * math.pi / length)
    cosine = jnp.cos(angle_grid)[:, :, None]
    sine_grid = jnp.sin(angle_grid)[:, :, None]
    return (real_part * cosine + imag_part * sine_grid, imag_part * cosine - real_part * sine_grid)


def precise_dot(left_side, right_side):
    return jnp.dot(
        left_side, right_side, precision=lax.Precision.HIGHEST, preferred_element_type=jnp.float32
    )


def transform(cos_table, sin_table, real_part, imag_part):
    new_real = precise_dot(cos_table, real_part) + precise_dot(sin_table, imag_part)
    new_imag = precise_dot(cos_table, imag_part) - precise_dot(sin_table, real_part)
    return (new_real, new_imag)


def four_step(real_in, imag_in, samples):
    length = real_in.shape[0]
    columns = real_in.shape[1]
    outer_count = SPLIT
    inner_count = length // SPLIT
    real_part = real_in.reshape(outer_count, inner_count * columns)
    imag_part = imag_in.reshape(outer_count, inner_count * columns)
    cos_outer, sin_outer = dft_tables(outer_count)
    real_part, imag_part = transform(cos_outer, sin_outer, real_part, imag_part)
    real_part = real_part.reshape(outer_count, inner_count, columns)
    imag_part = imag_part.reshape(outer_count, inner_count, columns)
    real_part, imag_part = rotate(
        real_part,
        imag_part,
        jnp.arange(outer_count, dtype=jnp.int32),
        jnp.arange(inner_count, dtype=jnp.int32),
        length,
    )
    real_part = jnp.transpose(real_part, (1, 0, 2)).reshape(inner_count, outer_count * columns)
    imag_part = jnp.transpose(imag_part, (1, 0, 2)).reshape(inner_count, outer_count * columns)
    cos_inner, sin_inner = dft_tables(inner_count)
    real_part, imag_part = transform(cos_inner, sin_inner, real_part, imag_part)
    return (
        real_part.reshape(length, columns) / samples,
        imag_part.reshape(length, columns) / samples,
    )


def local_transform(received, samples):
    real_part, imag_part = four_step(received[0, 0], received[1, 0], samples)
    return (real_part.astype(jnp.bfloat16), imag_part.astype(jnp.bfloat16))


def inverse_weights(psd_row, position, devices_tm, epochs, samples, count):
    half = samples // 2
    mirrored = jnp.concatenate([psd_row[: half + 1], psd_row[1:half][::-1]])
    picked = lax.dynamic_slice_in_dim(mirrored.reshape(epochs, devices_tm), position, 1, axis=1)
    inverse = 8192.0 / picked[:count, 0].astype(jnp.float32)
    order = jnp.arange(count, dtype=jnp.int32)
    first = jnp.where(position == 0, 1.0, 2.0)
    middle = jnp.where(position == 0, 1.0, 0.0)
    fold = jnp.where(
        order == 0, first, jnp.where(order < epochs // 2, 2.0, jnp.where(order == epochs // 2, middle, 0.0))
    )
    return inverse, fold


def panel_spectra(spectra):
    panels = lax.axis_size("panel")
    blocks = [spectra]
    for shift in range(1, panels):
        pairs = [(src, (src + shift) % panels) for src in range(panels)]
        blocks.append(lax.ppermute(spectra, "panel", pairs))
    return blocks


def comp_sum(value):
    comps = lax.axis_size("comp")
    if comps == 1:
        return value
    if comps != 2:
        return lax.psum(value, "comp")
    other = lax.ppermute(value, "comp", [(0, 1), (1, 0)])
    return value + other


def class_partials(spread, position, samples):
    devices_tm, block_len, columns = spread.shape
    index = jnp.arange(devices_tm, dtype=jnp.int32)
    cos_table, sin_table = phase_tables(index, index, devices_tm)
    real_part = jnp.sum(cos_table[:, :, None, None] * spread[None], axis=1)
    imag_part = -jnp.sum(sin_table[:, :, None, None] * spread[None], axis=1)
    local_epoch = position * block_len + jnp.arange(block_len, dtype=jnp.int32)
    real_part, imag_part = rotate(real_part, imag_part, index, local_epoch, samples)
    return jnp.stack([real_part, imag_part], axis=1)


def class_spectrum(gathered, samples):
    devices_tm, _, block_len, columns = gathered.shape
    length = devices_tm * block_len
    index = jnp.arange(devices_tm, dtype=jnp.int32)
    cos_table, sin_table = phase_tables(index, index, devices_tm)
    real_in = gathered[:, 0]
    imag_in = gathered[:, 1]
    cos_b = cos_table[:, :, None, None]
    sin_b = sin_table[:, :, None, None]
    real_part = jnp.sum(cos_b * real_in[None] + sin_b * imag_in[None], axis=1)
    imag_part = jnp.sum(cos_b * imag_in[None] - sin_b * real_in[None], axis=1)
    real_part, imag_part = rotate(
        real_part, imag_part, index, jnp.arange(block_len, dtype=jnp.int32), length
    )
    kept = block_len // 2 + 1
    cos_inner, sin_inner = phase_tables(
        jnp.arange(kept, dtype=jnp.int32), jnp.arange(block_len, dtype=jnp.int32), block_len
    )
    dims = (((1,), (1,)), ((), ()))

    def mat(table, value):
        return lax.dot_general(
            table, value, dims, precision=lax.Precision.HIGH,
            preferred_element_type=jnp.float32,
        )

    new_real = mat(cos_inner, real_part) + mat(sin_inner, imag_part)
    new_imag = mat(cos_inner, imag_part) - mat(sin_inner, real_part)
    new_real = (new_real.reshape(kept * devices_tm, columns) / samples).astype(jnp.bfloat16)
    new_imag = (new_imag.reshape(kept * devices_tm, columns) / samples).astype(jnp.bfloat16)
    return jnp.stack([new_real, new_imag])


def swap_blocks(blocks, axis, ordered):
    count = lax.axis_size(axis)
    if count > 8:
        received = lax.all_to_all(blocks, axis, 0, 0, tiled=True)
        return received if ordered else jnp.sum(received, axis=0)
    me = lax.axis_index(axis)
    arrived = [lax.dynamic_index_in_dim(blocks, me, 0, keepdims=False)]
    for shift in range(1, count):
        outgoing = lax.dynamic_index_in_dim(blocks, (me + shift) % count, 0, keepdims=False)
        pairs = [(src, (src + shift) % count) for src in range(count)]
        arrived.append(lax.ppermute(outgoing, axis, pairs))
    if not ordered:
        total = arrived[0]
        for part in arrived[1:]:
            total = total + part
        return total
    order = (me - jnp.arange(count, dtype=jnp.int32)) % count
    return jnp.take(jnp.stack(arrived), order, axis=0)


def body(orbit_angles, gap_mask, column_index, lat_coeffs, psd_table):
    devices_tm = lax.axis_size("tm")
    panels = lax.axis_size("panel")
    epochs = orbit_angles.shape[1]
    block_len = epochs // devices_tm
    samples = epochs * devices_tm
    columns = lat_coeffs.shape[2]
    coeffs = lat_coeffs[0]
    keep_rows = gap_mask.astype(jnp.float32)
    packed = jnp.concatenate([orbit_angles, keep_rows[None]], axis=0)
    packed = packed.reshape(3, devices_tm, block_len).transpose(1, 0, 2)
    received = swap_blocks(packed, "tm", True)
    flat_orbit = received.transpose(1, 0, 2).reshape(3, devices_tm * block_len)
    spread = synthesize(flat_orbit[0:2], flat_orbit[2], column_index, coeffs).reshape(
        devices_tm, block_len, columns
    )
    position = lax.axis_index("tm")
    twisted = class_partials(spread, position, samples)
    gathered = lax.all_to_all(twisted, "tm", 0, 0, tiled=True)
    spectra = class_spectrum(gathered, samples)
    inverse_psd, fold = inverse_weights(
        psd_table[0], position, devices_tm, epochs, samples, spectra.shape[1]
    )
    weighted = (spectra.astype(jnp.float32) * inverse_psd[None, :, None]).astype(jnp.bfloat16)
    weighted = weighted * fold[None, :, None].astype(jnp.bfloat16)
    contract = (((0, 1), (0, 1)), ((), ()))
    products = [
        lax.dot_general(block, weighted, contract, preferred_element_type=jnp.float32)
        for block in panel_spectra(spectra)
    ]
    by_shift = jnp.stack(products)
    panel = lax.axis_index("panel")
    order = (panel - jnp.arange(panels, dtype=jnp.int32)) % panels
    partial_value = jnp.take(by_shift, order, axis=0).reshape(panels * columns, columns)
    return settle_rows(partial_value)


def settle_rows(partial_value):
    devices_tm = lax.axis_size("tm")
    comps = lax.axis_size("comp")
    rows_total, columns = partial_value.shape
    rows = rows_total // devices_tm
    if comps != 2 or columns % 256 != 0:
        pieces = lax.all_to_all(
            partial_value.reshape(devices_tm, rows, columns), "tm", 0, 0, tiled=True
        )
        return comp_sum(jnp.sum(pieces, axis=0))
    half = columns // 2
    comp = lax.axis_index("comp")
    mine = lax.dynamic_slice_in_dim(partial_value, comp * half, half, axis=1)
    theirs = lax.dynamic_slice_in_dim(partial_value, (1 - comp) * half, half, axis=1)
    summed = mine + lax.ppermute(theirs, "comp", [(0, 1), (1, 0)])
    block = swap_blocks(summed.reshape(devices_tm, rows, half), "tm", False)
    other = lax.ppermute(block, "comp", [(0, 1), (1, 0)])
    first = jnp.where(comp == 0, block, other)
    second = jnp.where(comp == 0, other, block)
    return jnp.concatenate([first, second], axis=1)


def solution(mesh):
    return jax.shard_map(
        body,
        mesh=mesh,
        in_specs=(
            P(None, ("groups", "tm")),
            P(("groups", "tm")),
            P(None, "panel"),
            P("comp", None, "panel"),
            P("comp", None),
        ),
        out_specs=P(("groups", "tm"), "panel"),
        check_vma=False,
    )
```

```python
import math

import jax
import jax.numpy as jnp
from jax import lax
from jax.sharding import PartitionSpec as P

SPLIT = 64


def synthesize(angles, keep_rows, column_index, coeffs):
    terms_lat = coeffs.shape[0] // 2
    colatitude = angles[0]
    longit = angles[1]
    wavenumbers = jnp.arange(terms_lat, dtype=jnp.float32)
    phases = colatitude[:, None] * wavenumbers[None, :]
    basis_rows = jnp.concatenate([jnp.cos(phases), jnp.sin(phases)], axis=1).astype(jnp.bfloat16)
    degree = column_index[0]
    orders = column_index[1]
    levels = jnp.arange(2 * terms_lat, dtype=jnp.int32) % terms_lat
    allowed = levels[:, None] <= degree[None, :]
    masked = jnp.where(allowed, coeffs, jnp.zeros_like(coeffs))
    latitude = jnp.dot(basis_rows, masked, preferred_element_type=jnp.float32)
    lon_phase = longit[:, None] * jnp.abs(orders).astype(jnp.float32)[None, :]
    lon_wave = jnp.where(orders[None, :] >= 0, jnp.cos(lon_phase), jnp.sin(lon_phase))
    norm_scale = 1.0 / jnp.sqrt(degree.astype(jnp.float32) + 1.0)
    return latitude * lon_wave * (keep_rows[:, None] * norm_scale[None, :])


def phase_tables(row_index, col_index, length):
    product = row_index[:, None] * col_index[None, :] % length
    angle_grid = product.astype(jnp.float32) * (2.0 * math.pi / length)
    return (jnp.cos(angle_grid), jnp.sin(angle_grid))


def dft_tables(length):
    indices = jnp.arange(length, dtype=jnp.int32)
    return phase_tables(indices, indices, length)


def rotate(real_part, imag_part, outer_index, inner_index, length):
    index_grid = outer_index[:, None] * inner_index[None, :] % length
    angle_grid = index_grid.astype(jnp.float32) * (2.0 * math.pi / length)
    cosine = jnp.cos(angle_grid)[:, :, None]
    sine_grid = jnp.sin(angle_grid)[:, :, None]
    return (real_part * cosine + imag_part * sine_grid, imag_part * cosine - real_part * sine_grid)


def precise_dot(left_side, right_side):
    return jnp.dot(
        left_side, right_side, precision=lax.Precision.HIGHEST, preferred_element_type=jnp.float32
    )


def transform(cos_table, sin_table, real_part, imag_part):
    new_real = precise_dot(cos_table, real_part) + precise_dot(sin_table, imag_part)
    new_imag = precise_dot(cos_table, imag_part) - precise_dot(sin_table, real_part)
    return (new_real, new_imag)


def four_step(real_in, imag_in, samples):
    length = real_in.shape[0]
    columns = real_in.shape[1]
    outer_count = SPLIT
    inner_count = length // SPLIT
    real_part = real_in.reshape(outer_count, inner_count * columns)
    imag_part = imag_in.reshape(outer_count, inner_count * columns)
    cos_outer, sin_outer = dft_tables(outer_count)
    real_part, imag_part = transform(cos_outer, sin_outer, real_part, imag_part)
    real_part = real_part.reshape(outer_count, inner_count, columns)
    imag_part = imag_part.reshape(outer_count, inner_count, columns)
    real_part, imag_part = rotate(
        real_part,
        imag_part,
        jnp.arange(outer_count, dtype=jnp.int32),
        jnp.arange(inner_count, dtype=jnp.int32),
        length,
    )
    real_part = jnp.transpose(real_part, (1, 0, 2)).reshape(inner_count, outer_count * columns)
    imag_part = jnp.transpose(imag_part, (1, 0, 2)).reshape(inner_count, outer_count * columns)
    cos_inner, sin_inner = dft_tables(inner_count)
    real_part, imag_part = transform(cos_inner, sin_inner, real_part, imag_part)
    return (
        real_part.reshape(length, columns) / samples,
        imag_part.reshape(length, columns) / samples,
    )


def local_transform(received, samples):
    real_part, imag_part = four_step(received[0, 0], received[1, 0], samples)
    return (real_part.astype(jnp.bfloat16), imag_part.astype(jnp.bfloat16))


def inverse_weights(psd_row, position, devices_tm, epochs, samples, count):
    half = samples // 2
    mirrored = jnp.concatenate([psd_row[: half + 1], psd_row[1:half][::-1]])
    picked = lax.dynamic_slice_in_dim(mirrored.reshape(epochs, devices_tm), position, 1, axis=1)
    inverse = 8192.0 / picked[:count, 0].astype(jnp.float32)
    order = jnp.arange(count, dtype=jnp.int32)
    first = jnp.where(position == 0, 1.0, 2.0)
    middle = jnp.where(position == 0, 1.0, 0.0)
    fold = jnp.where(
        order == 0, first, jnp.where(order < epochs // 2, 2.0, jnp.where(order == epochs // 2, middle, 0.0))
    )
    return inverse, fold


def panel_spectra(spectra):
    panels = lax.axis_size("panel")
    blocks = [spectra]
    for shift in range(1, panels):
        pairs = [(src, (src + shift) % panels) for src in range(panels)]
        blocks.append(lax.ppermute(spectra, "panel", pairs))
    return blocks


def comp_sum(value):
    comps = lax.axis_size("comp")
    if comps == 1:
        return value
    if comps != 2:
        return lax.psum(value, "comp")
    other = lax.ppermute(value, "comp", [(0, 1), (1, 0)])
    return value + other


def class_partials(spread, position, samples):
    devices_tm, block_len, columns = spread.shape
    index = jnp.arange(devices_tm, dtype=jnp.int32)
    cos_table, sin_table = phase_tables(index, index, devices_tm)
    real_part = jnp.sum(cos_table[:, :, None, None] * spread[None], axis=1)
    imag_part = -jnp.sum(sin_table[:, :, None, None] * spread[None], axis=1)
    local_epoch = position * block_len + jnp.arange(block_len, dtype=jnp.int32)
    real_part, imag_part = rotate(real_part, imag_part, index, local_epoch, samples)
    return jnp.stack([real_part, imag_part], axis=1)


def class_spectrum(gathered, samples):
    devices_tm, _, block_len, columns = gathered.shape
    length = devices_tm * block_len
    index = jnp.arange(devices_tm, dtype=jnp.int32)
    cos_table, sin_table = phase_tables(index, index, devices_tm)
    real_in = gathered[:, 0]
    imag_in = gathered[:, 1]
    cos_b = cos_table[:, :, None, None]
    sin_b = sin_table[:, :, None, None]
    real_part = jnp.sum(cos_b * real_in[None] + sin_b * imag_in[None], axis=1)
    imag_part = jnp.sum(cos_b * imag_in[None] - sin_b * real_in[None], axis=1)
    real_part, imag_part = rotate(
        real_part, imag_part, index, jnp.arange(block_len, dtype=jnp.int32), length
    )
    kept = block_len // 2 + 1
    cos_inner, sin_inner = phase_tables(
        jnp.arange(kept, dtype=jnp.int32), jnp.arange(block_len, dtype=jnp.int32), block_len
    )
    dims = (((1,), (1,)), ((), ()))

    def mat(table, value):
        return lax.dot_general(
            table, value, dims, precision=lax.Precision.HIGH,
            preferred_element_type=jnp.float32,
        )

    new_real = mat(cos_inner, real_part) + mat(sin_inner, imag_part)
    new_imag = mat(cos_inner, imag_part) - mat(sin_inner, real_part)
    new_real = (new_real.reshape(kept * devices_tm, columns) / samples).astype(jnp.bfloat16)
    new_imag = (new_imag.reshape(kept * devices_tm, columns) / samples).astype(jnp.bfloat16)
    return jnp.stack([new_real, new_imag])


def swap_blocks(blocks, axis, ordered):
    count = lax.axis_size(axis)
    if count > 8:
        received = lax.all_to_all(blocks, axis, 0, 0, tiled=True)
        return received if ordered else jnp.sum(received, axis=0)
    me = lax.axis_index(axis)
    arrived = [lax.dynamic_index_in_dim(blocks, me, 0, keepdims=False)]
    for shift in range(1, count):
        outgoing = lax.dynamic_index_in_dim(blocks, (me + shift) % count, 0, keepdims=False)
        pairs = [(src, (src + shift) % count) for src in range(count)]
        arrived.append(lax.ppermute(outgoing, axis, pairs))
    if not ordered:
        total = arrived[0]
        for part in arrived[1:]:
            total = total + part
        return total
    order = (me - jnp.arange(count, dtype=jnp.int32)) % count
    return jnp.take(jnp.stack(arrived), order, axis=0)


def packed_partials(real_in, imag_in, position, samples):
    devices_tm, block_len, columns = real_in.shape
    index = jnp.arange(devices_tm, dtype=jnp.int32)
    cos_table, sin_table = phase_tables(index, index, devices_tm)
    cos_b = cos_table[:, :, None, None]
    sin_b = sin_table[:, :, None, None]
    real_part = jnp.sum(cos_b * real_in[None] + sin_b * imag_in[None], axis=1)
    imag_part = jnp.sum(cos_b * imag_in[None] - sin_b * real_in[None], axis=1)
    local_epoch = position * block_len + jnp.arange(block_len, dtype=jnp.int32)
    real_part, imag_part = rotate(real_part, imag_part, index, local_epoch, samples)
    return jnp.stack([real_part, imag_part], axis=1)


def packed_transform(gathered):
    devices_tm, _, block_len, columns = gathered.shape
    length = devices_tm * block_len
    index = jnp.arange(devices_tm, dtype=jnp.int32)
    cos_table, sin_table = phase_tables(index, index, devices_tm)
    real_in = gathered[:, 0]
    imag_in = gathered[:, 1]
    cos_b = cos_table[:, :, None, None]
    sin_b = sin_table[:, :, None, None]
    real_part = jnp.sum(cos_b * real_in[None] + sin_b * imag_in[None], axis=1)
    imag_part = jnp.sum(cos_b * imag_in[None] - sin_b * real_in[None], axis=1)
    real_part, imag_part = rotate(
        real_part, imag_part, index, jnp.arange(block_len, dtype=jnp.int32), length
    )
    cos_inner, sin_inner = dft_tables(block_len)
    dims = (((1,), (1,)), ((), ()))

    def mat(table, value):
        return lax.dot_general(
            table, value, dims, precision=lax.Precision.HIGH,
            preferred_element_type=jnp.float32,
        )

    new_real = mat(cos_inner, real_part) + mat(sin_inner, imag_part)
    new_imag = mat(cos_inner, imag_part) - mat(sin_inner, real_part)
    return new_real.reshape(length, columns), new_imag.reshape(length, columns)


def unpack_spectra(real_z, imag_z, position, samples):
    devices_tm = lax.axis_size("tm")
    length = real_z.shape[0]
    kept = length // 2 + devices_tm
    stacked = jnp.stack([real_z, imag_z])
    backward = stacked[:, ::-1]
    shifted = jnp.roll(backward, 1, axis=1)
    outgoing = jnp.where(position == 0, shifted, backward)[:, :kept]
    pairs = [(src, (devices_tm - src) % devices_tm) for src in range(devices_tm)]
    mirror = lax.ppermute(outgoing, "tm", pairs)
    own_real = real_z[:kept]
    own_imag = imag_z[:kept]
    first_real = (own_real + mirror[0]) * 0.5
    first_imag = (own_imag - mirror[1]) * 0.5
    second_real = (own_imag + mirror[1]) * 0.5
    second_imag = (mirror[0] - own_real) * 0.5
    new_real = jnp.concatenate([first_real, second_real], axis=1) / samples
    new_imag = jnp.concatenate([first_imag, second_imag], axis=1) / samples
    return jnp.stack([new_real.astype(jnp.bfloat16), new_imag.astype(jnp.bfloat16)])


def body(orbit_angles, gap_mask, column_index, lat_coeffs, psd_table):
    devices_tm = lax.axis_size("tm")
    panels = lax.axis_size("panel")
    epochs = orbit_angles.shape[1]
    block_len = epochs // devices_tm
    samples = epochs * devices_tm
    columns = lat_coeffs.shape[2]
    coeffs = lat_coeffs[0]
    keep_rows = gap_mask.astype(jnp.float32)
    packed = jnp.concatenate([orbit_angles, keep_rows[None]], axis=0)
    packed = packed.reshape(3, devices_tm, block_len).transpose(1, 0, 2)
    received = swap_blocks(packed, "tm", True)
    flat_orbit = received.transpose(1, 0, 2).reshape(3, devices_tm * block_len)
    spread = synthesize(flat_orbit[0:2], flat_orbit[2], column_index, coeffs).reshape(
        devices_tm, block_len, columns
    )
    position = lax.axis_index("tm")
    half_cols = columns // 2
    twisted = packed_partials(spread[..., :half_cols], spread[..., half_cols:], position, samples)
    gathered = lax.all_to_all(twisted, "tm", 0, 0, tiled=True)
    real_z, imag_z = packed_transform(gathered)
    spectra = unpack_spectra(real_z, imag_z, position, samples)
    inverse_psd, fold = inverse_weights(
        psd_table[0], position, devices_tm, epochs, samples, spectra.shape[1]
    )
    weighted = (spectra.astype(jnp.float32) * inverse_psd[None, :, None]).astype(jnp.bfloat16)
    weighted = weighted * fold[None, :, None].astype(jnp.bfloat16)
    contract = (((0, 1), (0, 1)), ((), ()))
    products = [
        lax.dot_general(block, weighted, contract, preferred_element_type=jnp.float32)
        for block in panel_spectra(spectra)
    ]
    by_shift = jnp.stack(products)
    panel = lax.axis_index("panel")
    order = (panel - jnp.arange(panels, dtype=jnp.int32)) % panels
    partial_value = jnp.take(by_shift, order, axis=0).reshape(panels * columns, columns)
    return settle_rows(partial_value)


def settle_rows(partial_value):
    devices_tm = lax.axis_size("tm")
    comps = lax.axis_size("comp")
    rows_total, columns = partial_value.shape
    rows = rows_total // devices_tm
    if comps != 2 or columns % 256 != 0:
        pieces = lax.all_to_all(
            partial_value.reshape(devices_tm, rows, columns), "tm", 0, 0, tiled=True
        )
        return comp_sum(jnp.sum(pieces, axis=0))
    half = columns // 2
    comp = lax.axis_index("comp")
    mine = lax.dynamic_slice_in_dim(partial_value, comp * half, half, axis=1)
    theirs = lax.dynamic_slice_in_dim(partial_value, (1 - comp) * half, half, axis=1)
    summed = mine + lax.ppermute(theirs, "comp", [(0, 1), (1, 0)])
    block = swap_blocks(summed.reshape(devices_tm, rows, half), "tm", False)
    other = lax.ppermute(block, "comp", [(0, 1), (1, 0)])
    first = jnp.where(comp == 0, block, other)
    second = jnp.where(comp == 0, other, block)
    return jnp.concatenate([first, second], axis=1)


def solution(mesh):
    return jax.shard_map(
        body,
        mesh=mesh,
        in_specs=(
            P(None, ("groups", "tm")),
            P(("groups", "tm")),
            P(None, "panel"),
            P("comp", None, "panel"),
            P("comp", None),
        ),
        out_specs=P(("groups", "tm"), "panel"),
        check_vma=False,
    )
```

```python
import math

import jax
import jax.numpy as jnp
from jax import lax
from jax.sharding import PartitionSpec as P

SPLIT = 64


def synthesize(angles, keep_rows, column_index, coeffs):
    terms_lat = coeffs.shape[0] // 2
    colatitude = angles[0]
    longit = angles[1]
    wavenumbers = jnp.arange(terms_lat, dtype=jnp.float32)
    phases = colatitude[:, None] * wavenumbers[None, :]
    basis_rows = jnp.concatenate([jnp.cos(phases), jnp.sin(phases)], axis=1).astype(jnp.bfloat16)
    degree = column_index[0]
    orders = column_index[1]
    levels = jnp.arange(2 * terms_lat, dtype=jnp.int32) % terms_lat
    allowed = levels[:, None] <= degree[None, :]
    masked = jnp.where(allowed, coeffs, jnp.zeros_like(coeffs))
    latitude = jnp.dot(basis_rows, masked, preferred_element_type=jnp.float32)
    lon_phase = longit[:, None] * jnp.abs(orders).astype(jnp.float32)[None, :]
    lon_wave = jnp.where(orders[None, :] >= 0, jnp.cos(lon_phase), jnp.sin(lon_phase))
    norm_scale = 1.0 / jnp.sqrt(degree.astype(jnp.float32) + 1.0)
    return latitude * lon_wave * (keep_rows[:, None] * norm_scale[None, :])


def phase_tables(row_index, col_index, length):
    product = row_index[:, None] * col_index[None, :] % length
    angle_grid = product.astype(jnp.float32) * (2.0 * math.pi / length)
    return (jnp.cos(angle_grid), jnp.sin(angle_grid))


def dft_tables(length):
    indices = jnp.arange(length, dtype=jnp.int32)
    return phase_tables(indices, indices, length)


def rotate(real_part, imag_part, outer_index, inner_index, length):
    index_grid = outer_index[:, None] * inner_index[None, :] % length
    angle_grid = index_grid.astype(jnp.float32) * (2.0 * math.pi / length)
    cosine = jnp.cos(angle_grid)[:, :, None]
    sine_grid = jnp.sin(angle_grid)[:, :, None]
    return (real_part * cosine + imag_part * sine_grid, imag_part * cosine - real_part * sine_grid)


def precise_dot(left_side, right_side):
    return jnp.dot(
        left_side, right_side, precision=lax.Precision.HIGHEST, preferred_element_type=jnp.float32
    )


def transform(cos_table, sin_table, real_part, imag_part):
    new_real = precise_dot(cos_table, real_part) + precise_dot(sin_table, imag_part)
    new_imag = precise_dot(cos_table, imag_part) - precise_dot(sin_table, real_part)
    return (new_real, new_imag)


def four_step(real_in, imag_in, samples):
    length = real_in.shape[0]
    columns = real_in.shape[1]
    outer_count = SPLIT
    inner_count = length // SPLIT
    real_part = real_in.reshape(outer_count, inner_count * columns)
    imag_part = imag_in.reshape(outer_count, inner_count * columns)
    cos_outer, sin_outer = dft_tables(outer_count)
    real_part, imag_part = transform(cos_outer, sin_outer, real_part, imag_part)
    real_part = real_part.reshape(outer_count, inner_count, columns)
    imag_part = imag_part.reshape(outer_count, inner_count, columns)
    real_part, imag_part = rotate(
        real_part,
        imag_part,
        jnp.arange(outer_count, dtype=jnp.int32),
        jnp.arange(inner_count, dtype=jnp.int32),
        length,
    )
    real_part = jnp.transpose(real_part, (1, 0, 2)).reshape(inner_count, outer_count * columns)
    imag_part = jnp.transpose(imag_part, (1, 0, 2)).reshape(inner_count, outer_count * columns)
    cos_inner, sin_inner = dft_tables(inner_count)
    real_part, imag_part = transform(cos_inner, sin_inner, real_part, imag_part)
    return (
        real_part.reshape(length, columns) / samples,
        imag_part.reshape(length, columns) / samples,
    )


def local_transform(received, samples):
    real_part, imag_part = four_step(received[0, 0], received[1, 0], samples)
    return (real_part.astype(jnp.bfloat16), imag_part.astype(jnp.bfloat16))


def inverse_weights(psd_row, position, devices_tm, epochs, samples, count):
    half = samples // 2
    mirrored = jnp.concatenate([psd_row[: half + 1], psd_row[1:half][::-1]])
    picked = lax.dynamic_slice_in_dim(mirrored.reshape(epochs, devices_tm), position, 1, axis=1)
    inverse = 8192.0 / picked[:count, 0].astype(jnp.float32)
    order = jnp.arange(count, dtype=jnp.int32)
    first = jnp.where(position == 0, 1.0, 2.0)
    middle = jnp.where(position == 0, 1.0, 0.0)
    fold = jnp.where(
        order == 0, first, jnp.where(order < epochs // 2, 2.0, jnp.where(order == epochs // 2, middle, 0.0))
    )
    return inverse, fold


def panel_spectra(spectra):
    panels = lax.axis_size("panel")
    blocks = [spectra]
    for shift in range(1, panels):
        pairs = [(src, (src + shift) % panels) for src in range(panels)]
        blocks.append(lax.ppermute(spectra, "panel", pairs))
    return blocks


def comp_sum(value):
    comps = lax.axis_size("comp")
    if comps == 1:
        return value
    if comps != 2:
        return lax.psum(value, "comp")
    other = lax.ppermute(value, "comp", [(0, 1), (1, 0)])
    return value + other


def class_partials(spread, position, samples):
    devices_tm, block_len, columns = spread.shape
    index = jnp.arange(devices_tm, dtype=jnp.int32)
    cos_table, sin_table = phase_tables(index, index, devices_tm)
    real_part = jnp.sum(cos_table[:, :, None, None] * spread[None], axis=1)
    imag_part = -jnp.sum(sin_table[:, :, None, None] * spread[None], axis=1)
    local_epoch = position * block_len + jnp.arange(block_len, dtype=jnp.int32)
    real_part, imag_part = rotate(real_part, imag_part, index, local_epoch, samples)
    return jnp.stack([real_part, imag_part], axis=1)


def class_spectrum(gathered, samples):
    devices_tm, _, block_len, columns = gathered.shape
    length = devices_tm * block_len
    index = jnp.arange(devices_tm, dtype=jnp.int32)
    cos_table, sin_table = phase_tables(index, index, devices_tm)
    real_in = gathered[:, 0]
    imag_in = gathered[:, 1]
    cos_b = cos_table[:, :, None, None]
    sin_b = sin_table[:, :, None, None]
    real_part = jnp.sum(cos_b * real_in[None] + sin_b * imag_in[None], axis=1)
    imag_part = jnp.sum(cos_b * imag_in[None] - sin_b * real_in[None], axis=1)
    real_part, imag_part = rotate(
        real_part, imag_part, index, jnp.arange(block_len, dtype=jnp.int32), length
    )
    kept = block_len // 2 + 1
    cos_inner, sin_inner = phase_tables(
        jnp.arange(kept, dtype=jnp.int32), jnp.arange(block_len, dtype=jnp.int32), block_len
    )
    dims = (((1,), (1,)), ((), ()))

    def mat(table, value):
        return lax.dot_general(
            table, value, dims, precision=lax.Precision.HIGH,
            preferred_element_type=jnp.float32,
        )

    new_real = mat(cos_inner, real_part) + mat(sin_inner, imag_part)
    new_imag = mat(cos_inner, imag_part) - mat(sin_inner, real_part)
    new_real = (new_real.reshape(kept * devices_tm, columns) / samples).astype(jnp.bfloat16)
    new_imag = (new_imag.reshape(kept * devices_tm, columns) / samples).astype(jnp.bfloat16)
    return jnp.stack([new_real, new_imag])


def swap_blocks(blocks, axis, ordered):
    count = lax.axis_size(axis)
    if count > 8:
        received = lax.all_to_all(blocks, axis, 0, 0, tiled=True)
        return received if ordered else jnp.sum(received, axis=0)
    me = lax.axis_index(axis)
    arrived = [lax.dynamic_index_in_dim(blocks, me, 0, keepdims=False)]
    for shift in range(1, count):
        outgoing = lax.dynamic_index_in_dim(blocks, (me + shift) % count, 0, keepdims=False)
        pairs = [(src, (src + shift) % count) for src in range(count)]
        arrived.append(lax.ppermute(outgoing, axis, pairs))
    if not ordered:
        total = arrived[0]
        for part in arrived[1:]:
            total = total + part
        return total
    order = (me - jnp.arange(count, dtype=jnp.int32)) % count
    return jnp.take(jnp.stack(arrived), order, axis=0)


def packed_partials(real_in, imag_in, position, samples):
    devices_tm, block_len, columns = real_in.shape
    index = jnp.arange(devices_tm, dtype=jnp.int32)
    cos_table, sin_table = phase_tables(index, index, devices_tm)
    cos_b = cos_table[:, :, None, None]
    sin_b = sin_table[:, :, None, None]
    real_part = jnp.sum(cos_b * real_in[None] + sin_b * imag_in[None], axis=1)
    imag_part = jnp.sum(cos_b * imag_in[None] - sin_b * real_in[None], axis=1)
    local_epoch = position * block_len + jnp.arange(block_len, dtype=jnp.int32)
    real_part, imag_part = rotate(real_part, imag_part, index, local_epoch, samples)
    return jnp.stack([real_part, imag_part], axis=1)


def packed_transform(gathered):
    devices_tm, _, block_len, columns = gathered.shape
    length = devices_tm * block_len
    index = jnp.arange(devices_tm, dtype=jnp.int32)
    cos_table, sin_table = phase_tables(index, index, devices_tm)
    real_in = gathered[:, 0]
    imag_in = gathered[:, 1]
    cos_b = cos_table[:, :, None, None]
    sin_b = sin_table[:, :, None, None]
    real_part = jnp.sum(cos_b * real_in[None] + sin_b * imag_in[None], axis=1)
    imag_part = jnp.sum(cos_b * imag_in[None] - sin_b * real_in[None], axis=1)
    real_part, imag_part = rotate(
        real_part, imag_part, index, jnp.arange(block_len, dtype=jnp.int32), length
    )
    kept = block_len // 2 + 1
    rows = jnp.arange(kept, dtype=jnp.int32)
    cols = jnp.arange(block_len, dtype=jnp.int32)
    cos_own, sin_own = phase_tables(rows, cols, block_len)
    cos_far, sin_far = phase_tables(block_len - 1 - rows, cols, block_len)
    dims = (((1,), (1,)), ((), ()))

    def mat(table, value):
        return lax.dot_general(
            table, value, dims, precision=lax.Precision.HIGH,
            preferred_element_type=jnp.float32,
        )

    def apply(cos_table, sin_table, real_in, imag_in):
        new_real = mat(cos_table, real_in) + mat(sin_table, imag_in)
        new_imag = mat(cos_table, imag_in) - mat(sin_table, real_in)
        return jnp.stack([new_real, new_imag]).reshape(2, kept * devices_tm, columns)

    own = apply(cos_own, sin_own, real_part, imag_part)
    far = apply(cos_far, sin_far, real_part[::-1], imag_part[::-1])
    return own, far


def unpack_spectra(own, far, position, samples):
    devices_tm = lax.axis_size("tm")
    shifted = jnp.concatenate([own[:, :1], far[:, :-1]], axis=1)
    outgoing = jnp.where(position == 0, shifted, far)
    pairs = [(src, (devices_tm - src) % devices_tm) for src in range(devices_tm)]
    mirror = lax.ppermute(outgoing, "tm", pairs)
    own_real = own[0]
    own_imag = own[1]
    first_real = (own_real + mirror[0]) * 0.5
    first_imag = (own_imag - mirror[1]) * 0.5
    second_real = (own_imag + mirror[1]) * 0.5
    second_imag = (mirror[0] - own_real) * 0.5
    new_real = jnp.concatenate([first_real, second_real], axis=1) / samples
    new_imag = jnp.concatenate([first_imag, second_imag], axis=1) / samples
    return jnp.stack([new_real.astype(jnp.bfloat16), new_imag.astype(jnp.bfloat16)])


def body(orbit_angles, gap_mask, column_index, lat_coeffs, psd_table):
    devices_tm = lax.axis_size("tm")
    panels = lax.axis_size("panel")
    epochs = orbit_angles.shape[1]
    block_len = epochs // devices_tm
    samples = epochs * devices_tm
    columns = lat_coeffs.shape[2]
    coeffs = lat_coeffs[0]
    keep_rows = gap_mask.astype(jnp.float32)
    packed = jnp.concatenate([orbit_angles, keep_rows[None]], axis=0)
    packed = packed.reshape(3, devices_tm, block_len).transpose(1, 0, 2)
    received = swap_blocks(packed, "tm", True)
    flat_orbit = received.transpose(1, 0, 2).reshape(3, devices_tm * block_len)
    spread = synthesize(flat_orbit[0:2], flat_orbit[2], column_index, coeffs).reshape(
        devices_tm, block_len, columns
    )
    position = lax.axis_index("tm")
    half_cols = columns // 2
    twisted = packed_partials(spread[..., :half_cols], spread[..., half_cols:], position, samples)
    gathered = lax.all_to_all(twisted, "tm", 0, 0, tiled=True)
    own, far = packed_transform(gathered)
    spectra = unpack_spectra(own, far, position, samples)
    inverse_psd, fold = inverse_weights(
        psd_table[0], position, devices_tm, epochs, samples, spectra.shape[1]
    )
    weighted = (spectra.astype(jnp.float32) * inverse_psd[None, :, None]).astype(jnp.bfloat16)
    weighted = weighted * fold[None, :, None].astype(jnp.bfloat16)
    contract = (((0, 1), (0, 1)), ((), ()))
    products = [
        lax.dot_general(block, weighted, contract, preferred_element_type=jnp.float32)
        for block in panel_spectra(spectra)
    ]
    by_shift = jnp.stack(products)
    panel = lax.axis_index("panel")
    order = (panel - jnp.arange(panels, dtype=jnp.int32)) % panels
    partial_value = jnp.take(by_shift, order, axis=0).reshape(panels * columns, columns)
    return settle_rows(partial_value)


def settle_rows(partial_value):
    devices_tm = lax.axis_size("tm")
    comps = lax.axis_size("comp")
    rows_total, columns = partial_value.shape
    rows = rows_total // devices_tm
    if comps != 2 or columns % 256 != 0:
        pieces = lax.all_to_all(
            partial_value.reshape(devices_tm, rows, columns), "tm", 0, 0, tiled=True
        )
        return comp_sum(jnp.sum(pieces, axis=0))
    half = columns // 2
    comp = lax.axis_index("comp")
    mine = lax.dynamic_slice_in_dim(partial_value, comp * half, half, axis=1)
    theirs = lax.dynamic_slice_in_dim(partial_value, (1 - comp) * half, half, axis=1)
    summed = mine + lax.ppermute(theirs, "comp", [(0, 1), (1, 0)])
    block = swap_blocks(summed.reshape(devices_tm, rows, half), "tm", False)
    other = lax.ppermute(block, "comp", [(0, 1), (1, 0)])
    first = jnp.where(comp == 0, block, other)
    second = jnp.where(comp == 0, other, block)
    return jnp.concatenate([first, second], axis=1)


def solution(mesh):
    return jax.shard_map(
        body,
        mesh=mesh,
        in_specs=(
            P(None, ("groups", "tm")),
            P(("groups", "tm")),
            P(None, "panel"),
            P("comp", None, "panel"),
            P("comp", None),
        ),
        out_specs=P(("groups", "tm"), "panel"),
        check_vma=False,
    )
```

```python
import math

import jax
import jax.numpy as jnp
from jax import lax
from jax.sharding import PartitionSpec as P

SPLIT = 64


def rounding_error(value, factor, product):
    high = lax.reduce_precision(value, exponent_bits=8, mantissa_bits=11)
    low = value - high
    return (product - high * factor) - low * factor


def colatitude_basis(colatitude, terms):
    wavenumbers = jnp.arange(terms, dtype=jnp.float32)
    theta = colatitude[:, None]
    phases = lax.optimization_barrier(theta * wavenumbers[None, :])
    if terms % 16 != 0:
        return jnp.concatenate([jnp.cos(phases), jnp.sin(phases)], axis=1)
    groups = terms // 16
    coarse = jnp.arange(groups, dtype=jnp.float32) * 16.0
    fine = jnp.arange(16, dtype=jnp.float32)
    phase_a = lax.optimization_barrier(theta * coarse[None, :])
    phase_b = lax.optimization_barrier(theta * fine[None, :])
    count = colatitude.shape[0]
    delta = (
        rounding_error(theta, wavenumbers[None, :], phases).reshape(count, groups, 16)
        - rounding_error(theta, coarse[None, :], phase_a)[:, :, None]
        - rounding_error(theta, fine[None, :], phase_b)[:, None, :]
    )
    cos_a = jnp.cos(phase_a)[:, :, None]
    sin_a = jnp.sin(phase_a)[:, :, None]
    cos_b = jnp.cos(phase_b)[:, None, :]
    sin_b = jnp.sin(phase_b)[:, None, :]
    cos_sum = cos_a * cos_b - sin_a * sin_b
    sin_sum = sin_a * cos_b + cos_a * sin_b
    cos_k = (cos_sum - delta * sin_sum).reshape(count, terms)
    sin_k = (sin_sum + delta * cos_sum).reshape(count, terms)
    return jnp.concatenate([cos_k, sin_k], axis=1)


def synthesize(angles, keep_rows, column_index, coeffs):
    terms_lat = coeffs.shape[0] // 2
    colatitude = angles[0]
    longit = angles[1]
    basis_rows = colatitude_basis(colatitude, terms_lat).astype(jnp.bfloat16)
    degree = column_index[0]
    orders = column_index[1]
    levels = jnp.arange(2 * terms_lat, dtype=jnp.int32) % terms_lat
    allowed = levels[:, None] <= degree[None, :]
    masked = jnp.where(allowed, coeffs, jnp.zeros_like(coeffs))
    latitude = jnp.dot(basis_rows, masked, preferred_element_type=jnp.float32)
    lon_phase = longit[:, None] * jnp.abs(orders).astype(jnp.float32)[None, :]
    lon_wave = jnp.where(orders[None, :] >= 0, jnp.cos(lon_phase), jnp.sin(lon_phase))
    norm_scale = 1.0 / jnp.sqrt(degree.astype(jnp.float32) + 1.0)
    return latitude * lon_wave * (keep_rows[:, None] * norm_scale[None, :])


def phase_tables(row_index, col_index, length):
    product = row_index[:, None] * col_index[None, :] % length
    angle_grid = product.astype(jnp.float32) * (2.0 * math.pi / length)
    return (jnp.cos(angle_grid), jnp.sin(angle_grid))


def dft_tables(length):
    indices = jnp.arange(length, dtype=jnp.int32)
    return phase_tables(indices, indices, length)


def rotate(real_part, imag_part, outer_index, inner_index, length):
    index_grid = outer_index[:, None] * inner_index[None, :] % length
    angle_grid = index_grid.astype(jnp.float32) * (2.0 * math.pi / length)
    cosine = jnp.cos(angle_grid)[:, :, None]
    sine_grid = jnp.sin(angle_grid)[:, :, None]
    return (real_part * cosine + imag_part * sine_grid, imag_part * cosine - real_part * sine_grid)


def precise_dot(left_side, right_side):
    return jnp.dot(
        left_side, right_side, precision=lax.Precision.HIGHEST, preferred_element_type=jnp.float32
    )


def transform(cos_table, sin_table, real_part, imag_part):
    new_real = precise_dot(cos_table, real_part) + precise_dot(sin_table, imag_part)
    new_imag = precise_dot(cos_table, imag_part) - precise_dot(sin_table, real_part)
    return (new_real, new_imag)


def four_step(real_in, imag_in, samples):
    length = real_in.shape[0]
    columns = real_in.shape[1]
    outer_count = SPLIT
    inner_count = length // SPLIT
    real_part = real_in.reshape(outer_count, inner_count * columns)
    imag_part = imag_in.reshape(outer_count, inner_count * columns)
    cos_outer, sin_outer = dft_tables(outer_count)
    real_part, imag_part = transform(cos_outer, sin_outer, real_part, imag_part)
    real_part = real_part.reshape(outer_count, inner_count, columns)
    imag_part = imag_part.reshape(outer_count, inner_count, columns)
    real_part, imag_part = rotate(
        real_part,
        imag_part,
        jnp.arange(outer_count, dtype=jnp.int32),
        jnp.arange(inner_count, dtype=jnp.int32),
        length,
    )
    real_part = jnp.transpose(real_part, (1, 0, 2)).reshape(inner_count, outer_count * columns)
    imag_part = jnp.transpose(imag_part, (1, 0, 2)).reshape(inner_count, outer_count * columns)
    cos_inner, sin_inner = dft_tables(inner_count)
    real_part, imag_part = transform(cos_inner, sin_inner, real_part, imag_part)
    return (
        real_part.reshape(length, columns) / samples,
        imag_part.reshape(length, columns) / samples,
    )


def local_transform(received, samples):
    real_part, imag_part = four_step(received[0, 0], received[1, 0], samples)
    return (real_part.astype(jnp.bfloat16), imag_part.astype(jnp.bfloat16))


def inverse_weights(psd_row, position, devices_tm, epochs, samples, count):
    half = samples // 2
    mirrored = jnp.concatenate([psd_row[: half + 1], psd_row[1:half][::-1]])
    picked = lax.dynamic_slice_in_dim(mirrored.reshape(epochs, devices_tm), position, 1, axis=1)
    inverse = 8192.0 / picked[:count, 0].astype(jnp.float32)
    order = jnp.arange(count, dtype=jnp.int32)
    first = jnp.where(position == 0, 1.0, 2.0)
    middle = jnp.where(position == 0, 1.0, 0.0)
    fold = jnp.where(
        order == 0, first, jnp.where(order < epochs // 2, 2.0, jnp.where(order == epochs // 2, middle, 0.0))
    )
    return inverse, fold


def panel_spectra(spectra):
    panels = lax.axis_size("panel")
    blocks = [spectra]
    for shift in range(1, panels):
        pairs = [(src, (src + shift) % panels) for src in range(panels)]
        blocks.append(lax.ppermute(spectra, "panel", pairs))
    return blocks


def comp_sum(value):
    comps = lax.axis_size("comp")
    if comps == 1:
        return value
    if comps != 2:
        return lax.psum(value, "comp")
    other = lax.ppermute(value, "comp", [(0, 1), (1, 0)])
    return value + other


def class_partials(spread, position, samples):
    devices_tm, block_len, columns = spread.shape
    index = jnp.arange(devices_tm, dtype=jnp.int32)
    cos_table, sin_table = phase_tables(index, index, devices_tm)
    real_part = jnp.sum(cos_table[:, :, None, None] * spread[None], axis=1)
    imag_part = -jnp.sum(sin_table[:, :, None, None] * spread[None], axis=1)
    local_epoch = position * block_len + jnp.arange(block_len, dtype=jnp.int32)
    real_part, imag_part = rotate(real_part, imag_part, index, local_epoch, samples)
    return jnp.stack([real_part, imag_part], axis=1)


def class_spectrum(gathered, samples):
    devices_tm, _, block_len, columns = gathered.shape
    length = devices_tm * block_len
    index = jnp.arange(devices_tm, dtype=jnp.int32)
    cos_table, sin_table = phase_tables(index, index, devices_tm)
    real_in = gathered[:, 0]
    imag_in = gathered[:, 1]
    cos_b = cos_table[:, :, None, None]
    sin_b = sin_table[:, :, None, None]
    real_part = jnp.sum(cos_b * real_in[None] + sin_b * imag_in[None], axis=1)
    imag_part = jnp.sum(cos_b * imag_in[None] - sin_b * real_in[None], axis=1)
    real_part, imag_part = rotate(
        real_part, imag_part, index, jnp.arange(block_len, dtype=jnp.int32), length
    )
    kept = block_len // 2 + 1
    cos_inner, sin_inner = phase_tables(
        jnp.arange(kept, dtype=jnp.int32), jnp.arange(block_len, dtype=jnp.int32), block_len
    )
    dims = (((1,), (1,)), ((), ()))

    def mat(table, value):
        return lax.dot_general(
            table, value, dims, precision=lax.Precision.HIGH,
            preferred_element_type=jnp.float32,
        )

    new_real = mat(cos_inner, real_part) + mat(sin_inner, imag_part)
    new_imag = mat(cos_inner, imag_part) - mat(sin_inner, real_part)
    new_real = (new_real.reshape(kept * devices_tm, columns) / samples).astype(jnp.bfloat16)
    new_imag = (new_imag.reshape(kept * devices_tm, columns) / samples).astype(jnp.bfloat16)
    return jnp.stack([new_real, new_imag])


def swap_blocks(blocks, axis, ordered):
    count = lax.axis_size(axis)
    if count > 8:
        received = lax.all_to_all(blocks, axis, 0, 0, tiled=True)
        return received if ordered else jnp.sum(received, axis=0)
    me = lax.axis_index(axis)
    arrived = [lax.dynamic_index_in_dim(blocks, me, 0, keepdims=False)]
    for shift in range(1, count):
        outgoing = lax.dynamic_index_in_dim(blocks, (me + shift) % count, 0, keepdims=False)
        pairs = [(src, (src + shift) % count) for src in range(count)]
        arrived.append(lax.ppermute(outgoing, axis, pairs))
    if not ordered:
        total = arrived[0]
        for part in arrived[1:]:
            total = total + part
        return total
    order = (me - jnp.arange(count, dtype=jnp.int32)) % count
    return jnp.take(jnp.stack(arrived), order, axis=0)


def packed_partials(real_in, imag_in, position, samples):
    devices_tm, block_len, columns = real_in.shape
    index = jnp.arange(devices_tm, dtype=jnp.int32)
    cos_table, sin_table = phase_tables(index, index, devices_tm)
    cos_b = cos_table[:, :, None, None]
    sin_b = sin_table[:, :, None, None]
    real_part = jnp.sum(cos_b * real_in[None] + sin_b * imag_in[None], axis=1)
    imag_part = jnp.sum(cos_b * imag_in[None] - sin_b * real_in[None], axis=1)
    local_epoch = position * block_len + jnp.arange(block_len, dtype=jnp.int32)
    real_part, imag_part = rotate(real_part, imag_part, index, local_epoch, samples)
    return jnp.stack([real_part, imag_part], axis=1)


def packed_transform(gathered):
    devices_tm, _, block_len, columns = gathered.shape
    length = devices_tm * block_len
    index = jnp.arange(devices_tm, dtype=jnp.int32)
    cos_table, sin_table = phase_tables(index, index, devices_tm)
    real_in = gathered[:, 0]
    imag_in = gathered[:, 1]
    cos_b = cos_table[:, :, None, None]
    sin_b = sin_table[:, :, None, None]
    real_part = jnp.sum(cos_b * real_in[None] + sin_b * imag_in[None], axis=1)
    imag_part = jnp.sum(cos_b * imag_in[None] - sin_b * real_in[None], axis=1)
    real_part, imag_part = rotate(
        real_part, imag_part, index, jnp.arange(block_len, dtype=jnp.int32), length
    )
    kept = block_len // 2 + 1
    rows = jnp.arange(kept, dtype=jnp.int32)
    cols = jnp.arange(block_len, dtype=jnp.int32)
    cos_own, sin_own = phase_tables(rows, cols, block_len)
    cos_far, sin_far = phase_tables(block_len - 1 - rows, cols, block_len)
    dims = (((1,), (1,)), ((), ()))

    def mat(table, value):
        return lax.dot_general(
            table, value, dims, precision=lax.Precision.HIGH,
            preferred_element_type=jnp.float32,
        )

    def apply(cos_table, sin_table, real_in, imag_in):
        table = jnp.concatenate([cos_table, sin_table], axis=0)
        from_real = mat(table, real_in)
        from_imag = mat(table, imag_in)
        new_real = from_real[:kept] + from_imag[kept:]
        new_imag = from_imag[:kept] - from_real[kept:]
        return jnp.stack([new_real, new_imag]).reshape(2, kept * devices_tm, columns)

    own = apply(cos_own, sin_own, real_part, imag_part)
    far = apply(cos_far, sin_far, real_part[::-1], imag_part[::-1])
    return own, far


def unpack_spectra(own, far, position, samples):
    devices_tm = lax.axis_size("tm")
    shifted = jnp.concatenate([own[:, :1], far[:, :-1]], axis=1)
    outgoing = jnp.where(position == 0, shifted, far)
    pairs = [(src, (devices_tm - src) % devices_tm) for src in range(devices_tm)]
    mirror = lax.ppermute(outgoing, "tm", pairs)
    own_real = own[0]
    own_imag = own[1]
    first_real = (own_real + mirror[0]) * 0.5
    first_imag = (own_imag - mirror[1]) * 0.5
    second_real = (own_imag + mirror[1]) * 0.5
    second_imag = (mirror[0] - own_real) * 0.5
    new_real = jnp.concatenate([first_real, second_real], axis=1) / samples
    new_imag = jnp.concatenate([first_imag, second_imag], axis=1) / samples
    return jnp.stack([new_real.astype(jnp.bfloat16), new_imag.astype(jnp.bfloat16)])


def body(orbit_angles, gap_mask, column_index, lat_coeffs, psd_table):
    devices_tm = lax.axis_size("tm")
    panels = lax.axis_size("panel")
    epochs = orbit_angles.shape[1]
    block_len = epochs // devices_tm
    samples = epochs * devices_tm
    columns = lat_coeffs.shape[2]
    coeffs = lat_coeffs[0]
    keep_rows = gap_mask.astype(jnp.float32)
    packed = jnp.concatenate([orbit_angles, keep_rows[None]], axis=0)
    packed = packed.reshape(3, devices_tm, block_len).transpose(1, 0, 2)
    received = swap_blocks(packed, "tm", True)
    flat_orbit = received.transpose(1, 0, 2).reshape(3, devices_tm * block_len)
    spread = synthesize(flat_orbit[0:2], flat_orbit[2], column_index, coeffs).reshape(
        devices_tm, block_len, columns
    )
    position = lax.axis_index("tm")
    half_cols = columns // 2
    twisted = packed_partials(spread[..., :half_cols], spread[..., half_cols:], position, samples)
    gathered = lax.all_to_all(twisted, "tm", 0, 0, tiled=True)
    own, far = packed_transform(gathered)
    spectra = unpack_spectra(own, far, position, samples)
    inverse_psd, fold = inverse_weights(
        psd_table[0], position, devices_tm, epochs, samples, spectra.shape[1]
    )
    weighted = (spectra.astype(jnp.float32) * inverse_psd[None, :, None]).astype(jnp.bfloat16)
    weighted = weighted * fold[None, :, None].astype(jnp.bfloat16)
    contract = (((0, 1), (0, 1)), ((), ()))
    products = [
        lax.dot_general(block, weighted, contract, preferred_element_type=jnp.float32)
        for block in panel_spectra(spectra)
    ]
    by_shift = jnp.stack(products)
    panel = lax.axis_index("panel")
    order = (panel - jnp.arange(panels, dtype=jnp.int32)) % panels
    partial_value = jnp.take(by_shift, order, axis=0).reshape(panels * columns, columns)
    return settle_rows(partial_value)


def settle_rows(partial_value):
    devices_tm = lax.axis_size("tm")
    comps = lax.axis_size("comp")
    rows_total, columns = partial_value.shape
    rows = rows_total // devices_tm
    if comps != 2 or columns % 256 != 0:
        pieces = lax.all_to_all(
            partial_value.reshape(devices_tm, rows, columns), "tm", 0, 0, tiled=True
        )
        return comp_sum(jnp.sum(pieces, axis=0))
    half = columns // 2
    comp = lax.axis_index("comp")
    mine = lax.dynamic_slice_in_dim(partial_value, comp * half, half, axis=1)
    theirs = lax.dynamic_slice_in_dim(partial_value, (1 - comp) * half, half, axis=1)
    summed = mine + lax.ppermute(theirs, "comp", [(0, 1), (1, 0)])
    block = swap_blocks(summed.reshape(devices_tm, rows, half), "tm", False)
    other = lax.ppermute(block, "comp", [(0, 1), (1, 0)])
    first = jnp.where(comp == 0, block, other)
    second = jnp.where(comp == 0, other, block)
    return jnp.concatenate([first, second], axis=1)


def solution(mesh):
    return jax.shard_map(
        body,
        mesh=mesh,
        in_specs=(
            P(None, ("groups", "tm")),
            P(("groups", "tm")),
            P(None, "panel"),
            P("comp", None, "panel"),
            P("comp", None),
        ),
        out_specs=P(("groups", "tm"), "panel"),
        check_vma=False,
    )
```

```python
import math

import jax
import jax.numpy as jnp
from jax import lax
from jax.sharding import PartitionSpec as P

SPLIT = 64


def rounding_error(value, factor, product):
    high = lax.reduce_precision(value, exponent_bits=8, mantissa_bits=11)
    low = value - high
    return (product - high * factor) - low * factor


def colatitude_basis(colatitude, terms):
    wavenumbers = jnp.arange(terms, dtype=jnp.float32)
    theta = colatitude[:, None]
    phases = lax.optimization_barrier(theta * wavenumbers[None, :])
    if terms % 16 != 0:
        return jnp.concatenate([jnp.cos(phases), jnp.sin(phases)], axis=1)
    groups = terms // 16
    coarse = jnp.arange(groups, dtype=jnp.float32) * 16.0
    fine = jnp.arange(16, dtype=jnp.float32)
    phase_a = lax.optimization_barrier(theta * coarse[None, :])
    phase_b = lax.optimization_barrier(theta * fine[None, :])
    count = colatitude.shape[0]
    delta = (
        rounding_error(theta, wavenumbers[None, :], phases).reshape(count, groups, 16)
        - rounding_error(theta, coarse[None, :], phase_a)[:, :, None]
        - rounding_error(theta, fine[None, :], phase_b)[:, None, :]
    )
    cos_a = jnp.cos(phase_a)[:, :, None]
    sin_a = jnp.sin(phase_a)[:, :, None]
    cos_b = jnp.cos(phase_b)[:, None, :]
    sin_b = jnp.sin(phase_b)[:, None, :]
    cos_sum = cos_a * cos_b - sin_a * sin_b
    sin_sum = sin_a * cos_b + cos_a * sin_b
    cos_k = (cos_sum - delta * sin_sum).reshape(count, terms)
    sin_k = (sin_sum + delta * cos_sum).reshape(count, terms)
    return jnp.concatenate([cos_k, sin_k], axis=1)


def synthesize(angles, keep_rows, column_index, coeffs):
    terms_lat = coeffs.shape[0] // 2
    colatitude = angles[0]
    longit = angles[1]
    basis_rows = colatitude_basis(colatitude, terms_lat).astype(jnp.bfloat16)
    degree = column_index[0]
    orders = column_index[1]
    levels = jnp.arange(2 * terms_lat, dtype=jnp.int32) % terms_lat
    allowed = levels[:, None] <= degree[None, :]
    masked = jnp.where(allowed, coeffs, jnp.zeros_like(coeffs))
    latitude = jnp.dot(basis_rows, masked, preferred_element_type=jnp.float32)
    lon_phase = longit[:, None] * jnp.abs(orders).astype(jnp.float32)[None, :]
    lon_wave = jnp.where(orders[None, :] >= 0, jnp.cos(lon_phase), jnp.sin(lon_phase))
    norm_scale = 1.0 / jnp.sqrt(degree.astype(jnp.float32) + 1.0)
    return latitude * lon_wave * (keep_rows[:, None] * norm_scale[None, :])


def phase_tables(row_index, col_index, length):
    product = row_index[:, None] * col_index[None, :] % length
    angle_grid = product.astype(jnp.float32) * (2.0 * math.pi / length)
    return (jnp.cos(angle_grid), jnp.sin(angle_grid))


def dft_tables(length):
    indices = jnp.arange(length, dtype=jnp.int32)
    return phase_tables(indices, indices, length)


def rotate(real_part, imag_part, outer_index, inner_index, length):
    index_grid = outer_index[:, None] * inner_index[None, :] % length
    angle_grid = index_grid.astype(jnp.float32) * (2.0 * math.pi / length)
    cosine = jnp.cos(angle_grid)[:, :, None]
    sine_grid = jnp.sin(angle_grid)[:, :, None]
    return (real_part * cosine + imag_part * sine_grid, imag_part * cosine - real_part * sine_grid)


def precise_dot(left_side, right_side):
    return jnp.dot(
        left_side, right_side, precision=lax.Precision.HIGHEST, preferred_element_type=jnp.float32
    )


def transform(cos_table, sin_table, real_part, imag_part):
    new_real = precise_dot(cos_table, real_part) + precise_dot(sin_table, imag_part)
    new_imag = precise_dot(cos_table, imag_part) - precise_dot(sin_table, real_part)
    return (new_real, new_imag)


def four_step(real_in, imag_in, samples):
    length = real_in.shape[0]
    columns = real_in.shape[1]
    outer_count = SPLIT
    inner_count = length // SPLIT
    real_part = real_in.reshape(outer_count, inner_count * columns)
    imag_part = imag_in.reshape(outer_count, inner_count * columns)
    cos_outer, sin_outer = dft_tables(outer_count)
    real_part, imag_part = transform(cos_outer, sin_outer, real_part, imag_part)
    real_part = real_part.reshape(outer_count, inner_count, columns)
    imag_part = imag_part.reshape(outer_count, inner_count, columns)
    real_part, imag_part = rotate(
        real_part,
        imag_part,
        jnp.arange(outer_count, dtype=jnp.int32),
        jnp.arange(inner_count, dtype=jnp.int32),
        length,
    )
    real_part = jnp.transpose(real_part, (1, 0, 2)).reshape(inner_count, outer_count * columns)
    imag_part = jnp.transpose(imag_part, (1, 0, 2)).reshape(inner_count, outer_count * columns)
    cos_inner, sin_inner = dft_tables(inner_count)
    real_part, imag_part = transform(cos_inner, sin_inner, real_part, imag_part)
    return (
        real_part.reshape(length, columns) / samples,
        imag_part.reshape(length, columns) / samples,
    )


def local_transform(received, samples):
    real_part, imag_part = four_step(received[0, 0], received[1, 0], samples)
    return (real_part.astype(jnp.bfloat16), imag_part.astype(jnp.bfloat16))


def inverse_weights(psd_row, position, devices_tm, epochs, samples, count):
    half = samples // 2
    mirrored = jnp.concatenate([psd_row[: half + 1], psd_row[1:half][::-1]])
    picked = lax.dynamic_slice_in_dim(mirrored.reshape(epochs, devices_tm), position, 1, axis=1)
    inverse = 8192.0 / picked[:count, 0].astype(jnp.float32)
    order = jnp.arange(count, dtype=jnp.int32)
    first = jnp.where(position == 0, 1.0, 2.0)
    middle = jnp.where(position == 0, 1.0, 0.0)
    fold = jnp.where(
        order == 0, first, jnp.where(order < epochs // 2, 2.0, jnp.where(order == epochs // 2, middle, 0.0))
    )
    return inverse, fold


def panel_spectra(spectra):
    panels = lax.axis_size("panel")
    blocks = [spectra]
    for shift in range(1, panels):
        pairs = [(src, (src + shift) % panels) for src in range(panels)]
        blocks.append(lax.ppermute(spectra, "panel", pairs))
    return blocks


def comp_sum(value):
    comps = lax.axis_size("comp")
    if comps == 1:
        return value
    if comps != 2:
        return lax.psum(value, "comp")
    other = lax.ppermute(value, "comp", [(0, 1), (1, 0)])
    return value + other


def class_partials(spread, position, samples):
    devices_tm, block_len, columns = spread.shape
    index = jnp.arange(devices_tm, dtype=jnp.int32)
    cos_table, sin_table = phase_tables(index, index, devices_tm)
    real_part = jnp.sum(cos_table[:, :, None, None] * spread[None], axis=1)
    imag_part = -jnp.sum(sin_table[:, :, None, None] * spread[None], axis=1)
    local_epoch = position * block_len + jnp.arange(block_len, dtype=jnp.int32)
    real_part, imag_part = rotate(real_part, imag_part, index, local_epoch, samples)
    return jnp.stack([real_part, imag_part], axis=1)


def class_spectrum(gathered, samples):
    devices_tm, _, block_len, columns = gathered.shape
    length = devices_tm * block_len
    index = jnp.arange(devices_tm, dtype=jnp.int32)
    cos_table, sin_table = phase_tables(index, index, devices_tm)
    real_in = gathered[:, 0]
    imag_in = gathered[:, 1]
    cos_b = cos_table[:, :, None, None]
    sin_b = sin_table[:, :, None, None]
    real_part = jnp.sum(cos_b * real_in[None] + sin_b * imag_in[None], axis=1)
    imag_part = jnp.sum(cos_b * imag_in[None] - sin_b * real_in[None], axis=1)
    real_part, imag_part = rotate(
        real_part, imag_part, index, jnp.arange(block_len, dtype=jnp.int32), length
    )
    kept = block_len // 2 + 1
    cos_inner, sin_inner = phase_tables(
        jnp.arange(kept, dtype=jnp.int32), jnp.arange(block_len, dtype=jnp.int32), block_len
    )
    dims = (((1,), (1,)), ((), ()))

    def mat(table, value):
        return lax.dot_general(
            table, value, dims, precision=lax.Precision.HIGH,
            preferred_element_type=jnp.float32,
        )

    new_real = mat(cos_inner, real_part) + mat(sin_inner, imag_part)
    new_imag = mat(cos_inner, imag_part) - mat(sin_inner, real_part)
    new_real = (new_real.reshape(kept * devices_tm, columns) / samples).astype(jnp.bfloat16)
    new_imag = (new_imag.reshape(kept * devices_tm, columns) / samples).astype(jnp.bfloat16)
    return jnp.stack([new_real, new_imag])


def swap_blocks(blocks, axis, ordered):
    count = lax.axis_size(axis)
    if count > 8:
        received = lax.all_to_all(blocks, axis, 0, 0, tiled=True)
        return received if ordered else jnp.sum(received, axis=0)
    me = lax.axis_index(axis)
    arrived = [lax.dynamic_index_in_dim(blocks, me, 0, keepdims=False)]
    for shift in range(1, count):
        outgoing = lax.dynamic_index_in_dim(blocks, (me + shift) % count, 0, keepdims=False)
        pairs = [(src, (src + shift) % count) for src in range(count)]
        arrived.append(lax.ppermute(outgoing, axis, pairs))
    if not ordered:
        total = arrived[0]
        for part in arrived[1:]:
            total = total + part
        return total
    order = (me - jnp.arange(count, dtype=jnp.int32)) % count
    return jnp.take(jnp.stack(arrived), order, axis=0)


def packed_partials(real_in, imag_in, position, samples):
    devices_tm, block_len, columns = real_in.shape
    index = jnp.arange(devices_tm, dtype=jnp.int32)
    cos_table, sin_table = phase_tables(index, index, devices_tm)
    cos_b = cos_table[:, :, None, None]
    sin_b = sin_table[:, :, None, None]
    real_part = jnp.sum(cos_b * real_in[None] + sin_b * imag_in[None], axis=1)
    imag_part = jnp.sum(cos_b * imag_in[None] - sin_b * real_in[None], axis=1)
    local_epoch = position * block_len + jnp.arange(block_len, dtype=jnp.int32)
    real_part, imag_part = rotate(real_part, imag_part, index, local_epoch, samples)
    return jnp.stack([real_part, imag_part], axis=1)


def packed_transform(gathered, sources):
    devices_tm, _, block_len, columns = gathered.shape
    length = devices_tm * block_len
    index = jnp.arange(devices_tm, dtype=jnp.int32)
    cos_table, sin_table = phase_tables(index, sources, devices_tm)
    real_in = gathered[:, 0]
    imag_in = gathered[:, 1]
    cos_b = cos_table[:, :, None, None]
    sin_b = sin_table[:, :, None, None]
    real_part = jnp.sum(cos_b * real_in[None] + sin_b * imag_in[None], axis=1)
    imag_part = jnp.sum(cos_b * imag_in[None] - sin_b * real_in[None], axis=1)
    real_part, imag_part = rotate(
        real_part, imag_part, index, jnp.arange(block_len, dtype=jnp.int32), length
    )
    kept = block_len // 2 + 1
    rows = jnp.arange(kept, dtype=jnp.int32)
    cols = jnp.arange(block_len, dtype=jnp.int32)
    cos_own, sin_own = phase_tables(rows, cols, block_len)
    cos_far, sin_far = phase_tables(block_len - 1 - rows, cols, block_len)
    dims = (((1,), (1,)), ((), ()))

    def mat(table, value):
        return lax.dot_general(
            table, value, dims, precision=lax.Precision.HIGH,
            preferred_element_type=jnp.float32,
        )

    def apply(cos_table, sin_table, real_in, imag_in):
        table = jnp.concatenate([cos_table, sin_table], axis=0)
        from_real = mat(table, real_in)
        from_imag = mat(table, imag_in)
        new_real = from_real[:kept] + from_imag[kept:]
        new_imag = from_imag[:kept] - from_real[kept:]
        return jnp.stack([new_real, new_imag]).reshape(2, kept * devices_tm, columns)

    own = apply(cos_own, sin_own, real_part, imag_part)
    far = apply(cos_far, sin_far, real_part[::-1], imag_part[::-1])
    return own, far


def unpack_spectra(own, far, position, samples):
    devices_tm = lax.axis_size("tm")
    shifted = jnp.concatenate([own[:, :1], far[:, :-1]], axis=1)
    outgoing = jnp.where(position == 0, shifted, far)
    pairs = [(src, (devices_tm - src) % devices_tm) for src in range(devices_tm)]
    mirror = lax.ppermute(outgoing, "tm", pairs)
    own_real = own[0]
    own_imag = own[1]
    first_real = (own_real + mirror[0]) * 0.5
    first_imag = (own_imag - mirror[1]) * 0.5
    second_real = (own_imag + mirror[1]) * 0.5
    second_imag = (mirror[0] - own_real) * 0.5
    new_real = jnp.concatenate([first_real, second_real], axis=1) / samples
    new_imag = jnp.concatenate([first_imag, second_imag], axis=1) / samples
    return jnp.stack([new_real.astype(jnp.bfloat16), new_imag.astype(jnp.bfloat16)])


def exchange_classes(twisted, position):
    devices_tm = lax.axis_size("tm")
    index = jnp.arange(devices_tm, dtype=jnp.int32)
    if devices_tm > 8:
        return lax.all_to_all(twisted, "tm", 0, 0, tiled=True), index
    arrived = [lax.dynamic_index_in_dim(twisted, position, 0, keepdims=False)]
    for shift in range(1, devices_tm):
        outgoing = lax.dynamic_index_in_dim(
            twisted, (position + shift) % devices_tm, 0, keepdims=False
        )
        pairs = [(src, (src + shift) % devices_tm) for src in range(devices_tm)]
        arrived.append(lax.ppermute(outgoing, "tm", pairs))
    return jnp.stack(arrived), (position - index) % devices_tm


def body(orbit_angles, gap_mask, column_index, lat_coeffs, psd_table):
    devices_tm = lax.axis_size("tm")
    panels = lax.axis_size("panel")
    epochs = orbit_angles.shape[1]
    block_len = epochs // devices_tm
    samples = epochs * devices_tm
    columns = lat_coeffs.shape[2]
    coeffs = lat_coeffs[0]
    keep_rows = gap_mask.astype(jnp.float32)
    packed = jnp.concatenate([orbit_angles, keep_rows[None]], axis=0)
    packed = packed.reshape(3, devices_tm, block_len).transpose(1, 0, 2)
    received = swap_blocks(packed, "tm", True)
    flat_orbit = received.transpose(1, 0, 2).reshape(3, devices_tm * block_len)
    spread = synthesize(flat_orbit[0:2], flat_orbit[2], column_index, coeffs).reshape(
        devices_tm, block_len, columns
    )
    position = lax.axis_index("tm")
    half_cols = columns // 2
    twisted = packed_partials(spread[..., :half_cols], spread[..., half_cols:], position, samples)
    gathered, sources = exchange_classes(twisted, position)
    own, far = packed_transform(gathered, sources)
    spectra = unpack_spectra(own, far, position, samples)
    inverse_psd, fold = inverse_weights(
        psd_table[0], position, devices_tm, epochs, samples, spectra.shape[1]
    )
    weighted = (spectra.astype(jnp.float32) * inverse_psd[None, :, None]).astype(jnp.bfloat16)
    weighted = weighted * fold[None, :, None].astype(jnp.bfloat16)
    contract = (((0, 1), (0, 1)), ((), ()))
    products = [
        lax.dot_general(block, weighted, contract, preferred_element_type=jnp.float32)
        for block in panel_spectra(spectra)
    ]
    by_shift = jnp.stack(products)
    panel = lax.axis_index("panel")
    order = (panel - jnp.arange(panels, dtype=jnp.int32)) % panels
    partial_value = jnp.take(by_shift, order, axis=0).reshape(panels * columns, columns)
    return settle_rows(partial_value)


def settle_rows(partial_value):
    devices_tm = lax.axis_size("tm")
    comps = lax.axis_size("comp")
    rows_total, columns = partial_value.shape
    rows = rows_total // devices_tm
    if comps != 2 or columns % 256 != 0:
        pieces = lax.all_to_all(
            partial_value.reshape(devices_tm, rows, columns), "tm", 0, 0, tiled=True
        )
        return comp_sum(jnp.sum(pieces, axis=0))
    half = columns // 2
    comp = lax.axis_index("comp")
    mine = lax.dynamic_slice_in_dim(partial_value, comp * half, half, axis=1)
    theirs = lax.dynamic_slice_in_dim(partial_value, (1 - comp) * half, half, axis=1)
    summed = mine + lax.ppermute(theirs, "comp", [(0, 1), (1, 0)])
    block = swap_blocks(summed.reshape(devices_tm, rows, half), "tm", False)
    other = lax.ppermute(block, "comp", [(0, 1), (1, 0)])
    first = jnp.where(comp == 0, block, other)
    second = jnp.where(comp == 0, other, block)
    return jnp.concatenate([first, second], axis=1)


def solution(mesh):
    return jax.shard_map(
        body,
        mesh=mesh,
        in_specs=(
            P(None, ("groups", "tm")),
            P(("groups", "tm")),
            P(None, "panel"),
            P("comp", None, "panel"),
            P("comp", None),
        ),
        out_specs=P(("groups", "tm"), "panel"),
        check_vma=False,
    )
```

```python
import math

import jax
import jax.numpy as jnp
from jax import lax
from jax.sharding import PartitionSpec as P

SPLIT = 64


def rounding_error(value, factor, product):
    high = lax.reduce_precision(value, exponent_bits=8, mantissa_bits=11)
    low = value - high
    return (product - high * factor) - low * factor


def colatitude_basis(colatitude, terms):
    wavenumbers = jnp.arange(terms, dtype=jnp.float32)
    theta = colatitude[:, None]
    phases = lax.optimization_barrier(theta * wavenumbers[None, :])
    if terms % 16 != 0:
        return jnp.concatenate([jnp.cos(phases), jnp.sin(phases)], axis=1)
    groups = terms // 16
    coarse = jnp.arange(groups, dtype=jnp.float32) * 16.0
    fine = jnp.arange(16, dtype=jnp.float32)
    phase_a = lax.optimization_barrier(theta * coarse[None, :])
    phase_b = lax.optimization_barrier(theta * fine[None, :])
    count = colatitude.shape[0]
    delta = (
        rounding_error(theta, wavenumbers[None, :], phases).reshape(count, groups, 16)
        - rounding_error(theta, coarse[None, :], phase_a)[:, :, None]
        - rounding_error(theta, fine[None, :], phase_b)[:, None, :]
    )
    cos_a = jnp.cos(phase_a)[:, :, None]
    sin_a = jnp.sin(phase_a)[:, :, None]
    cos_b = jnp.cos(phase_b)[:, None, :]
    sin_b = jnp.sin(phase_b)[:, None, :]
    cos_sum = cos_a * cos_b - sin_a * sin_b
    sin_sum = sin_a * cos_b + cos_a * sin_b
    cos_k = (cos_sum - delta * sin_sum).reshape(count, terms)
    sin_k = (sin_sum + delta * cos_sum).reshape(count, terms)
    return jnp.concatenate([cos_k, sin_k], axis=1)


def synthesize(angles, keep_rows, column_index, coeffs):
    terms_lat = coeffs.shape[0] // 2
    colatitude = angles[0]
    longit = angles[1]
    basis_rows = colatitude_basis(colatitude, terms_lat).astype(jnp.bfloat16)
    degree = column_index[0]
    orders = column_index[1]
    levels = jnp.arange(2 * terms_lat, dtype=jnp.int32) % terms_lat
    allowed = levels[:, None] <= degree[None, :]
    masked = jnp.where(allowed, coeffs, jnp.zeros_like(coeffs))
    latitude = jnp.dot(basis_rows, masked, preferred_element_type=jnp.float32)
    lon_phase = longit[:, None] * jnp.abs(orders).astype(jnp.float32)[None, :]
    lon_wave = jnp.where(orders[None, :] >= 0, jnp.cos(lon_phase), jnp.sin(lon_phase))
    norm_scale = 1.0 / jnp.sqrt(degree.astype(jnp.float32) + 1.0)
    return latitude * lon_wave * (keep_rows[:, None] * norm_scale[None, :])


def phase_tables(row_index, col_index, length):
    product = row_index[:, None] * col_index[None, :] % length
    angle_grid = product.astype(jnp.float32) * (2.0 * math.pi / length)
    return (jnp.cos(angle_grid), jnp.sin(angle_grid))


def dft_tables(length):
    indices = jnp.arange(length, dtype=jnp.int32)
    return phase_tables(indices, indices, length)


def rotate(real_part, imag_part, outer_index, inner_index, length):
    index_grid = outer_index[:, None] * inner_index[None, :] % length
    angle_grid = index_grid.astype(jnp.float32) * (2.0 * math.pi / length)
    cosine = jnp.cos(angle_grid)[:, :, None]
    sine_grid = jnp.sin(angle_grid)[:, :, None]
    return (real_part * cosine + imag_part * sine_grid, imag_part * cosine - real_part * sine_grid)


def precise_dot(left_side, right_side):
    return jnp.dot(
        left_side, right_side, precision=lax.Precision.HIGHEST, preferred_element_type=jnp.float32
    )


def transform(cos_table, sin_table, real_part, imag_part):
    new_real = precise_dot(cos_table, real_part) + precise_dot(sin_table, imag_part)
    new_imag = precise_dot(cos_table, imag_part) - precise_dot(sin_table, real_part)
    return (new_real, new_imag)


def four_step(real_in, imag_in, samples):
    length = real_in.shape[0]
    columns = real_in.shape[1]
    outer_count = SPLIT
    inner_count = length // SPLIT
    real_part = real_in.reshape(outer_count, inner_count * columns)
    imag_part = imag_in.reshape(outer_count, inner_count * columns)
    cos_outer, sin_outer = dft_tables(outer_count)
    real_part, imag_part = transform(cos_outer, sin_outer, real_part, imag_part)
    real_part = real_part.reshape(outer_count, inner_count, columns)
    imag_part = imag_part.reshape(outer_count, inner_count, columns)
    real_part, imag_part = rotate(
        real_part,
        imag_part,
        jnp.arange(outer_count, dtype=jnp.int32),
        jnp.arange(inner_count, dtype=jnp.int32),
        length,
    )
    real_part = jnp.transpose(real_part, (1, 0, 2)).reshape(inner_count, outer_count * columns)
    imag_part = jnp.transpose(imag_part, (1, 0, 2)).reshape(inner_count, outer_count * columns)
    cos_inner, sin_inner = dft_tables(inner_count)
    real_part, imag_part = transform(cos_inner, sin_inner, real_part, imag_part)
    return (
        real_part.reshape(length, columns) / samples,
        imag_part.reshape(length, columns) / samples,
    )


def local_transform(received, samples):
    real_part, imag_part = four_step(received[0, 0], received[1, 0], samples)
    return (real_part.astype(jnp.bfloat16), imag_part.astype(jnp.bfloat16))


def inverse_weights(psd_row, position, devices_tm, epochs, samples, count):
    half = samples // 2
    mirrored = jnp.concatenate([psd_row[: half + 1], psd_row[1:half][::-1]])
    picked = lax.dynamic_slice_in_dim(mirrored.reshape(epochs, devices_tm), position, 1, axis=1)
    inverse = 8192.0 / picked[:count, 0].astype(jnp.float32)
    order = jnp.arange(count, dtype=jnp.int32)
    first = jnp.where(position == 0, 1.0, 2.0)
    middle = jnp.where(position == 0, 1.0, 0.0)
    fold = jnp.where(
        order == 0, first, jnp.where(order < epochs // 2, 2.0, jnp.where(order == epochs // 2, middle, 0.0))
    )
    return inverse, fold


def panel_spectra(spectra):
    panels = lax.axis_size("panel")
    blocks = [spectra]
    for shift in range(1, panels):
        pairs = [(src, (src + shift) % panels) for src in range(panels)]
        blocks.append(lax.ppermute(spectra, "panel", pairs))
    return blocks


def comp_sum(value):
    comps = lax.axis_size("comp")
    if comps == 1:
        return value
    if comps != 2:
        return lax.psum(value, "comp")
    other = lax.ppermute(value, "comp", [(0, 1), (1, 0)])
    return value + other


def class_partials(spread, position, samples):
    devices_tm, block_len, columns = spread.shape
    index = jnp.arange(devices_tm, dtype=jnp.int32)
    cos_table, sin_table = phase_tables(index, index, devices_tm)
    real_part = jnp.sum(cos_table[:, :, None, None] * spread[None], axis=1)
    imag_part = -jnp.sum(sin_table[:, :, None, None] * spread[None], axis=1)
    local_epoch = position * block_len + jnp.arange(block_len, dtype=jnp.int32)
    real_part, imag_part = rotate(real_part, imag_part, index, local_epoch, samples)
    return jnp.stack([real_part, imag_part], axis=1)


def class_spectrum(gathered, samples):
    devices_tm, _, block_len, columns = gathered.shape
    length = devices_tm * block_len
    index = jnp.arange(devices_tm, dtype=jnp.int32)
    cos_table, sin_table = phase_tables(index, index, devices_tm)
    real_in = gathered[:, 0]
    imag_in = gathered[:, 1]
    cos_b = cos_table[:, :, None, None]
    sin_b = sin_table[:, :, None, None]
    real_part = jnp.sum(cos_b * real_in[None] + sin_b * imag_in[None], axis=1)
    imag_part = jnp.sum(cos_b * imag_in[None] - sin_b * real_in[None], axis=1)
    real_part, imag_part = rotate(
        real_part, imag_part, index, jnp.arange(block_len, dtype=jnp.int32), length
    )
    kept = block_len // 2 + 1
    cos_inner, sin_inner = phase_tables(
        jnp.arange(kept, dtype=jnp.int32), jnp.arange(block_len, dtype=jnp.int32), block_len
    )
    dims = (((1,), (1,)), ((), ()))

    def mat(table, value):
        return lax.dot_general(
            table, value, dims, precision=lax.Precision.HIGH,
            preferred_element_type=jnp.float32,
        )

    new_real = mat(cos_inner, real_part) + mat(sin_inner, imag_part)
    new_imag = mat(cos_inner, imag_part) - mat(sin_inner, real_part)
    new_real = (new_real.reshape(kept * devices_tm, columns) / samples).astype(jnp.bfloat16)
    new_imag = (new_imag.reshape(kept * devices_tm, columns) / samples).astype(jnp.bfloat16)
    return jnp.stack([new_real, new_imag])


def swap_blocks(blocks, axis, ordered):
    count = lax.axis_size(axis)
    if count > 8:
        received = lax.all_to_all(blocks, axis, 0, 0, tiled=True)
        return received if ordered else jnp.sum(received, axis=0)
    me = lax.axis_index(axis)
    arrived = [lax.dynamic_index_in_dim(blocks, me, 0, keepdims=False)]
    for shift in range(1, count):
        outgoing = lax.dynamic_index_in_dim(blocks, (me + shift) % count, 0, keepdims=False)
        pairs = [(src, (src + shift) % count) for src in range(count)]
        arrived.append(lax.ppermute(outgoing, axis, pairs))
    if not ordered:
        total = arrived[0]
        for part in arrived[1:]:
            total = total + part
        return total
    order = (me - jnp.arange(count, dtype=jnp.int32)) % count
    return jnp.take(jnp.stack(arrived), order, axis=0)


def class_order(count):
    order = [0]
    for low in range(1, (count + 1) // 2):
        order += [low, count - low]
    if count % 2 == 0 and count > 1:
        order.append(count // 2)
    return order


def packed_partials(real_in, imag_in, position, samples):
    devices_tm, block_len, columns = real_in.shape
    index = jnp.arange(devices_tm, dtype=jnp.int32)
    classes = jnp.asarray(class_order(devices_tm), dtype=jnp.int32)
    cos_table, sin_table = phase_tables(classes, index, devices_tm)
    cos_b = cos_table[:, :, None, None]
    sin_b = sin_table[:, :, None, None]
    real_part = jnp.sum(cos_b * real_in[None] + sin_b * imag_in[None], axis=1)
    imag_part = jnp.sum(cos_b * imag_in[None] - sin_b * real_in[None], axis=1)
    local_epoch = position * block_len + jnp.arange(block_len, dtype=jnp.int32)
    real_part, imag_part = rotate(real_part, imag_part, classes, local_epoch, samples)
    return jnp.stack([real_part, imag_part], axis=1)


def packed_transform(gathered):
    devices_tm, _, block_len, columns = gathered.shape
    length = devices_tm * block_len
    index = jnp.arange(devices_tm, dtype=jnp.int32)
    cos_table, sin_table = phase_tables(index, index, devices_tm)
    real_in = gathered[:, 0]
    imag_in = gathered[:, 1]
    cos_b = cos_table[:, :, None, None]
    sin_b = sin_table[:, :, None, None]
    real_part = jnp.sum(cos_b * real_in[None] + sin_b * imag_in[None], axis=1)
    imag_part = jnp.sum(cos_b * imag_in[None] - sin_b * real_in[None], axis=1)
    real_part, imag_part = rotate(
        real_part, imag_part, index, jnp.arange(block_len, dtype=jnp.int32), length
    )
    kept = block_len // 2 + 1
    rows = jnp.arange(kept, dtype=jnp.int32)
    cols = jnp.arange(block_len, dtype=jnp.int32)
    cos_own, sin_own = phase_tables(rows, cols, block_len)
    cos_far, sin_far = phase_tables(block_len - 1 - rows, cols, block_len)
    dims = (((1,), (1,)), ((), ()))

    def mat(table, value):
        return lax.dot_general(
            table, value, dims, precision=lax.Precision.HIGH,
            preferred_element_type=jnp.float32,
        )

    def apply(cos_table, sin_table, real_in, imag_in):
        table = jnp.concatenate([cos_table, sin_table], axis=0)
        from_real = mat(table, real_in)
        from_imag = mat(table, imag_in)
        new_real = from_real[:kept] + from_imag[kept:]
        new_imag = from_imag[:kept] - from_real[kept:]
        return jnp.stack([new_real, new_imag]).reshape(2, kept * devices_tm, columns)

    own = apply(cos_own, sin_own, real_part, imag_part)
    far = apply(cos_far, sin_far, real_part[::-1], imag_part[::-1])
    return own, far


def unpack_spectra(own, far, klass, samples):
    devices_tm = lax.axis_size("tm")
    shifted = jnp.concatenate([own[:, :1], far[:, :-1]], axis=1)
    outgoing = jnp.where(klass == 0, shifted, far)
    order = class_order(devices_tm)
    holder = {value: place for place, value in enumerate(order)}
    pairs = [(src, holder[(devices_tm - order[src]) % devices_tm]) for src in range(devices_tm)]
    mirror = lax.ppermute(outgoing, "tm", pairs)
    own_real = own[0]
    own_imag = own[1]
    first_real = (own_real + mirror[0]) * 0.5
    first_imag = (own_imag - mirror[1]) * 0.5
    second_real = (own_imag + mirror[1]) * 0.5
    second_imag = (mirror[0] - own_real) * 0.5
    new_real = jnp.concatenate([first_real, second_real], axis=1) / samples
    new_imag = jnp.concatenate([first_imag, second_imag], axis=1) / samples
    return jnp.stack([new_real.astype(jnp.bfloat16), new_imag.astype(jnp.bfloat16)])


def body(orbit_angles, gap_mask, column_index, lat_coeffs, psd_table):
    devices_tm = lax.axis_size("tm")
    panels = lax.axis_size("panel")
    epochs = orbit_angles.shape[1]
    block_len = epochs // devices_tm
    samples = epochs * devices_tm
    columns = lat_coeffs.shape[2]
    coeffs = lat_coeffs[0]
    keep_rows = gap_mask.astype(jnp.float32)
    packed = jnp.concatenate([orbit_angles, keep_rows[None]], axis=0)
    packed = packed.reshape(3, devices_tm, block_len).transpose(1, 0, 2)
    received = swap_blocks(packed, "tm", True)
    flat_orbit = received.transpose(1, 0, 2).reshape(3, devices_tm * block_len)
    spread = synthesize(flat_orbit[0:2], flat_orbit[2], column_index, coeffs).reshape(
        devices_tm, block_len, columns
    )
    position = lax.axis_index("tm")
    half_cols = columns // 2
    twisted = packed_partials(spread[..., :half_cols], spread[..., half_cols:], position, samples)
    gathered = lax.all_to_all(twisted, "tm", 0, 0, tiled=True)
    own, far = packed_transform(gathered)
    klass = jnp.asarray(class_order(devices_tm), dtype=jnp.int32)[position]
    spectra = unpack_spectra(own, far, klass, samples)
    inverse_psd, fold = inverse_weights(
        psd_table[0], klass, devices_tm, epochs, samples, spectra.shape[1]
    )
    weighted = (spectra.astype(jnp.float32) * inverse_psd[None, :, None]).astype(jnp.bfloat16)
    weighted = weighted * fold[None, :, None].astype(jnp.bfloat16)
    contract = (((0, 1), (0, 1)), ((), ()))
    products = [
        lax.dot_general(block, weighted, contract, preferred_element_type=jnp.float32)
        for block in panel_spectra(spectra)
    ]
    by_shift = jnp.stack(products)
    panel = lax.axis_index("panel")
    order = (panel - jnp.arange(panels, dtype=jnp.int32)) % panels
    partial_value = jnp.take(by_shift, order, axis=0).reshape(panels * columns, columns)
    return settle_rows(partial_value)


def settle_rows(partial_value):
    devices_tm = lax.axis_size("tm")
    comps = lax.axis_size("comp")
    rows_total, columns = partial_value.shape
    rows = rows_total // devices_tm
    if comps != 2 or columns % 256 != 0:
        pieces = lax.all_to_all(
            partial_value.reshape(devices_tm, rows, columns), "tm", 0, 0, tiled=True
        )
        return comp_sum(jnp.sum(pieces, axis=0))
    half = columns // 2
    comp = lax.axis_index("comp")
    mine = lax.dynamic_slice_in_dim(partial_value, comp * half, half, axis=1)
    theirs = lax.dynamic_slice_in_dim(partial_value, (1 - comp) * half, half, axis=1)
    summed = mine + lax.ppermute(theirs, "comp", [(0, 1), (1, 0)])
    block = swap_blocks(summed.reshape(devices_tm, rows, half), "tm", False)
    other = lax.ppermute(block, "comp", [(0, 1), (1, 0)])
    first = jnp.where(comp == 0, block, other)
    second = jnp.where(comp == 0, other, block)
    return jnp.concatenate([first, second], axis=1)


def solution(mesh):
    return jax.shard_map(
        body,
        mesh=mesh,
        in_specs=(
            P(None, ("groups", "tm")),
            P(("groups", "tm")),
            P(None, "panel"),
            P("comp", None, "panel"),
            P("comp", None),
        ),
        out_specs=P(("groups", "tm"), "panel"),
        check_vma=False,
    )
```

```python
import math

import jax
import jax.numpy as jnp
from jax import lax
from jax.sharding import PartitionSpec as P

SPLIT = 64


def rounding_error(value, factor, product):
    high = lax.reduce_precision(value, exponent_bits=8, mantissa_bits=11)
    low = value - high
    return (product - high * factor) - low * factor


def colatitude_basis(colatitude, terms):
    wavenumbers = jnp.arange(terms, dtype=jnp.float32)
    theta = colatitude[:, None]
    phases = lax.optimization_barrier(theta * wavenumbers[None, :])
    if terms % 16 != 0:
        return jnp.concatenate([jnp.cos(phases), jnp.sin(phases)], axis=1)
    groups = terms // 16
    coarse = jnp.arange(groups, dtype=jnp.float32) * 16.0
    fine = jnp.arange(16, dtype=jnp.float32)
    phase_a = lax.optimization_barrier(theta * coarse[None, :])
    phase_b = lax.optimization_barrier(theta * fine[None, :])
    count = colatitude.shape[0]
    delta = (
        rounding_error(theta, wavenumbers[None, :], phases).reshape(count, groups, 16)
        - rounding_error(theta, coarse[None, :], phase_a)[:, :, None]
        - rounding_error(theta, fine[None, :], phase_b)[:, None, :]
    )
    cos_a = jnp.cos(phase_a)[:, :, None]
    sin_a = jnp.sin(phase_a)[:, :, None]
    cos_b = jnp.cos(phase_b)[:, None, :]
    sin_b = jnp.sin(phase_b)[:, None, :]
    cos_sum = cos_a * cos_b - sin_a * sin_b
    sin_sum = sin_a * cos_b + cos_a * sin_b
    cos_k = (cos_sum - delta * sin_sum).reshape(count, terms)
    sin_k = (sin_sum + delta * cos_sum).reshape(count, terms)
    return jnp.concatenate([cos_k, sin_k], axis=1)


def synthesize(angles, keep_rows, column_index, coeffs):
    terms_lat = coeffs.shape[0] // 2
    colatitude = angles[0]
    longit = angles[1]
    basis_rows = colatitude_basis(colatitude, terms_lat).astype(jnp.bfloat16)
    degree = column_index[0]
    orders = column_index[1]
    levels = jnp.arange(2 * terms_lat, dtype=jnp.int32) % terms_lat
    allowed = levels[:, None] <= degree[None, :]
    masked = jnp.where(allowed, coeffs, jnp.zeros_like(coeffs))
    latitude = jnp.dot(basis_rows, masked, preferred_element_type=jnp.float32)
    lon_phase = longit[:, None] * jnp.abs(orders).astype(jnp.float32)[None, :]
    lon_wave = jnp.where(orders[None, :] >= 0, jnp.cos(lon_phase), jnp.sin(lon_phase))
    norm_scale = 1.0 / jnp.sqrt(degree.astype(jnp.float32) + 1.0)
    return latitude * lon_wave * (keep_rows[:, None] * norm_scale[None, :])


def phase_tables(row_index, col_index, length):
    product = row_index[:, None] * col_index[None, :] % length
    angle_grid = product.astype(jnp.float32) * (2.0 * math.pi / length)
    return (jnp.cos(angle_grid), jnp.sin(angle_grid))


def dft_tables(length):
    indices = jnp.arange(length, dtype=jnp.int32)
    return phase_tables(indices, indices, length)


def rotate(real_part, imag_part, outer_index, inner_index, length):
    index_grid = outer_index[:, None] * inner_index[None, :] % length
    angle_grid = index_grid.astype(jnp.float32) * (2.0 * math.pi / length)
    cosine = jnp.cos(angle_grid)[:, :, None]
    sine_grid = jnp.sin(angle_grid)[:, :, None]
    return (real_part * cosine + imag_part * sine_grid, imag_part * cosine - real_part * sine_grid)


def precise_dot(left_side, right_side):
    return jnp.dot(
        left_side, right_side, precision=lax.Precision.HIGHEST, preferred_element_type=jnp.float32
    )


def transform(cos_table, sin_table, real_part, imag_part):
    new_real = precise_dot(cos_table, real_part) + precise_dot(sin_table, imag_part)
    new_imag = precise_dot(cos_table, imag_part) - precise_dot(sin_table, real_part)
    return (new_real, new_imag)


def four_step(real_in, imag_in, samples):
    length = real_in.shape[0]
    columns = real_in.shape[1]
    outer_count = SPLIT
    inner_count = length // SPLIT
    real_part = real_in.reshape(outer_count, inner_count * columns)
    imag_part = imag_in.reshape(outer_count, inner_count * columns)
    cos_outer, sin_outer = dft_tables(outer_count)
    real_part, imag_part = transform(cos_outer, sin_outer, real_part, imag_part)
    real_part = real_part.reshape(outer_count, inner_count, columns)
    imag_part = imag_part.reshape(outer_count, inner_count, columns)
    real_part, imag_part = rotate(
        real_part,
        imag_part,
        jnp.arange(outer_count, dtype=jnp.int32),
        jnp.arange(inner_count, dtype=jnp.int32),
        length,
    )
    real_part = jnp.transpose(real_part, (1, 0, 2)).reshape(inner_count, outer_count * columns)
    imag_part = jnp.transpose(imag_part, (1, 0, 2)).reshape(inner_count, outer_count * columns)
    cos_inner, sin_inner = dft_tables(inner_count)
    real_part, imag_part = transform(cos_inner, sin_inner, real_part, imag_part)
    return (
        real_part.reshape(length, columns) / samples,
        imag_part.reshape(length, columns) / samples,
    )


def local_transform(received, samples):
    real_part, imag_part = four_step(received[0, 0], received[1, 0], samples)
    return (real_part.astype(jnp.bfloat16), imag_part.astype(jnp.bfloat16))


def inverse_weights(psd_row, position, devices_tm, epochs, samples, count):
    half = samples // 2
    mirrored = jnp.concatenate([psd_row[: half + 1], psd_row[1:half][::-1]])
    picked = lax.dynamic_slice_in_dim(mirrored.reshape(epochs, devices_tm), position, 1, axis=1)
    inverse = 8192.0 / picked[:count, 0].astype(jnp.float32)
    order = jnp.arange(count, dtype=jnp.int32)
    first = jnp.where(position == 0, 1.0, 2.0)
    middle = jnp.where(position == 0, 1.0, 0.0)
    fold = jnp.where(
        order == 0, first, jnp.where(order < epochs // 2, 2.0, jnp.where(order == epochs // 2, middle, 0.0))
    )
    return inverse, fold


def panel_spectra(spectra):
    panels = lax.axis_size("panel")
    blocks = [spectra]
    for shift in range(1, panels):
        pairs = [(src, (src + shift) % panels) for src in range(panels)]
        blocks.append(lax.ppermute(spectra, "panel", pairs))
    return blocks


def comp_sum(value):
    comps = lax.axis_size("comp")
    if comps == 1:
        return value
    if comps != 2:
        return lax.psum(value, "comp")
    other = lax.ppermute(value, "comp", [(0, 1), (1, 0)])
    return value + other


def class_partials(spread, position, samples):
    devices_tm, block_len, columns = spread.shape
    index = jnp.arange(devices_tm, dtype=jnp.int32)
    cos_table, sin_table = phase_tables(index, index, devices_tm)
    real_part = jnp.sum(cos_table[:, :, None, None] * spread[None], axis=1)
    imag_part = -jnp.sum(sin_table[:, :, None, None] * spread[None], axis=1)
    local_epoch = position * block_len + jnp.arange(block_len, dtype=jnp.int32)
    real_part, imag_part = rotate(real_part, imag_part, index, local_epoch, samples)
    return jnp.stack([real_part, imag_part], axis=1)


def class_spectrum(gathered, samples):
    devices_tm, _, block_len, columns = gathered.shape
    length = devices_tm * block_len
    index = jnp.arange(devices_tm, dtype=jnp.int32)
    cos_table, sin_table = phase_tables(index, index, devices_tm)
    real_in = gathered[:, 0]
    imag_in = gathered[:, 1]
    cos_b = cos_table[:, :, None, None]
    sin_b = sin_table[:, :, None, None]
    real_part = jnp.sum(cos_b * real_in[None] + sin_b * imag_in[None], axis=1)
    imag_part = jnp.sum(cos_b * imag_in[None] - sin_b * real_in[None], axis=1)
    real_part, imag_part = rotate(
        real_part, imag_part, index, jnp.arange(block_len, dtype=jnp.int32), length
    )
    kept = block_len // 2 + 1
    cos_inner, sin_inner = phase_tables(
        jnp.arange(kept, dtype=jnp.int32), jnp.arange(block_len, dtype=jnp.int32), block_len
    )
    dims = (((1,), (1,)), ((), ()))

    def mat(table, value):
        return lax.dot_general(
            table, value, dims, precision=lax.Precision.HIGH,
            preferred_element_type=jnp.float32,
        )

    new_real = mat(cos_inner, real_part) + mat(sin_inner, imag_part)
    new_imag = mat(cos_inner, imag_part) - mat(sin_inner, real_part)
    new_real = (new_real.reshape(kept * devices_tm, columns) / samples).astype(jnp.bfloat16)
    new_imag = (new_imag.reshape(kept * devices_tm, columns) / samples).astype(jnp.bfloat16)
    return jnp.stack([new_real, new_imag])


def swap_blocks(blocks, axis, ordered):
    count = lax.axis_size(axis)
    if count > 8:
        received = lax.all_to_all(blocks, axis, 0, 0, tiled=True)
        if ordered:
            return received, jnp.arange(count, dtype=jnp.int32)
        return jnp.sum(received, axis=0)
    me = lax.axis_index(axis)
    arrived = [lax.dynamic_index_in_dim(blocks, me, 0, keepdims=False)]
    for shift in range(1, count):
        outgoing = lax.dynamic_index_in_dim(blocks, (me + shift) % count, 0, keepdims=False)
        pairs = [(src, (src + shift) % count) for src in range(count)]
        arrived.append(lax.ppermute(outgoing, axis, pairs))
    if not ordered:
        total = arrived[0]
        for part in arrived[1:]:
            total = total + part
        return total
    return jnp.stack(arrived), (me - jnp.arange(count, dtype=jnp.int32)) % count


def packed_partials(real_in, imag_in, position, samples, sources):
    devices_tm, block_len, columns = real_in.shape
    index = jnp.arange(devices_tm, dtype=jnp.int32)
    cos_table, sin_table = phase_tables(index, sources, devices_tm)
    cos_b = cos_table[:, :, None, None]
    sin_b = sin_table[:, :, None, None]
    real_part = jnp.sum(cos_b * real_in[None] + sin_b * imag_in[None], axis=1)
    imag_part = jnp.sum(cos_b * imag_in[None] - sin_b * real_in[None], axis=1)
    local_epoch = position * block_len + jnp.arange(block_len, dtype=jnp.int32)
    real_part, imag_part = rotate(real_part, imag_part, index, local_epoch, samples)
    return jnp.stack([real_part, imag_part], axis=1)


def packed_transform(gathered):
    devices_tm, _, block_len, columns = gathered.shape
    length = devices_tm * block_len
    index = jnp.arange(devices_tm, dtype=jnp.int32)
    cos_table, sin_table = phase_tables(index, index, devices_tm)
    real_in = gathered[:, 0]
    imag_in = gathered[:, 1]
    cos_b = cos_table[:, :, None, None]
    sin_b = sin_table[:, :, None, None]
    real_part = jnp.sum(cos_b * real_in[None] + sin_b * imag_in[None], axis=1)
    imag_part = jnp.sum(cos_b * imag_in[None] - sin_b * real_in[None], axis=1)
    real_part, imag_part = rotate(
        real_part, imag_part, index, jnp.arange(block_len, dtype=jnp.int32), length
    )
    kept = block_len // 2 + 1
    rows = jnp.arange(kept, dtype=jnp.int32)
    cols = jnp.arange(block_len, dtype=jnp.int32)
    cos_own, sin_own = phase_tables(rows, cols, block_len)
    cos_far, sin_far = phase_tables(block_len - 1 - rows, cols, block_len)
    dims = (((1,), (1,)), ((), ()))

    def mat(table, value):
        return lax.dot_general(
            table, value, dims, precision=lax.Precision.HIGH,
            preferred_element_type=jnp.float32,
        )

    def apply(cos_table, sin_table, real_in, imag_in):
        table = jnp.concatenate([cos_table, sin_table], axis=0)
        from_real = mat(table, real_in)
        from_imag = mat(table, imag_in)
        new_real = from_real[:kept] + from_imag[kept:]
        new_imag = from_imag[:kept] - from_real[kept:]
        return jnp.stack([new_real, new_imag]).reshape(2, kept * devices_tm, columns)

    own = apply(cos_own, sin_own, real_part, imag_part)
    far = apply(cos_far, sin_far, real_part[::-1], imag_part[::-1])
    return own, far


def unpack_spectra(own, far, position, samples):
    devices_tm = lax.axis_size("tm")
    shifted = jnp.concatenate([own[:, :1], far[:, :-1]], axis=1)
    outgoing = jnp.where(position == 0, shifted, far)
    pairs = [(src, (devices_tm - src) % devices_tm) for src in range(devices_tm)]
    mirror = lax.ppermute(outgoing, "tm", pairs)
    own_real = own[0]
    own_imag = own[1]
    first_real = (own_real + mirror[0]) * 0.5
    first_imag = (own_imag - mirror[1]) * 0.5
    second_real = (own_imag + mirror[1]) * 0.5
    second_imag = (mirror[0] - own_real) * 0.5
    new_real = jnp.concatenate([first_real, second_real], axis=1) / samples
    new_imag = jnp.concatenate([first_imag, second_imag], axis=1) / samples
    return jnp.stack([new_real.astype(jnp.bfloat16), new_imag.astype(jnp.bfloat16)])


def body(orbit_angles, gap_mask, column_index, lat_coeffs, psd_table):
    devices_tm = lax.axis_size("tm")
    panels = lax.axis_size("panel")
    epochs = orbit_angles.shape[1]
    block_len = epochs // devices_tm
    samples = epochs * devices_tm
    columns = lat_coeffs.shape[2]
    coeffs = lat_coeffs[0]
    keep_rows = gap_mask.astype(jnp.float32)
    packed = jnp.concatenate([orbit_angles, keep_rows[None]], axis=0)
    packed = packed.reshape(3, devices_tm, block_len).transpose(1, 0, 2)
    received, sources = swap_blocks(packed, "tm", True)
    flat_orbit = received.transpose(1, 0, 2).reshape(3, devices_tm * block_len)
    spread = synthesize(flat_orbit[0:2], flat_orbit[2], column_index, coeffs).reshape(
        devices_tm, block_len, columns
    )
    position = lax.axis_index("tm")
    half_cols = columns // 2
    twisted = packed_partials(
        spread[..., :half_cols], spread[..., half_cols:], position, samples, sources
    )
    gathered = lax.all_to_all(twisted, "tm", 0, 0, tiled=True)
    own, far = packed_transform(gathered)
    spectra = unpack_spectra(own, far, position, samples)
    inverse_psd, fold = inverse_weights(
        psd_table[0], position, devices_tm, epochs, samples, spectra.shape[1]
    )
    weighted = (spectra.astype(jnp.float32) * inverse_psd[None, :, None]).astype(jnp.bfloat16)
    weighted = weighted * fold[None, :, None].astype(jnp.bfloat16)
    contract = (((0, 1), (0, 1)), ((), ()))
    products = [
        lax.dot_general(block, weighted, contract, preferred_element_type=jnp.float32)
        for block in panel_spectra(spectra)
    ]
    by_shift = jnp.stack(products)
    panel = lax.axis_index("panel")
    order = (panel - jnp.arange(panels, dtype=jnp.int32)) % panels
    partial_value = jnp.take(by_shift, order, axis=0).reshape(panels * columns, columns)
    return settle_rows(partial_value)


def settle_rows(partial_value):
    devices_tm = lax.axis_size("tm")
    comps = lax.axis_size("comp")
    rows_total, columns = partial_value.shape
    rows = rows_total // devices_tm
    if comps != 2 or columns % 256 != 0 or devices_tm <= 8:
        return comp_sum(swap_blocks(partial_value.reshape(devices_tm, rows, columns), "tm", False))
    half = columns // 2
    comp = lax.axis_index("comp")
    mine = lax.dynamic_slice_in_dim(partial_value, comp * half, half, axis=1)
    theirs = lax.dynamic_slice_in_dim(partial_value, (1 - comp) * half, half, axis=1)
    summed = mine + lax.ppermute(theirs, "comp", [(0, 1), (1, 0)])
    block = swap_blocks(summed.reshape(devices_tm, rows, half), "tm", False)
    other = lax.ppermute(block, "comp", [(0, 1), (1, 0)])
    first = jnp.where(comp == 0, block, other)
    second = jnp.where(comp == 0, other, block)
    return jnp.concatenate([first, second], axis=1)


def solution(mesh):
    return jax.shard_map(
        body,
        mesh=mesh,
        in_specs=(
            P(None, ("groups", "tm")),
            P(("groups", "tm")),
            P(None, "panel"),
            P("comp", None, "panel"),
            P("comp", None),
        ),
        out_specs=P(("groups", "tm"), "panel"),
        check_vma=False,
    )
```

```python
import math

import jax
import jax.numpy as jnp
from jax import lax
from jax.sharding import PartitionSpec as P

SPLIT = 64


def rounding_error(value, factor, product):
    high = lax.reduce_precision(value, exponent_bits=8, mantissa_bits=11)
    low = value - high
    return (product - high * factor) - low * factor


def colatitude_basis(colatitude, terms):
    wavenumbers = jnp.arange(terms, dtype=jnp.float32)
    theta = colatitude[:, None]
    phases = lax.optimization_barrier(theta * wavenumbers[None, :])
    if terms % 16 != 0:
        return jnp.concatenate([jnp.cos(phases), jnp.sin(phases)], axis=1)
    groups = terms // 16
    coarse = jnp.arange(groups, dtype=jnp.float32) * 16.0
    fine = jnp.arange(16, dtype=jnp.float32)
    phase_a = lax.optimization_barrier(theta * coarse[None, :])
    phase_b = lax.optimization_barrier(theta * fine[None, :])
    count = colatitude.shape[0]
    delta = (
        rounding_error(theta, wavenumbers[None, :], phases).reshape(count, groups, 16)
        - rounding_error(theta, coarse[None, :], phase_a)[:, :, None]
        - rounding_error(theta, fine[None, :], phase_b)[:, None, :]
    )
    cos_a = jnp.cos(phase_a)[:, :, None]
    sin_a = jnp.sin(phase_a)[:, :, None]
    cos_b = jnp.cos(phase_b)[:, None, :]
    sin_b = jnp.sin(phase_b)[:, None, :]
    cos_sum = cos_a * cos_b - sin_a * sin_b
    sin_sum = sin_a * cos_b + cos_a * sin_b
    cos_k = (cos_sum - delta * sin_sum).reshape(count, terms)
    sin_k = (sin_sum + delta * cos_sum).reshape(count, terms)
    return jnp.concatenate([cos_k, sin_k], axis=1)


def column_factors(column_index, coeffs):
    terms_lat = coeffs.shape[0] // 2
    degree = column_index[0]
    orders = column_index[1]
    levels = jnp.arange(2 * terms_lat, dtype=jnp.int32) % terms_lat
    allowed = levels[:, None] <= degree[None, :]
    masked = jnp.where(allowed, coeffs, jnp.zeros_like(coeffs))
    norm_scale = 1.0 / jnp.sqrt(degree.astype(jnp.float32) + 1.0)
    return masked, norm_scale


def synthesize(angles, keep_rows, column_index, masked, norm_scale):
    terms_lat = masked.shape[0] // 2
    colatitude = angles[0]
    longit = angles[1]
    basis_rows = colatitude_basis(colatitude, terms_lat).astype(jnp.bfloat16)
    orders = column_index[1]
    latitude = jnp.dot(basis_rows, masked, preferred_element_type=jnp.float32)
    lon_phase = longit[:, None] * jnp.abs(orders).astype(jnp.float32)[None, :]
    lon_wave = jnp.where(orders[None, :] >= 0, jnp.cos(lon_phase), jnp.sin(lon_phase))
    return latitude * lon_wave * (keep_rows[:, None] * norm_scale[None, :])


def phase_tables(row_index, col_index, length):
    product = row_index[:, None] * col_index[None, :] % length
    angle_grid = product.astype(jnp.float32) * (2.0 * math.pi / length)
    return (jnp.cos(angle_grid), jnp.sin(angle_grid))


def dft_tables(length):
    indices = jnp.arange(length, dtype=jnp.int32)
    return phase_tables(indices, indices, length)


def rotate(real_part, imag_part, outer_index, inner_index, length):
    index_grid = outer_index[:, None] * inner_index[None, :] % length
    angle_grid = index_grid.astype(jnp.float32) * (2.0 * math.pi / length)
    cosine = jnp.cos(angle_grid)[:, :, None]
    sine_grid = jnp.sin(angle_grid)[:, :, None]
    return (real_part * cosine + imag_part * sine_grid, imag_part * cosine - real_part * sine_grid)


def precise_dot(left_side, right_side):
    return jnp.dot(
        left_side, right_side, precision=lax.Precision.HIGHEST, preferred_element_type=jnp.float32
    )


def transform(cos_table, sin_table, real_part, imag_part):
    new_real = precise_dot(cos_table, real_part) + precise_dot(sin_table, imag_part)
    new_imag = precise_dot(cos_table, imag_part) - precise_dot(sin_table, real_part)
    return (new_real, new_imag)


def four_step(real_in, imag_in, samples):
    length = real_in.shape[0]
    columns = real_in.shape[1]
    outer_count = SPLIT
    inner_count = length // SPLIT
    real_part = real_in.reshape(outer_count, inner_count * columns)
    imag_part = imag_in.reshape(outer_count, inner_count * columns)
    cos_outer, sin_outer = dft_tables(outer_count)
    real_part, imag_part = transform(cos_outer, sin_outer, real_part, imag_part)
    real_part = real_part.reshape(outer_count, inner_count, columns)
    imag_part = imag_part.reshape(outer_count, inner_count, columns)
    real_part, imag_part = rotate(
        real_part,
        imag_part,
        jnp.arange(outer_count, dtype=jnp.int32),
        jnp.arange(inner_count, dtype=jnp.int32),
        length,
    )
    real_part = jnp.transpose(real_part, (1, 0, 2)).reshape(inner_count, outer_count * columns)
    imag_part = jnp.transpose(imag_part, (1, 0, 2)).reshape(inner_count, outer_count * columns)
    cos_inner, sin_inner = dft_tables(inner_count)
    real_part, imag_part = transform(cos_inner, sin_inner, real_part, imag_part)
    return (
        real_part.reshape(length, columns) / samples,
        imag_part.reshape(length, columns) / samples,
    )


def local_transform(received, samples):
    real_part, imag_part = four_step(received[0, 0], received[1, 0], samples)
    return (real_part.astype(jnp.bfloat16), imag_part.astype(jnp.bfloat16))


def inverse_weights(psd_row, position, devices_tm, epochs, samples, count):
    half = samples // 2
    mirrored = jnp.concatenate([psd_row[: half + 1], psd_row[1:half][::-1]])
    picked = lax.dynamic_slice_in_dim(mirrored.reshape(epochs, devices_tm), position, 1, axis=1)
    inverse = 8192.0 / picked[:count, 0].astype(jnp.float32)
    order = jnp.arange(count, dtype=jnp.int32)
    first = jnp.where(position == 0, 1.0, 2.0)
    middle = jnp.where(position == 0, 1.0, 0.0)
    fold = jnp.where(
        order == 0, first, jnp.where(order < epochs // 2, 2.0, jnp.where(order == epochs // 2, middle, 0.0))
    )
    return inverse, fold


def panel_spectra(spectra):
    panels = lax.axis_size("panel")
    blocks = [spectra]
    for shift in range(1, panels):
        pairs = [(src, (src + shift) % panels) for src in range(panels)]
        blocks.append(lax.ppermute(spectra, "panel", pairs))
    return blocks


def comp_sum(value):
    comps = lax.axis_size("comp")
    if comps == 1:
        return value
    if comps != 2:
        return lax.psum(value, "comp")
    other = lax.ppermute(value, "comp", [(0, 1), (1, 0)])
    return value + other


def class_partials(spread, position, samples):
    devices_tm, block_len, columns = spread.shape
    index = jnp.arange(devices_tm, dtype=jnp.int32)
    cos_table, sin_table = phase_tables(index, index, devices_tm)
    real_part = jnp.sum(cos_table[:, :, None, None] * spread[None], axis=1)
    imag_part = -jnp.sum(sin_table[:, :, None, None] * spread[None], axis=1)
    local_epoch = position * block_len + jnp.arange(block_len, dtype=jnp.int32)
    real_part, imag_part = rotate(real_part, imag_part, index, local_epoch, samples)
    return jnp.stack([real_part, imag_part], axis=1)


def class_spectrum(gathered, samples):
    devices_tm, _, block_len, columns = gathered.shape
    length = devices_tm * block_len
    index = jnp.arange(devices_tm, dtype=jnp.int32)
    cos_table, sin_table = phase_tables(index, index, devices_tm)
    real_in = gathered[:, 0]
    imag_in = gathered[:, 1]
    cos_b = cos_table[:, :, None, None]
    sin_b = sin_table[:, :, None, None]
    real_part = jnp.sum(cos_b * real_in[None] + sin_b * imag_in[None], axis=1)
    imag_part = jnp.sum(cos_b * imag_in[None] - sin_b * real_in[None], axis=1)
    real_part, imag_part = rotate(
        real_part, imag_part, index, jnp.arange(block_len, dtype=jnp.int32), length
    )
    kept = block_len // 2 + 1
    cos_inner, sin_inner = phase_tables(
        jnp.arange(kept, dtype=jnp.int32), jnp.arange(block_len, dtype=jnp.int32), block_len
    )
    dims = (((1,), (1,)), ((), ()))

    def mat(table, value):
        return lax.dot_general(
            table, value, dims, precision=lax.Precision.HIGH,
            preferred_element_type=jnp.float32,
        )

    new_real = mat(cos_inner, real_part) + mat(sin_inner, imag_part)
    new_imag = mat(cos_inner, imag_part) - mat(sin_inner, real_part)
    new_real = (new_real.reshape(kept * devices_tm, columns) / samples).astype(jnp.bfloat16)
    new_imag = (new_imag.reshape(kept * devices_tm, columns) / samples).astype(jnp.bfloat16)
    return jnp.stack([new_real, new_imag])


def swap_blocks(blocks, axis, ordered):
    count = lax.axis_size(axis)
    if count > 8:
        received = lax.all_to_all(blocks, axis, 0, 0, tiled=True)
        if ordered:
            return received, jnp.arange(count, dtype=jnp.int32)
        return jnp.sum(received, axis=0)
    me = lax.axis_index(axis)
    arrived = [lax.dynamic_index_in_dim(blocks, me, 0, keepdims=False)]
    for shift in range(1, count):
        outgoing = lax.dynamic_index_in_dim(blocks, (me + shift) % count, 0, keepdims=False)
        pairs = [(src, (src + shift) % count) for src in range(count)]
        arrived.append(lax.ppermute(outgoing, axis, pairs))
    if not ordered:
        total = arrived[0]
        for part in arrived[1:]:
            total = total + part
        return total
    return jnp.stack(arrived), (me - jnp.arange(count, dtype=jnp.int32)) % count


def packed_partials(real_in, imag_in, position, samples, sources):
    devices_tm, block_len, columns = real_in.shape
    index = jnp.arange(devices_tm, dtype=jnp.int32)
    cos_table, sin_table = phase_tables(index, sources, devices_tm)
    cos_b = cos_table[:, :, None, None]
    sin_b = sin_table[:, :, None, None]
    real_part = jnp.sum(cos_b * real_in[None] + sin_b * imag_in[None], axis=1)
    imag_part = jnp.sum(cos_b * imag_in[None] - sin_b * real_in[None], axis=1)
    local_epoch = position * block_len + jnp.arange(block_len, dtype=jnp.int32)
    real_part, imag_part = rotate(real_part, imag_part, index, local_epoch, samples)
    return jnp.stack([real_part, imag_part], axis=1)


def packed_transform(gathered):
    devices_tm, _, block_len, columns = gathered.shape
    length = devices_tm * block_len
    index = jnp.arange(devices_tm, dtype=jnp.int32)
    cos_table, sin_table = phase_tables(index, index, devices_tm)
    real_in = gathered[:, 0]
    imag_in = gathered[:, 1]
    cos_b = cos_table[:, :, None, None]
    sin_b = sin_table[:, :, None, None]
    real_part = jnp.sum(cos_b * real_in[None] + sin_b * imag_in[None], axis=1)
    imag_part = jnp.sum(cos_b * imag_in[None] - sin_b * real_in[None], axis=1)
    real_part, imag_part = rotate(
        real_part, imag_part, index, jnp.arange(block_len, dtype=jnp.int32), length
    )
    kept = block_len // 2 + 1
    rows = jnp.arange(kept, dtype=jnp.int32)
    cols = jnp.arange(block_len, dtype=jnp.int32)
    cos_own, sin_own = phase_tables(rows, cols, block_len)
    cos_far, sin_far = phase_tables(block_len - 1 - rows, cols, block_len)
    dims = (((1,), (1,)), ((), ()))

    def mat(table, value):
        return lax.dot_general(
            table, value, dims, precision=lax.Precision.HIGH,
            preferred_element_type=jnp.float32,
        )

    def apply(cos_table, sin_table, real_in, imag_in):
        table = jnp.concatenate([cos_table, sin_table], axis=0)
        from_real = mat(table, real_in)
        from_imag = mat(table, imag_in)
        new_real = from_real[:kept] + from_imag[kept:]
        new_imag = from_imag[:kept] - from_real[kept:]
        return jnp.stack([new_real, new_imag]).reshape(2, kept * devices_tm, columns)

    own = apply(cos_own, sin_own, real_part, imag_part)
    far = apply(cos_far, sin_far, real_part[::-1], imag_part[::-1])
    return own, far


def unpack_spectra(own, far, position, samples):
    devices_tm = lax.axis_size("tm")
    shifted = jnp.concatenate([own[:, :1], far[:, :-1]], axis=1)
    outgoing = jnp.where(position == 0, shifted, far)
    pairs = [(src, (devices_tm - src) % devices_tm) for src in range(devices_tm)]
    mirror = lax.ppermute(outgoing, "tm", pairs)
    own_real = own[0]
    own_imag = own[1]
    first_real = (own_real + mirror[0]) * 0.5
    first_imag = (own_imag - mirror[1]) * 0.5
    second_real = (own_imag + mirror[1]) * 0.5
    second_imag = (mirror[0] - own_real) * 0.5
    new_real = jnp.concatenate([first_real, second_real], axis=1) / samples
    new_imag = jnp.concatenate([first_imag, second_imag], axis=1) / samples
    return jnp.stack([new_real.astype(jnp.bfloat16), new_imag.astype(jnp.bfloat16)])


def body(orbit_angles, gap_mask, column_index, lat_coeffs, psd_table):
    devices_tm = lax.axis_size("tm")
    panels = lax.axis_size("panel")
    epochs = orbit_angles.shape[1]
    block_len = epochs // devices_tm
    samples = epochs * devices_tm
    columns = lat_coeffs.shape[2]
    coeffs = lat_coeffs[0]
    keep_rows = gap_mask.astype(jnp.float32)
    packed = jnp.concatenate([orbit_angles, keep_rows[None]], axis=0)
    packed = packed.reshape(3, devices_tm, block_len).transpose(1, 0, 2)
    masked, norm_scale = column_factors(column_index, coeffs)
    packed, masked, norm_scale = lax.optimization_barrier((packed, masked, norm_scale))
    received, sources = swap_blocks(packed, "tm", True)
    flat_orbit = received.transpose(1, 0, 2).reshape(3, devices_tm * block_len)
    spread = synthesize(flat_orbit[0:2], flat_orbit[2], column_index, masked, norm_scale).reshape(
        devices_tm, block_len, columns
    )
    position = lax.axis_index("tm")
    half_cols = columns // 2
    twisted = packed_partials(
        spread[..., :half_cols], spread[..., half_cols:], position, samples, sources
    )
    gathered = lax.all_to_all(twisted, "tm", 0, 0, tiled=True)
    own, far = packed_transform(gathered)
    spectra = unpack_spectra(own, far, position, samples)
    inverse_psd, fold = inverse_weights(
        psd_table[0], position, devices_tm, epochs, samples, spectra.shape[1]
    )
    weighted = (spectra.astype(jnp.float32) * inverse_psd[None, :, None]).astype(jnp.bfloat16)
    weighted = weighted * fold[None, :, None].astype(jnp.bfloat16)
    contract = (((0, 1), (0, 1)), ((), ()))
    products = [
        lax.dot_general(block, weighted, contract, preferred_element_type=jnp.float32)
        for block in panel_spectra(spectra)
    ]
    by_shift = jnp.stack(products)
    panel = lax.axis_index("panel")
    order = (panel - jnp.arange(panels, dtype=jnp.int32)) % panels
    partial_value = jnp.take(by_shift, order, axis=0).reshape(panels * columns, columns)
    return settle_rows(partial_value)


def settle_rows(partial_value):
    devices_tm = lax.axis_size("tm")
    comps = lax.axis_size("comp")
    rows_total, columns = partial_value.shape
    rows = rows_total // devices_tm
    if comps != 2 or columns % 256 != 0 or devices_tm <= 8:
        return comp_sum(swap_blocks(partial_value.reshape(devices_tm, rows, columns), "tm", False))
    half = columns // 2
    comp = lax.axis_index("comp")
    mine = lax.dynamic_slice_in_dim(partial_value, comp * half, half, axis=1)
    theirs = lax.dynamic_slice_in_dim(partial_value, (1 - comp) * half, half, axis=1)
    summed = mine + lax.ppermute(theirs, "comp", [(0, 1), (1, 0)])
    block = swap_blocks(summed.reshape(devices_tm, rows, half), "tm", False)
    other = lax.ppermute(block, "comp", [(0, 1), (1, 0)])
    first = jnp.where(comp == 0, block, other)
    second = jnp.where(comp == 0, other, block)
    return jnp.concatenate([first, second], axis=1)


def solution(mesh):
    return jax.shard_map(
        body,
        mesh=mesh,
        in_specs=(
            P(None, ("groups", "tm")),
            P(("groups", "tm")),
            P(None, "panel"),
            P("comp", None, "panel"),
            P("comp", None),
        ),
        out_specs=P(("groups", "tm"), "panel"),
        check_vma=False,
    )
```

```python
import math

import jax
import jax.numpy as jnp
from jax import lax
from jax.sharding import PartitionSpec as P

SPLIT = 64


def rounding_error(value, factor, product):
    high = lax.reduce_precision(value, exponent_bits=8, mantissa_bits=11)
    low = value - high
    return (product - high * factor) - low * factor


def colatitude_basis(colatitude, terms):
    wavenumbers = jnp.arange(terms, dtype=jnp.float32)
    theta = colatitude[:, None]
    phases = lax.optimization_barrier(theta * wavenumbers[None, :])
    if terms % 16 != 0:
        return jnp.concatenate([jnp.cos(phases), jnp.sin(phases)], axis=1)
    groups = terms // 16
    coarse = jnp.arange(groups, dtype=jnp.float32) * 16.0
    fine = jnp.arange(16, dtype=jnp.float32)
    phase_a = lax.optimization_barrier(theta * coarse[None, :])
    phase_b = lax.optimization_barrier(theta * fine[None, :])
    count = colatitude.shape[0]
    delta = (
        rounding_error(theta, wavenumbers[None, :], phases).reshape(count, groups, 16)
        - rounding_error(theta, coarse[None, :], phase_a)[:, :, None]
        - rounding_error(theta, fine[None, :], phase_b)[:, None, :]
    )
    cos_a = jnp.cos(phase_a)[:, :, None]
    sin_a = jnp.sin(phase_a)[:, :, None]
    cos_b = jnp.cos(phase_b)[:, None, :]
    sin_b = jnp.sin(phase_b)[:, None, :]
    cos_sum = cos_a * cos_b - sin_a * sin_b
    sin_sum = sin_a * cos_b + cos_a * sin_b
    cos_k = (cos_sum - delta * sin_sum).reshape(count, terms)
    sin_k = (sin_sum + delta * cos_sum).reshape(count, terms)
    return jnp.concatenate([cos_k, sin_k], axis=1)


def synthesize(angles, keep_rows, column_index, coeffs):
    terms_lat = coeffs.shape[0] // 2
    colatitude = angles[0]
    longit = angles[1]
    basis_rows = colatitude_basis(colatitude, terms_lat).astype(jnp.bfloat16)
    degree = column_index[0]
    orders = column_index[1]
    levels = jnp.arange(2 * terms_lat, dtype=jnp.int32) % terms_lat
    allowed = levels[:, None] <= degree[None, :]
    masked = jnp.where(allowed, coeffs, jnp.zeros_like(coeffs))
    latitude = jnp.dot(basis_rows, masked, preferred_element_type=jnp.float32)
    lon_phase = longit[:, None] * jnp.abs(orders).astype(jnp.float32)[None, :]
    lon_wave = jnp.where(orders[None, :] >= 0, jnp.cos(lon_phase), jnp.sin(lon_phase))
    norm_scale = 1.0 / jnp.sqrt(degree.astype(jnp.float32) + 1.0)
    return latitude * lon_wave * (keep_rows[:, None] * norm_scale[None, :])


def phase_tables(row_index, col_index, length):
    product = row_index[:, None] * col_index[None, :] % length
    angle_grid = product.astype(jnp.float32) * (2.0 * math.pi / length)
    return (jnp.cos(angle_grid), jnp.sin(angle_grid))


def dft_tables(length):
    indices = jnp.arange(length, dtype=jnp.int32)
    return phase_tables(indices, indices, length)


def rotate(real_part, imag_part, outer_index, inner_index, length):
    index_grid = outer_index[:, None] * inner_index[None, :] % length
    angle_grid = index_grid.astype(jnp.float32) * (2.0 * math.pi / length)
    cosine = jnp.cos(angle_grid)[:, :, None]
    sine_grid = jnp.sin(angle_grid)[:, :, None]
    return (real_part * cosine + imag_part * sine_grid, imag_part * cosine - real_part * sine_grid)


def precise_dot(left_side, right_side):
    return jnp.dot(
        left_side, right_side, precision=lax.Precision.HIGHEST, preferred_element_type=jnp.float32
    )


def transform(cos_table, sin_table, real_part, imag_part):
    new_real = precise_dot(cos_table, real_part) + precise_dot(sin_table, imag_part)
    new_imag = precise_dot(cos_table, imag_part) - precise_dot(sin_table, real_part)
    return (new_real, new_imag)


def four_step(real_in, imag_in, samples):
    length = real_in.shape[0]
    columns = real_in.shape[1]
    outer_count = SPLIT
    inner_count = length // SPLIT
    real_part = real_in.reshape(outer_count, inner_count * columns)
    imag_part = imag_in.reshape(outer_count, inner_count * columns)
    cos_outer, sin_outer = dft_tables(outer_count)
    real_part, imag_part = transform(cos_outer, sin_outer, real_part, imag_part)
    real_part = real_part.reshape(outer_count, inner_count, columns)
    imag_part = imag_part.reshape(outer_count, inner_count, columns)
    real_part, imag_part = rotate(
        real_part,
        imag_part,
        jnp.arange(outer_count, dtype=jnp.int32),
        jnp.arange(inner_count, dtype=jnp.int32),
        length,
    )
    real_part = jnp.transpose(real_part, (1, 0, 2)).reshape(inner_count, outer_count * columns)
    imag_part = jnp.transpose(imag_part, (1, 0, 2)).reshape(inner_count, outer_count * columns)
    cos_inner, sin_inner = dft_tables(inner_count)
    real_part, imag_part = transform(cos_inner, sin_inner, real_part, imag_part)
    return (
        real_part.reshape(length, columns) / samples,
        imag_part.reshape(length, columns) / samples,
    )


def local_transform(received, samples):
    real_part, imag_part = four_step(received[0, 0], received[1, 0], samples)
    return (real_part.astype(jnp.bfloat16), imag_part.astype(jnp.bfloat16))


def inverse_weights(psd_row, position, devices_tm, epochs, samples, count):
    half = samples // 2
    mirrored = jnp.concatenate([psd_row[: half + 1], psd_row[1:half][::-1]])
    picked = lax.dynamic_slice_in_dim(mirrored.reshape(epochs, devices_tm), position, 1, axis=1)
    inverse = 8192.0 / picked[:count, 0].astype(jnp.float32)
    order = jnp.arange(count, dtype=jnp.int32)
    first = jnp.where(position == 0, 1.0, 2.0)
    middle = jnp.where(position == 0, 1.0, 0.0)
    fold = jnp.where(
        order == 0, first, jnp.where(order < epochs // 2, 2.0, jnp.where(order == epochs // 2, middle, 0.0))
    )
    return inverse, fold


def panel_spectra(spectra):
    panels = lax.axis_size("panel")
    blocks = [spectra]
    for shift in range(1, panels):
        pairs = [(src, (src + shift) % panels) for src in range(panels)]
        blocks.append(lax.ppermute(spectra, "panel", pairs))
    return blocks


def comp_sum(value):
    comps = lax.axis_size("comp")
    if comps == 1:
        return value
    if comps != 2:
        return lax.psum(value, "comp")
    other = lax.ppermute(value, "comp", [(0, 1), (1, 0)])
    return value + other


def class_partials(spread, position, samples):
    devices_tm, block_len, columns = spread.shape
    index = jnp.arange(devices_tm, dtype=jnp.int32)
    cos_table, sin_table = phase_tables(index, index, devices_tm)
    real_part = jnp.sum(cos_table[:, :, None, None] * spread[None], axis=1)
    imag_part = -jnp.sum(sin_table[:, :, None, None] * spread[None], axis=1)
    local_epoch = position * block_len + jnp.arange(block_len, dtype=jnp.int32)
    real_part, imag_part = rotate(real_part, imag_part, index, local_epoch, samples)
    return jnp.stack([real_part, imag_part], axis=1)


def class_spectrum(gathered, samples):
    devices_tm, _, block_len, columns = gathered.shape
    length = devices_tm * block_len
    index = jnp.arange(devices_tm, dtype=jnp.int32)
    cos_table, sin_table = phase_tables(index, index, devices_tm)
    real_in = gathered[:, 0]
    imag_in = gathered[:, 1]
    cos_b = cos_table[:, :, None, None]
    sin_b = sin_table[:, :, None, None]
    real_part = jnp.sum(cos_b * real_in[None] + sin_b * imag_in[None], axis=1)
    imag_part = jnp.sum(cos_b * imag_in[None] - sin_b * real_in[None], axis=1)
    real_part, imag_part = rotate(
        real_part, imag_part, index, jnp.arange(block_len, dtype=jnp.int32), length
    )
    kept = block_len // 2 + 1
    cos_inner, sin_inner = phase_tables(
        jnp.arange(kept, dtype=jnp.int32), jnp.arange(block_len, dtype=jnp.int32), block_len
    )
    dims = (((1,), (1,)), ((), ()))

    def mat(table, value):
        return lax.dot_general(
            table, value, dims, precision=lax.Precision.HIGH,
            preferred_element_type=jnp.float32,
        )

    new_real = mat(cos_inner, real_part) + mat(sin_inner, imag_part)
    new_imag = mat(cos_inner, imag_part) - mat(sin_inner, real_part)
    new_real = (new_real.reshape(kept * devices_tm, columns) / samples).astype(jnp.bfloat16)
    new_imag = (new_imag.reshape(kept * devices_tm, columns) / samples).astype(jnp.bfloat16)
    return jnp.stack([new_real, new_imag])


def swap_blocks(blocks, axis, ordered):
    count = lax.axis_size(axis)
    if count > 8:
        received = lax.all_to_all(blocks, axis, 0, 0, tiled=True)
        if ordered:
            return received, jnp.arange(count, dtype=jnp.int32)
        return jnp.sum(received, axis=0)
    me = lax.axis_index(axis)
    arrived = [lax.dynamic_index_in_dim(blocks, me, 0, keepdims=False)]
    for shift in range(1, count):
        outgoing = lax.dynamic_index_in_dim(blocks, (me + shift) % count, 0, keepdims=False)
        pairs = [(src, (src + shift) % count) for src in range(count)]
        arrived.append(lax.ppermute(outgoing, axis, pairs))
    if not ordered:
        total = arrived[0]
        for part in arrived[1:]:
            total = total + part
        return total
    return jnp.stack(arrived), (me - jnp.arange(count, dtype=jnp.int32)) % count


def packed_partials(real_in, imag_in, position, samples, sources):
    devices_tm, block_len, columns = real_in.shape
    index = jnp.arange(devices_tm, dtype=jnp.int32)
    cos_table, sin_table = phase_tables(index, sources, devices_tm)
    cos_b = cos_table[:, :, None, None]
    sin_b = sin_table[:, :, None, None]
    real_part = jnp.sum(cos_b * real_in[None] + sin_b * imag_in[None], axis=1)
    imag_part = jnp.sum(cos_b * imag_in[None] - sin_b * real_in[None], axis=1)
    local_epoch = position * block_len + jnp.arange(block_len, dtype=jnp.int32)
    real_part, imag_part = rotate(real_part, imag_part, index, local_epoch, samples)
    return jnp.stack([real_part, imag_part], axis=1)


def packed_transform(gathered):
    devices_tm, _, block_len, columns = gathered.shape
    length = devices_tm * block_len
    index = jnp.arange(devices_tm, dtype=jnp.int32)
    cos_table, sin_table = phase_tables(index, index, devices_tm)
    real_in = gathered[:, 0]
    imag_in = gathered[:, 1]
    cos_b = cos_table[:, :, None, None]
    sin_b = sin_table[:, :, None, None]
    real_part = jnp.sum(cos_b * real_in[None] + sin_b * imag_in[None], axis=1)
    imag_part = jnp.sum(cos_b * imag_in[None] - sin_b * real_in[None], axis=1)
    real_part, imag_part = rotate(
        real_part, imag_part, index, jnp.arange(block_len, dtype=jnp.int32), length
    )
    kept = block_len // 2 + 1
    rows = jnp.arange(kept, dtype=jnp.int32)
    cols = jnp.arange(block_len, dtype=jnp.int32)
    cos_own, sin_own = phase_tables(rows, cols, block_len)
    cos_far, sin_far = phase_tables(block_len - 1 - rows, cols, block_len)
    dims = (((1,), (1,)), ((), ()))

    def mat(table, value):
        return lax.dot_general(
            table, value, dims, precision=lax.Precision.HIGH,
            preferred_element_type=jnp.float32,
        )

    def apply(cos_table, sin_table, real_in, imag_in):
        table = jnp.concatenate([cos_table, sin_table], axis=0)
        from_real = mat(table, real_in)
        from_imag = mat(table, imag_in)
        new_real = from_real[:kept] + from_imag[kept:]
        new_imag = from_imag[:kept] - from_real[kept:]
        return jnp.stack([new_real, new_imag]).reshape(2, kept * devices_tm, columns)

    own = apply(cos_own, sin_own, real_part, imag_part)
    far = apply(cos_far, sin_far, real_part[::-1], imag_part[::-1])
    return own, far


def unpack_spectra(own, far, position, samples):
    devices_tm = lax.axis_size("tm")
    shifted = jnp.concatenate([own[:, :1], far[:, :-1]], axis=1)
    outgoing = jnp.where(position == 0, shifted, far)
    pairs = [(src, (devices_tm - src) % devices_tm) for src in range(devices_tm)]
    mirror = lax.ppermute(outgoing, "tm", pairs)
    own_real = own[0]
    own_imag = own[1]
    first_real = (own_real + mirror[0]) * 0.5
    first_imag = (own_imag - mirror[1]) * 0.5
    second_real = (own_imag + mirror[1]) * 0.5
    second_imag = (mirror[0] - own_real) * 0.5
    new_real = jnp.concatenate([first_real, second_real], axis=1) / samples
    new_imag = jnp.concatenate([first_imag, second_imag], axis=1) / samples
    return jnp.stack([new_real.astype(jnp.bfloat16), new_imag.astype(jnp.bfloat16)])


def packed_direct(spread, position, samples, sources):
    devices_tm, block_len, columns = spread.shape
    half_cols = columns // 2
    index = jnp.arange(devices_tm, dtype=jnp.int32)
    cos_table, sin_table = phase_tables(index, sources, devices_tm)
    local_epoch = position * block_len + jnp.arange(block_len, dtype=jnp.int32)
    cos_turn, sin_turn = phase_tables(index, local_epoch, samples)
    cos_k = cos_table[:, :, None]
    sin_k = sin_table[:, :, None]
    cos_u = cos_turn[:, None, :]
    sin_u = sin_turn[:, None, :]
    direct = cos_k * cos_u - sin_k * sin_u
    cross = sin_k * cos_u + cos_k * sin_u
    weights = jnp.stack(
        [jnp.stack([direct, cross], axis=-1), jnp.stack([-cross, direct], axis=-1)], axis=1
    )
    parts = spread.reshape(devices_tm, block_len, 2, half_cols)
    return jnp.sum(weights[..., None] * parts[None, None], axis=(2, 4))


def body(orbit_angles, gap_mask, column_index, lat_coeffs, psd_table):
    devices_tm = lax.axis_size("tm")
    panels = lax.axis_size("panel")
    epochs = orbit_angles.shape[1]
    block_len = epochs // devices_tm
    samples = epochs * devices_tm
    columns = lat_coeffs.shape[2]
    coeffs = lat_coeffs[0]
    keep_rows = gap_mask.astype(jnp.float32)
    packed = jnp.concatenate([orbit_angles, keep_rows[None]], axis=0)
    packed = packed.reshape(3, devices_tm, block_len).transpose(1, 0, 2)
    received, sources = swap_blocks(packed, "tm", True)
    flat_orbit = received.transpose(1, 0, 2).reshape(3, devices_tm * block_len)
    spread = synthesize(flat_orbit[0:2], flat_orbit[2], column_index, coeffs).reshape(
        devices_tm, block_len, columns
    )
    position = lax.axis_index("tm")
    half_cols = columns // 2
    twisted = packed_direct(spread, position, samples, sources)
    gathered = lax.all_to_all(twisted, "tm", 0, 0, tiled=True)
    own, far = packed_transform(gathered)
    spectra = unpack_spectra(own, far, position, samples)
    inverse_psd, fold = inverse_weights(
        psd_table[0], position, devices_tm, epochs, samples, spectra.shape[1]
    )
    weighted = (spectra.astype(jnp.float32) * inverse_psd[None, :, None]).astype(jnp.bfloat16)
    weighted = weighted * fold[None, :, None].astype(jnp.bfloat16)
    contract = (((0, 1), (0, 1)), ((), ()))
    products = [
        lax.dot_general(block, weighted, contract, preferred_element_type=jnp.float32)
        for block in panel_spectra(spectra)
    ]
    by_shift = jnp.stack(products)
    panel = lax.axis_index("panel")
    order = (panel - jnp.arange(panels, dtype=jnp.int32)) % panels
    partial_value = jnp.take(by_shift, order, axis=0).reshape(panels * columns, columns)
    return settle_rows(partial_value)


def settle_rows(partial_value):
    devices_tm = lax.axis_size("tm")
    comps = lax.axis_size("comp")
    rows_total, columns = partial_value.shape
    rows = rows_total // devices_tm
    if comps != 2 or columns % 256 != 0 or devices_tm <= 8:
        return comp_sum(swap_blocks(partial_value.reshape(devices_tm, rows, columns), "tm", False))
    half = columns // 2
    comp = lax.axis_index("comp")
    mine = lax.dynamic_slice_in_dim(partial_value, comp * half, half, axis=1)
    theirs = lax.dynamic_slice_in_dim(partial_value, (1 - comp) * half, half, axis=1)
    summed = mine + lax.ppermute(theirs, "comp", [(0, 1), (1, 0)])
    block = swap_blocks(summed.reshape(devices_tm, rows, half), "tm", False)
    other = lax.ppermute(block, "comp", [(0, 1), (1, 0)])
    first = jnp.where(comp == 0, block, other)
    second = jnp.where(comp == 0, other, block)
    return jnp.concatenate([first, second], axis=1)


def solution(mesh):
    return jax.shard_map(
        body,
        mesh=mesh,
        in_specs=(
            P(None, ("groups", "tm")),
            P(("groups", "tm")),
            P(None, "panel"),
            P("comp", None, "panel"),
            P("comp", None),
        ),
        out_specs=P(("groups", "tm"), "panel"),
        check_vma=False,
    )
```

```python
import math

import jax
import jax.numpy as jnp
from jax import lax
from jax.sharding import PartitionSpec as P

SPLIT = 64


def rounding_error(value, factor, product):
    high = lax.reduce_precision(value, exponent_bits=8, mantissa_bits=11)
    low = value - high
    return (product - high * factor) - low * factor


def colatitude_basis(colatitude, terms):
    wavenumbers = jnp.arange(terms, dtype=jnp.float32)
    theta = colatitude[:, None]
    phases = lax.optimization_barrier(theta * wavenumbers[None, :])
    if terms % 16 != 0:
        return jnp.concatenate([jnp.cos(phases), jnp.sin(phases)], axis=1)
    groups = terms // 16
    coarse = jnp.arange(groups, dtype=jnp.float32) * 16.0
    fine = jnp.arange(16, dtype=jnp.float32)
    phase_a = lax.optimization_barrier(theta * coarse[None, :])
    phase_b = lax.optimization_barrier(theta * fine[None, :])
    count = colatitude.shape[0]
    delta = (
        rounding_error(theta, wavenumbers[None, :], phases).reshape(count, groups, 16)
        - rounding_error(theta, coarse[None, :], phase_a)[:, :, None]
        - rounding_error(theta, fine[None, :], phase_b)[:, None, :]
    )
    cos_a = jnp.cos(phase_a)[:, :, None]
    sin_a = jnp.sin(phase_a)[:, :, None]
    cos_b = jnp.cos(phase_b)[:, None, :]
    sin_b = jnp.sin(phase_b)[:, None, :]
    cos_sum = cos_a * cos_b - sin_a * sin_b
    sin_sum = sin_a * cos_b + cos_a * sin_b
    cos_k = (cos_sum - delta * sin_sum).reshape(count, terms)
    sin_k = (sin_sum + delta * cos_sum).reshape(count, terms)
    return jnp.concatenate([cos_k, sin_k], axis=1)


def synthesize(angles, keep_rows, column_index, coeffs):
    terms_lat = coeffs.shape[0] // 2
    colatitude = angles[0]
    longit = angles[1]
    basis_rows = colatitude_basis(colatitude, terms_lat).astype(jnp.bfloat16)
    degree = column_index[0]
    orders = column_index[1]
    levels = jnp.arange(2 * terms_lat, dtype=jnp.int32) % terms_lat
    allowed = levels[:, None] <= degree[None, :]
    masked = jnp.where(allowed, coeffs, jnp.zeros_like(coeffs))
    latitude = jnp.dot(basis_rows, masked, preferred_element_type=jnp.float32)
    lon_phase = longit[:, None] * jnp.abs(orders).astype(jnp.float32)[None, :]
    lon_wave = jnp.where(orders[None, :] >= 0, jnp.cos(lon_phase), jnp.sin(lon_phase))
    norm_scale = 1.0 / jnp.sqrt(degree.astype(jnp.float32) + 1.0)
    return latitude * lon_wave * (keep_rows[:, None] * norm_scale[None, :])


def phase_tables(row_index, col_index, length):
    product = row_index[:, None] * col_index[None, :] % length
    angle_grid = product.astype(jnp.float32) * (2.0 * math.pi / length)
    return (jnp.cos(angle_grid), jnp.sin(angle_grid))


def dft_tables(length):
    indices = jnp.arange(length, dtype=jnp.int32)
    return phase_tables(indices, indices, length)


def rotate(real_part, imag_part, outer_index, inner_index, length):
    index_grid = outer_index[:, None] * inner_index[None, :] % length
    angle_grid = index_grid.astype(jnp.float32) * (2.0 * math.pi / length)
    cosine = jnp.cos(angle_grid)[:, :, None]
    sine_grid = jnp.sin(angle_grid)[:, :, None]
    return (real_part * cosine + imag_part * sine_grid, imag_part * cosine - real_part * sine_grid)


def precise_dot(left_side, right_side):
    return jnp.dot(
        left_side, right_side, precision=lax.Precision.HIGHEST, preferred_element_type=jnp.float32
    )


def transform(cos_table, sin_table, real_part, imag_part):
    new_real = precise_dot(cos_table, real_part) + precise_dot(sin_table, imag_part)
    new_imag = precise_dot(cos_table, imag_part) - precise_dot(sin_table, real_part)
    return (new_real, new_imag)


def four_step(real_in, imag_in, samples):
    length = real_in.shape[0]
    columns = real_in.shape[1]
    outer_count = SPLIT
    inner_count = length // SPLIT
    real_part = real_in.reshape(outer_count, inner_count * columns)
    imag_part = imag_in.reshape(outer_count, inner_count * columns)
    cos_outer, sin_outer = dft_tables(outer_count)
    real_part, imag_part = transform(cos_outer, sin_outer, real_part, imag_part)
    real_part = real_part.reshape(outer_count, inner_count, columns)
    imag_part = imag_part.reshape(outer_count, inner_count, columns)
    real_part, imag_part = rotate(
        real_part,
        imag_part,
        jnp.arange(outer_count, dtype=jnp.int32),
        jnp.arange(inner_count, dtype=jnp.int32),
        length,
    )
    real_part = jnp.transpose(real_part, (1, 0, 2)).reshape(inner_count, outer_count * columns)
    imag_part = jnp.transpose(imag_part, (1, 0, 2)).reshape(inner_count, outer_count * columns)
    cos_inner, sin_inner = dft_tables(inner_count)
    real_part, imag_part = transform(cos_inner, sin_inner, real_part, imag_part)
    return (
        real_part.reshape(length, columns) / samples,
        imag_part.reshape(length, columns) / samples,
    )


def local_transform(received, samples):
    real_part, imag_part = four_step(received[0, 0], received[1, 0], samples)
    return (real_part.astype(jnp.bfloat16), imag_part.astype(jnp.bfloat16))


def inverse_weights(psd_row, position, devices_tm, epochs, samples, count):
    half = samples // 2
    mirrored = jnp.concatenate([psd_row[: half + 1], psd_row[1:half][::-1]])
    picked = lax.dynamic_slice_in_dim(mirrored.reshape(epochs, devices_tm), position, 1, axis=1)
    inverse = 8192.0 / picked[:count, 0].astype(jnp.float32)
    order = jnp.arange(count, dtype=jnp.int32)
    first = jnp.where(position == 0, 1.0, 2.0)
    middle = jnp.where(position == 0, 1.0, 0.0)
    fold = jnp.where(
        order == 0, first, jnp.where(order < epochs // 2, 2.0, jnp.where(order == epochs // 2, middle, 0.0))
    )
    return inverse, fold


def panel_spectra(spectra):
    panels = lax.axis_size("panel")
    blocks = [spectra]
    for shift in range(1, panels):
        pairs = [(src, (src + shift) % panels) for src in range(panels)]
        blocks.append(lax.ppermute(spectra, "panel", pairs))
    return blocks


def comp_sum(value):
    comps = lax.axis_size("comp")
    if comps == 1:
        return value
    if comps != 2:
        return lax.psum(value, "comp")
    other = lax.ppermute(value, "comp", [(0, 1), (1, 0)])
    return value + other


def class_partials(spread, position, samples):
    devices_tm, block_len, columns = spread.shape
    index = jnp.arange(devices_tm, dtype=jnp.int32)
    cos_table, sin_table = phase_tables(index, index, devices_tm)
    real_part = jnp.sum(cos_table[:, :, None, None] * spread[None], axis=1)
    imag_part = -jnp.sum(sin_table[:, :, None, None] * spread[None], axis=1)
    local_epoch = position * block_len + jnp.arange(block_len, dtype=jnp.int32)
    real_part, imag_part = rotate(real_part, imag_part, index, local_epoch, samples)
    return jnp.stack([real_part, imag_part], axis=1)


def class_spectrum(gathered, samples):
    devices_tm, _, block_len, columns = gathered.shape
    length = devices_tm * block_len
    index = jnp.arange(devices_tm, dtype=jnp.int32)
    cos_table, sin_table = phase_tables(index, index, devices_tm)
    real_in = gathered[:, 0]
    imag_in = gathered[:, 1]
    cos_b = cos_table[:, :, None, None]
    sin_b = sin_table[:, :, None, None]
    real_part = jnp.sum(cos_b * real_in[None] + sin_b * imag_in[None], axis=1)
    imag_part = jnp.sum(cos_b * imag_in[None] - sin_b * real_in[None], axis=1)
    real_part, imag_part = rotate(
        real_part, imag_part, index, jnp.arange(block_len, dtype=jnp.int32), length
    )
    kept = block_len // 2 + 1
    cos_inner, sin_inner = phase_tables(
        jnp.arange(kept, dtype=jnp.int32), jnp.arange(block_len, dtype=jnp.int32), block_len
    )
    dims = (((1,), (1,)), ((), ()))

    def mat(table, value):
        return lax.dot_general(
            table, value, dims, precision=lax.Precision.HIGH,
            preferred_element_type=jnp.float32,
        )

    new_real = mat(cos_inner, real_part) + mat(sin_inner, imag_part)
    new_imag = mat(cos_inner, imag_part) - mat(sin_inner, real_part)
    new_real = (new_real.reshape(kept * devices_tm, columns) / samples).astype(jnp.bfloat16)
    new_imag = (new_imag.reshape(kept * devices_tm, columns) / samples).astype(jnp.bfloat16)
    return jnp.stack([new_real, new_imag])


def swap_blocks(blocks, axis, ordered):
    count = lax.axis_size(axis)
    if count > 8:
        received = lax.all_to_all(blocks, axis, 0, 0, tiled=True)
        if ordered:
            return received, jnp.arange(count, dtype=jnp.int32)
        return jnp.sum(received, axis=0)
    me = lax.axis_index(axis)
    arrived = [lax.dynamic_index_in_dim(blocks, me, 0, keepdims=False)]
    for shift in range(1, count):
        outgoing = lax.dynamic_index_in_dim(blocks, (me + shift) % count, 0, keepdims=False)
        pairs = [(src, (src + shift) % count) for src in range(count)]
        arrived.append(lax.ppermute(outgoing, axis, pairs))
    if not ordered:
        total = arrived[0]
        for part in arrived[1:]:
            total = total + part
        return total
    return jnp.stack(arrived), (me - jnp.arange(count, dtype=jnp.int32)) % count


def packed_partials(real_in, imag_in, position, samples, sources):
    devices_tm, block_len, columns = real_in.shape
    index = jnp.arange(devices_tm, dtype=jnp.int32)
    cos_table, sin_table = phase_tables(index, sources, devices_tm)
    cos_b = cos_table[:, :, None, None]
    sin_b = sin_table[:, :, None, None]
    real_part = jnp.sum(cos_b * real_in[None] + sin_b * imag_in[None], axis=1)
    imag_part = jnp.sum(cos_b * imag_in[None] - sin_b * real_in[None], axis=1)
    local_epoch = position * block_len + jnp.arange(block_len, dtype=jnp.int32)
    real_part, imag_part = rotate(real_part, imag_part, index, local_epoch, samples)
    return jnp.stack([real_part, imag_part], axis=1)


def packed_transform(gathered):
    devices_tm, _, block_len, columns = gathered.shape
    length = devices_tm * block_len
    index = jnp.arange(devices_tm, dtype=jnp.int32)
    cos_table, sin_table = phase_tables(index, index, devices_tm)
    real_in = gathered[:, 0]
    imag_in = gathered[:, 1]
    cos_b = cos_table[:, :, None, None]
    sin_b = sin_table[:, :, None, None]
    real_part = jnp.sum(cos_b * real_in[None] + sin_b * imag_in[None], axis=1)
    imag_part = jnp.sum(cos_b * imag_in[None] - sin_b * real_in[None], axis=1)
    real_part, imag_part = rotate(
        real_part, imag_part, index, jnp.arange(block_len, dtype=jnp.int32), length
    )
    kept = block_len // 2 + 1
    rows = jnp.arange(kept, dtype=jnp.int32)
    cols = jnp.arange(block_len, dtype=jnp.int32)
    cos_own, sin_own = phase_tables(rows, cols, block_len)
    cos_far, sin_far = phase_tables(block_len - 1 - rows, cols, block_len)
    dims = (((1,), (1,)), ((), ()))

    def mat(table, value):
        return lax.dot_general(
            table, value, dims, precision=lax.Precision.HIGH,
            preferred_element_type=jnp.float32,
        )

    def apply(cos_table, sin_table, real_in, imag_in):
        table = jnp.concatenate([cos_table, sin_table], axis=0)
        from_real = mat(table, real_in)
        from_imag = mat(table, imag_in)
        new_real = from_real[:kept] + from_imag[kept:]
        new_imag = from_imag[:kept] - from_real[kept:]
        return jnp.stack([new_real, new_imag]).reshape(2, kept * devices_tm, columns)

    table = jnp.concatenate([cos_own, sin_own, cos_far, sin_far], axis=0)
    from_real = mat(table, real_part)
    from_imag = mat(table, imag_part)
    own_real = from_real[:kept] + from_imag[kept:2 * kept]
    own_imag = from_imag[:kept] - from_real[kept:2 * kept]
    far_real = from_real[2 * kept:3 * kept] + from_imag[3 * kept:]
    far_imag = from_imag[2 * kept:3 * kept] - from_real[3 * kept:]
    own = jnp.stack([own_real, own_imag]).reshape(2, kept * devices_tm, columns)
    far = jnp.stack([far_real, far_imag])[:, :, ::-1].reshape(2, kept * devices_tm, columns)
    return own, far


def unpack_spectra(own, far, position, samples):
    devices_tm = lax.axis_size("tm")
    shifted = jnp.concatenate([own[:, :1], far[:, :-1]], axis=1)
    outgoing = jnp.where(position == 0, shifted, far)
    pairs = [(src, (devices_tm - src) % devices_tm) for src in range(devices_tm)]
    mirror = lax.ppermute(outgoing, "tm", pairs)
    own_real = own[0]
    own_imag = own[1]
    first_real = (own_real + mirror[0]) * 0.5
    first_imag = (own_imag - mirror[1]) * 0.5
    second_real = (own_imag + mirror[1]) * 0.5
    second_imag = (mirror[0] - own_real) * 0.5
    new_real = jnp.concatenate([first_real, second_real], axis=1) / samples
    new_imag = jnp.concatenate([first_imag, second_imag], axis=1) / samples
    return jnp.stack([new_real.astype(jnp.bfloat16), new_imag.astype(jnp.bfloat16)])


def body(orbit_angles, gap_mask, column_index, lat_coeffs, psd_table):
    devices_tm = lax.axis_size("tm")
    panels = lax.axis_size("panel")
    epochs = orbit_angles.shape[1]
    block_len = epochs // devices_tm
    samples = epochs * devices_tm
    columns = lat_coeffs.shape[2]
    coeffs = lat_coeffs[0]
    keep_rows = gap_mask.astype(jnp.float32)
    packed = jnp.concatenate([orbit_angles, keep_rows[None]], axis=0)
    packed = packed.reshape(3, devices_tm, block_len).transpose(1, 0, 2)
    received, sources = swap_blocks(packed, "tm", True)
    flat_orbit = received.transpose(1, 0, 2).reshape(3, devices_tm * block_len)
    spread = synthesize(flat_orbit[0:2], flat_orbit[2], column_index, coeffs).reshape(
        devices_tm, block_len, columns
    )
    position = lax.axis_index("tm")
    half_cols = columns // 2
    twisted = packed_partials(
        spread[..., :half_cols], spread[..., half_cols:], position, samples, sources
    )
    gathered = lax.all_to_all(twisted, "tm", 0, 0, tiled=True)
    own, far = packed_transform(gathered)
    spectra = unpack_spectra(own, far, position, samples)
    inverse_psd, fold = inverse_weights(
        psd_table[0], position, devices_tm, epochs, samples, spectra.shape[1]
    )
    weighted = (spectra.astype(jnp.float32) * inverse_psd[None, :, None]).astype(jnp.bfloat16)
    weighted = weighted * fold[None, :, None].astype(jnp.bfloat16)
    contract = (((0, 1), (0, 1)), ((), ()))
    products = [
        lax.dot_general(block, weighted, contract, preferred_element_type=jnp.float32)
        for block in panel_spectra(spectra)
    ]
    by_shift = jnp.stack(products)
    panel = lax.axis_index("panel")
    order = (panel - jnp.arange(panels, dtype=jnp.int32)) % panels
    partial_value = jnp.take(by_shift, order, axis=0).reshape(panels * columns, columns)
    return settle_rows(partial_value)


def settle_rows(partial_value):
    devices_tm = lax.axis_size("tm")
    comps = lax.axis_size("comp")
    rows_total, columns = partial_value.shape
    rows = rows_total // devices_tm
    if comps != 2 or columns % 256 != 0 or devices_tm <= 8:
        return comp_sum(swap_blocks(partial_value.reshape(devices_tm, rows, columns), "tm", False))
    half = columns // 2
    comp = lax.axis_index("comp")
    mine = lax.dynamic_slice_in_dim(partial_value, comp * half, half, axis=1)
    theirs = lax.dynamic_slice_in_dim(partial_value, (1 - comp) * half, half, axis=1)
    summed = mine + lax.ppermute(theirs, "comp", [(0, 1), (1, 0)])
    block = swap_blocks(summed.reshape(devices_tm, rows, half), "tm", False)
    other = lax.ppermute(block, "comp", [(0, 1), (1, 0)])
    first = jnp.where(comp == 0, block, other)
    second = jnp.where(comp == 0, other, block)
    return jnp.concatenate([first, second], axis=1)


def solution(mesh):
    return jax.shard_map(
        body,
        mesh=mesh,
        in_specs=(
            P(None, ("groups", "tm")),
            P(("groups", "tm")),
            P(None, "panel"),
            P("comp", None, "panel"),
            P("comp", None),
        ),
        out_specs=P(("groups", "tm"), "panel"),
        check_vma=False,
    )
```

```python
import math

import jax
import jax.numpy as jnp
from jax import lax
from jax.sharding import PartitionSpec as P

SPLIT = 64


def rounding_error(value, factor, product):
    high = lax.reduce_precision(value, exponent_bits=8, mantissa_bits=11)
    low = value - high
    return (product - high * factor) - low * factor


def colatitude_basis(colatitude, terms):
    wavenumbers = jnp.arange(terms, dtype=jnp.float32)
    theta = colatitude[:, None]
    phases = lax.optimization_barrier(theta * wavenumbers[None, :])
    if terms % 16 != 0:
        return jnp.concatenate([jnp.cos(phases), jnp.sin(phases)], axis=1)
    groups = terms // 16
    coarse = jnp.arange(groups, dtype=jnp.float32) * 16.0
    fine = jnp.arange(16, dtype=jnp.float32)
    phase_a = lax.optimization_barrier(theta * coarse[None, :])
    phase_b = lax.optimization_barrier(theta * fine[None, :])
    count = colatitude.shape[0]
    delta = (
        rounding_error(theta, wavenumbers[None, :], phases).reshape(count, groups, 16)
        - rounding_error(theta, coarse[None, :], phase_a)[:, :, None]
        - rounding_error(theta, fine[None, :], phase_b)[:, None, :]
    )
    cos_a = jnp.cos(phase_a)[:, :, None]
    sin_a = jnp.sin(phase_a)[:, :, None]
    cos_b = jnp.cos(phase_b)[:, None, :]
    sin_b = jnp.sin(phase_b)[:, None, :]
    cos_sum = cos_a * cos_b - sin_a * sin_b
    sin_sum = sin_a * cos_b + cos_a * sin_b
    cos_k = (cos_sum - delta * sin_sum).reshape(count, terms)
    sin_k = (sin_sum + delta * cos_sum).reshape(count, terms)
    return jnp.concatenate([cos_k, sin_k], axis=1)


def synthesize(angles, keep_rows, column_index, coeffs):
    terms_lat = coeffs.shape[0] // 2
    colatitude = angles[0]
    longit = angles[1]
    basis_rows = colatitude_basis(colatitude, terms_lat).astype(jnp.bfloat16)
    degree = column_index[0]
    orders = column_index[1]
    levels = jnp.arange(2 * terms_lat, dtype=jnp.int32) % terms_lat
    allowed = levels[:, None] <= degree[None, :]
    masked = jnp.where(allowed, coeffs, jnp.zeros_like(coeffs))
    latitude = jnp.dot(basis_rows, masked, preferred_element_type=jnp.float32)
    lon_phase = longit[:, None] * jnp.abs(orders).astype(jnp.float32)[None, :]
    lon_wave = jnp.where(orders[None, :] >= 0, jnp.cos(lon_phase), jnp.sin(lon_phase))
    norm_scale = 1.0 / jnp.sqrt(degree.astype(jnp.float32) + 1.0)
    return latitude * lon_wave * (keep_rows[:, None] * norm_scale[None, :])


def phase_tables(row_index, col_index, length):
    product = row_index[:, None] * col_index[None, :] % length
    angle_grid = product.astype(jnp.float32) * (2.0 * math.pi / length)
    return (jnp.cos(angle_grid), jnp.sin(angle_grid))


def dft_tables(length):
    indices = jnp.arange(length, dtype=jnp.int32)
    return phase_tables(indices, indices, length)


def rotate(real_part, imag_part, outer_index, inner_index, length):
    index_grid = outer_index[:, None] * inner_index[None, :] % length
    angle_grid = index_grid.astype(jnp.float32) * (2.0 * math.pi / length)
    cosine = jnp.cos(angle_grid)[:, :, None]
    sine_grid = jnp.sin(angle_grid)[:, :, None]
    return (real_part * cosine + imag_part * sine_grid, imag_part * cosine - real_part * sine_grid)


def precise_dot(left_side, right_side):
    return jnp.dot(
        left_side, right_side, precision=lax.Precision.HIGHEST, preferred_element_type=jnp.float32
    )


def transform(cos_table, sin_table, real_part, imag_part):
    new_real = precise_dot(cos_table, real_part) + precise_dot(sin_table, imag_part)
    new_imag = precise_dot(cos_table, imag_part) - precise_dot(sin_table, real_part)
    return (new_real, new_imag)


def four_step(real_in, imag_in, samples):
    length = real_in.shape[0]
    columns = real_in.shape[1]
    outer_count = SPLIT
    inner_count = length // SPLIT
    real_part = real_in.reshape(outer_count, inner_count * columns)
    imag_part = imag_in.reshape(outer_count, inner_count * columns)
    cos_outer, sin_outer = dft_tables(outer_count)
    real_part, imag_part = transform(cos_outer, sin_outer, real_part, imag_part)
    real_part = real_part.reshape(outer_count, inner_count, columns)
    imag_part = imag_part.reshape(outer_count, inner_count, columns)
    real_part, imag_part = rotate(
        real_part,
        imag_part,
        jnp.arange(outer_count, dtype=jnp.int32),
        jnp.arange(inner_count, dtype=jnp.int32),
        length,
    )
    real_part = jnp.transpose(real_part, (1, 0, 2)).reshape(inner_count, outer_count * columns)
    imag_part = jnp.transpose(imag_part, (1, 0, 2)).reshape(inner_count, outer_count * columns)
    cos_inner, sin_inner = dft_tables(inner_count)
    real_part, imag_part = transform(cos_inner, sin_inner, real_part, imag_part)
    return (
        real_part.reshape(length, columns) / samples,
        imag_part.reshape(length, columns) / samples,
    )


def local_transform(received, samples):
    real_part, imag_part = four_step(received[0, 0], received[1, 0], samples)
    return (real_part.astype(jnp.bfloat16), imag_part.astype(jnp.bfloat16))


def inverse_weights(psd_row, position, devices_tm, epochs, samples, count):
    half = samples // 2
    mirrored = jnp.concatenate([psd_row[: half + 1], psd_row[1:half][::-1]])
    picked = lax.dynamic_slice_in_dim(mirrored.reshape(epochs, devices_tm), position, 1, axis=1)
    inverse = 8192.0 / picked[:count, 0].astype(jnp.float32)
    order = jnp.arange(count, dtype=jnp.int32)
    first = jnp.where(position == 0, 1.0, 2.0)
    middle = jnp.where(position == 0, 1.0, 0.0)
    fold = jnp.where(
        order == 0, first, jnp.where(order < epochs // 2, 2.0, jnp.where(order == epochs // 2, middle, 0.0))
    )
    return inverse, fold


def panel_spectra(spectra):
    panels = lax.axis_size("panel")
    blocks = [spectra]
    for shift in range(1, panels):
        pairs = [(src, (src + shift) % panels) for src in range(panels)]
        blocks.append(lax.ppermute(spectra, "panel", pairs))
    return blocks


def comp_sum(value):
    comps = lax.axis_size("comp")
    if comps == 1:
        return value
    if comps != 2:
        return lax.psum(value, "comp")
    other = lax.ppermute(value, "comp", [(0, 1), (1, 0)])
    return value + other


def class_partials(spread, position, samples):
    devices_tm, block_len, columns = spread.shape
    index = jnp.arange(devices_tm, dtype=jnp.int32)
    cos_table, sin_table = phase_tables(index, index, devices_tm)
    real_part = jnp.sum(cos_table[:, :, None, None] * spread[None], axis=1)
    imag_part = -jnp.sum(sin_table[:, :, None, None] * spread[None], axis=1)
    local_epoch = position * block_len + jnp.arange(block_len, dtype=jnp.int32)
    real_part, imag_part = rotate(real_part, imag_part, index, local_epoch, samples)
    return jnp.stack([real_part, imag_part], axis=1)


def class_spectrum(gathered, samples):
    devices_tm, _, block_len, columns = gathered.shape
    length = devices_tm * block_len
    index = jnp.arange(devices_tm, dtype=jnp.int32)
    cos_table, sin_table = phase_tables(index, index, devices_tm)
    real_in = gathered[:, 0]
    imag_in = gathered[:, 1]
    cos_b = cos_table[:, :, None, None]
    sin_b = sin_table[:, :, None, None]
    real_part = jnp.sum(cos_b * real_in[None] + sin_b * imag_in[None], axis=1)
    imag_part = jnp.sum(cos_b * imag_in[None] - sin_b * real_in[None], axis=1)
    real_part, imag_part = rotate(
        real_part, imag_part, index, jnp.arange(block_len, dtype=jnp.int32), length
    )
    kept = block_len // 2 + 1
    cos_inner, sin_inner = phase_tables(
        jnp.arange(kept, dtype=jnp.int32), jnp.arange(block_len, dtype=jnp.int32), block_len
    )
    dims = (((1,), (1,)), ((), ()))

    def mat(table, value):
        return lax.dot_general(
            table, value, dims, precision=lax.Precision.HIGH,
            preferred_element_type=jnp.float32,
        )

    new_real = mat(cos_inner, real_part) + mat(sin_inner, imag_part)
    new_imag = mat(cos_inner, imag_part) - mat(sin_inner, real_part)
    new_real = (new_real.reshape(kept * devices_tm, columns) / samples).astype(jnp.bfloat16)
    new_imag = (new_imag.reshape(kept * devices_tm, columns) / samples).astype(jnp.bfloat16)
    return jnp.stack([new_real, new_imag])


def swap_blocks(blocks, axis, ordered):
    count = lax.axis_size(axis)
    if count > 8:
        received = lax.all_to_all(blocks, axis, 0, 0, tiled=True)
        if ordered:
            return received, jnp.arange(count, dtype=jnp.int32)
        return jnp.sum(received, axis=0)
    me = lax.axis_index(axis)
    arrived = [lax.dynamic_index_in_dim(blocks, me, 0, keepdims=False)]
    for shift in range(1, count):
        outgoing = lax.dynamic_index_in_dim(blocks, (me + shift) % count, 0, keepdims=False)
        pairs = [(src, (src + shift) % count) for src in range(count)]
        arrived.append(lax.ppermute(outgoing, axis, pairs))
    if not ordered:
        total = arrived[0]
        for part in arrived[1:]:
            total = total + part
        return total
    return jnp.stack(arrived), (me - jnp.arange(count, dtype=jnp.int32)) % count


def packed_partials(real_in, imag_in, position, samples, sources):
    devices_tm, block_len, columns = real_in.shape
    index = jnp.arange(devices_tm, dtype=jnp.int32)
    cos_table, sin_table = phase_tables(index, sources, devices_tm)
    cos_b = cos_table[:, :, None, None]
    sin_b = sin_table[:, :, None, None]
    real_part = jnp.sum(cos_b * real_in[None] + sin_b * imag_in[None], axis=1)
    imag_part = jnp.sum(cos_b * imag_in[None] - sin_b * real_in[None], axis=1)
    local_epoch = position * block_len + jnp.arange(block_len, dtype=jnp.int32)
    real_part, imag_part = rotate(real_part, imag_part, index, local_epoch, samples)
    return jnp.stack([real_part, imag_part], axis=1)


def packed_transform(gathered):
    devices_tm, _, block_len, columns = gathered.shape
    length = devices_tm * block_len
    index = jnp.arange(devices_tm, dtype=jnp.int32)
    cos_table, sin_table = phase_tables(index, index, devices_tm)
    real_in = gathered[:, 0]
    imag_in = gathered[:, 1]
    cos_b = cos_table[:, :, None, None]
    sin_b = sin_table[:, :, None, None]
    real_part = jnp.sum(cos_b * real_in[None] + sin_b * imag_in[None], axis=1)
    imag_part = jnp.sum(cos_b * imag_in[None] - sin_b * real_in[None], axis=1)
    real_part, imag_part = rotate(
        real_part, imag_part, index, jnp.arange(block_len, dtype=jnp.int32), length
    )
    kept = block_len // 2 + 1
    rows = jnp.arange(kept, dtype=jnp.int32)
    cols = jnp.arange(block_len, dtype=jnp.int32)
    cos_own, sin_own = phase_tables(rows, cols, block_len)
    cos_far, sin_far = phase_tables(block_len - 1 - rows, cols, block_len)
    dims = (((1,), (1,)), ((), ()))

    def mat(table, value):
        return lax.dot_general(
            table, value, dims, precision=lax.Precision.HIGH,
            preferred_element_type=jnp.float32,
        )

    def apply(cos_table, sin_table, real_in, imag_in):
        table = jnp.concatenate([cos_table, sin_table], axis=0)
        from_real = mat(table, real_in)
        from_imag = mat(table, imag_in)
        new_real = from_real[:kept] + from_imag[kept:]
        new_imag = from_imag[:kept] - from_real[kept:]
        return jnp.stack([new_real, new_imag]).reshape(2, kept * devices_tm, columns)

    table = jnp.concatenate([cos_own, sin_own, cos_far, sin_far], axis=0)
    from_real = mat(table, real_part)
    from_imag = mat(table, imag_part)
    own_real = from_real[:kept] + from_imag[kept:2 * kept]
    own_imag = from_imag[:kept] - from_real[kept:2 * kept]
    far_real = from_real[2 * kept:3 * kept] + from_imag[3 * kept:]
    far_imag = from_imag[2 * kept:3 * kept] - from_real[3 * kept:]
    own = jnp.stack([own_real, own_imag]).reshape(2, kept * devices_tm, columns)
    far = jnp.stack([far_real, far_imag])[:, :, ::-1].reshape(2, kept * devices_tm, columns)
    return own, far


def unpack_spectra(own, far, position, samples):
    devices_tm = lax.axis_size("tm")
    shifted = jnp.concatenate([own[:, :1], far[:, :-1]], axis=1)
    outgoing = jnp.where(position == 0, shifted, far)
    pairs = [(src, (devices_tm - src) % devices_tm) for src in range(devices_tm)]
    mirror = lax.ppermute(outgoing, "tm", pairs)
    own_real = own[0]
    own_imag = own[1]
    first_real = (own_real + mirror[0]) * 0.5
    first_imag = (own_imag - mirror[1]) * 0.5
    second_real = (own_imag + mirror[1]) * 0.5
    second_imag = (mirror[0] - own_real) * 0.5
    new_real = jnp.concatenate([first_real, second_real], axis=1) / samples
    new_imag = jnp.concatenate([first_imag, second_imag], axis=1) / samples
    return jnp.stack([new_real.astype(jnp.bfloat16), new_imag.astype(jnp.bfloat16)])


def body(orbit_angles, gap_mask, column_index, lat_coeffs, psd_table):
    devices_tm = lax.axis_size("tm")
    panels = lax.axis_size("panel")
    epochs = orbit_angles.shape[1]
    block_len = epochs // devices_tm
    samples = epochs * devices_tm
    columns = lat_coeffs.shape[2]
    coeffs = lat_coeffs[0]
    keep_rows = gap_mask.astype(jnp.float32)
    packed = jnp.concatenate([orbit_angles, keep_rows[None]], axis=0)
    packed = packed.reshape(3, devices_tm, block_len).transpose(1, 0, 2)
    received, sources = swap_blocks(packed, "tm", True)
    flat_orbit = received.transpose(1, 0, 2).reshape(3, devices_tm * block_len)
    spread = synthesize(flat_orbit[0:2], flat_orbit[2], column_index, coeffs).reshape(
        devices_tm, block_len, columns
    )
    position = lax.axis_index("tm")
    half_cols = columns // 2
    twisted = packed_partials(
        spread[..., :half_cols], spread[..., half_cols:], position, samples, sources
    )
    gathered = lax.all_to_all(twisted, "tm", 0, 0, tiled=True)
    own, far = packed_transform(gathered)
    spectra = unpack_spectra(own, far, position, samples)
    inverse_psd, fold = inverse_weights(
        psd_table[0], position, devices_tm, epochs, samples, spectra.shape[1]
    )
    weighted = (spectra.astype(jnp.float32) * inverse_psd[None, :, None]).astype(jnp.bfloat16)
    weighted = weighted * fold[None, :, None].astype(jnp.bfloat16)
    contract = (((0, 1), (0, 1)), ((), ()))
    products = [
        lax.dot_general(block, weighted, contract, preferred_element_type=jnp.float32)
        for block in panel_spectra(spectra)
    ]
    by_shift = jnp.stack(products)
    panel = lax.axis_index("panel")
    rows = panels * columns // devices_tm
    if devices_tm <= 8 and columns % rows == 0:
        per_panel = columns // rows
        grid = by_shift.reshape(panels, per_panel, rows, columns)

        def block(target):
            start = ((panel - target // per_panel) % panels, target % per_panel, 0, 0)
            return lax.dynamic_slice(grid, start, (1, 1, rows, columns))[0, 0]

        total = block(position)
        for shift in range(1, devices_tm):
            pairs = [(src, (src + shift) % devices_tm) for src in range(devices_tm)]
            total = total + lax.ppermute(block((position + shift) % devices_tm), "tm", pairs)
        return comp_sum(total)
    order = (panel - jnp.arange(panels, dtype=jnp.int32)) % panels
    partial_value = jnp.take(by_shift, order, axis=0).reshape(panels * columns, columns)
    return settle_rows(partial_value)


def settle_rows(partial_value):
    devices_tm = lax.axis_size("tm")
    comps = lax.axis_size("comp")
    rows_total, columns = partial_value.shape
    rows = rows_total // devices_tm
    if comps != 2 or columns % 256 != 0 or devices_tm <= 8:
        return comp_sum(swap_blocks(partial_value.reshape(devices_tm, rows, columns), "tm", False))
    half = columns // 2
    comp = lax.axis_index("comp")
    mine = lax.dynamic_slice_in_dim(partial_value, comp * half, half, axis=1)
    theirs = lax.dynamic_slice_in_dim(partial_value, (1 - comp) * half, half, axis=1)
    summed = mine + lax.ppermute(theirs, "comp", [(0, 1), (1, 0)])
    block = swap_blocks(summed.reshape(devices_tm, rows, half), "tm", False)
    other = lax.ppermute(block, "comp", [(0, 1), (1, 0)])
    first = jnp.where(comp == 0, block, other)
    second = jnp.where(comp == 0, other, block)
    return jnp.concatenate([first, second], axis=1)


def solution(mesh):
    return jax.shard_map(
        body,
        mesh=mesh,
        in_specs=(
            P(None, ("groups", "tm")),
            P(("groups", "tm")),
            P(None, "panel"),
            P("comp", None, "panel"),
            P("comp", None),
        ),
        out_specs=P(("groups", "tm"), "panel"),
        check_vma=False,
    )
```

```python
import math

import jax
import jax.numpy as jnp
from jax import lax
from jax.sharding import PartitionSpec as P

SPLIT = 64


def rounding_error(value, factor, product):
    high = lax.reduce_precision(value, exponent_bits=8, mantissa_bits=11)
    low = value - high
    return (product - high * factor) - low * factor


def colatitude_basis(colatitude, terms):
    wavenumbers = jnp.arange(terms, dtype=jnp.float32)
    theta = colatitude[:, None]
    phases = lax.optimization_barrier(theta * wavenumbers[None, :])
    if terms % 16 != 0:
        return jnp.concatenate([jnp.cos(phases), jnp.sin(phases)], axis=1)
    groups = terms // 16
    coarse = jnp.arange(groups, dtype=jnp.float32) * 16.0
    fine = jnp.arange(16, dtype=jnp.float32)
    phase_a = lax.optimization_barrier(theta * coarse[None, :])
    phase_b = lax.optimization_barrier(theta * fine[None, :])
    count = colatitude.shape[0]
    delta = (
        rounding_error(theta, wavenumbers[None, :], phases).reshape(count, groups, 16)
        - rounding_error(theta, coarse[None, :], phase_a)[:, :, None]
        - rounding_error(theta, fine[None, :], phase_b)[:, None, :]
    )
    cos_a = jnp.cos(phase_a)[:, :, None]
    sin_a = jnp.sin(phase_a)[:, :, None]
    cos_b = jnp.cos(phase_b)[:, None, :]
    sin_b = jnp.sin(phase_b)[:, None, :]
    cos_sum = cos_a * cos_b - sin_a * sin_b
    sin_sum = sin_a * cos_b + cos_a * sin_b
    cos_k = (cos_sum - delta * sin_sum).reshape(count, terms)
    sin_k = (sin_sum + delta * cos_sum).reshape(count, terms)
    return jnp.concatenate([cos_k, sin_k], axis=1)


def synthesize(angles, keep_rows, column_index, coeffs):
    terms_lat = coeffs.shape[0] // 2
    colatitude = angles[0]
    longit = angles[1]
    basis_rows = colatitude_basis(colatitude, terms_lat).astype(jnp.bfloat16)
    degree = column_index[0]
    orders = column_index[1]
    levels = jnp.arange(2 * terms_lat, dtype=jnp.int32) % terms_lat
    allowed = levels[:, None] <= degree[None, :]
    masked = jnp.where(allowed, coeffs, jnp.zeros_like(coeffs))
    latitude = jnp.dot(basis_rows, masked, preferred_element_type=jnp.float32)
    lon_phase = longit[:, None] * jnp.abs(orders).astype(jnp.float32)[None, :]
    lon_wave = jnp.where(orders[None, :] >= 0, jnp.cos(lon_phase), jnp.sin(lon_phase))
    return latitude * lon_wave * keep_rows[:, None]


def phase_tables(row_index, col_index, length):
    product = row_index[:, None] * col_index[None, :] % length
    angle_grid = product.astype(jnp.float32) * (2.0 * math.pi / length)
    return (jnp.cos(angle_grid), jnp.sin(angle_grid))


def dft_tables(length):
    indices = jnp.arange(length, dtype=jnp.int32)
    return phase_tables(indices, indices, length)


def rotate(real_part, imag_part, outer_index, inner_index, length):
    index_grid = outer_index[:, None] * inner_index[None, :] % length
    angle_grid = index_grid.astype(jnp.float32) * (2.0 * math.pi / length)
    cosine = jnp.cos(angle_grid)[:, :, None]
    sine_grid = jnp.sin(angle_grid)[:, :, None]
    return (real_part * cosine + imag_part * sine_grid, imag_part * cosine - real_part * sine_grid)


def precise_dot(left_side, right_side):
    return jnp.dot(
        left_side, right_side, precision=lax.Precision.HIGHEST, preferred_element_type=jnp.float32
    )


def transform(cos_table, sin_table, real_part, imag_part):
    new_real = precise_dot(cos_table, real_part) + precise_dot(sin_table, imag_part)
    new_imag = precise_dot(cos_table, imag_part) - precise_dot(sin_table, real_part)
    return (new_real, new_imag)


def four_step(real_in, imag_in, samples):
    length = real_in.shape[0]
    columns = real_in.shape[1]
    outer_count = SPLIT
    inner_count = length // SPLIT
    real_part = real_in.reshape(outer_count, inner_count * columns)
    imag_part = imag_in.reshape(outer_count, inner_count * columns)
    cos_outer, sin_outer = dft_tables(outer_count)
    real_part, imag_part = transform(cos_outer, sin_outer, real_part, imag_part)
    real_part = real_part.reshape(outer_count, inner_count, columns)
    imag_part = imag_part.reshape(outer_count, inner_count, columns)
    real_part, imag_part = rotate(
        real_part,
        imag_part,
        jnp.arange(outer_count, dtype=jnp.int32),
        jnp.arange(inner_count, dtype=jnp.int32),
        length,
    )
    real_part = jnp.transpose(real_part, (1, 0, 2)).reshape(inner_count, outer_count * columns)
    imag_part = jnp.transpose(imag_part, (1, 0, 2)).reshape(inner_count, outer_count * columns)
    cos_inner, sin_inner = dft_tables(inner_count)
    real_part, imag_part = transform(cos_inner, sin_inner, real_part, imag_part)
    return (
        real_part.reshape(length, columns) / samples,
        imag_part.reshape(length, columns) / samples,
    )


def local_transform(received, samples):
    real_part, imag_part = four_step(received[0, 0], received[1, 0], samples)
    return (real_part.astype(jnp.bfloat16), imag_part.astype(jnp.bfloat16))


def inverse_weights(psd_row, position, devices_tm, epochs, samples, count):
    half = samples // 2
    mirrored = jnp.concatenate([psd_row[: half + 1], psd_row[1:half][::-1]])
    picked = lax.dynamic_slice_in_dim(mirrored.reshape(epochs, devices_tm), position, 1, axis=1)
    inverse = 8192.0 / picked[:count, 0].astype(jnp.float32)
    order = jnp.arange(count, dtype=jnp.int32)
    first = jnp.where(position == 0, 1.0, 2.0)
    middle = jnp.where(position == 0, 1.0, 0.0)
    fold = jnp.where(
        order == 0, first, jnp.where(order < epochs // 2, 2.0, jnp.where(order == epochs // 2, middle, 0.0))
    )
    return inverse, fold


def panel_spectra(spectra):
    panels = lax.axis_size("panel")
    blocks = [spectra]
    for shift in range(1, panels):
        pairs = [(src, (src + shift) % panels) for src in range(panels)]
        blocks.append(lax.ppermute(spectra, "panel", pairs))
    return blocks


def comp_sum(value):
    comps = lax.axis_size("comp")
    if comps == 1:
        return value
    if comps != 2:
        return lax.psum(value, "comp")
    other = lax.ppermute(value, "comp", [(0, 1), (1, 0)])
    return value + other


def class_partials(spread, position, samples):
    devices_tm, block_len, columns = spread.shape
    index = jnp.arange(devices_tm, dtype=jnp.int32)
    cos_table, sin_table = phase_tables(index, index, devices_tm)
    real_part = jnp.sum(cos_table[:, :, None, None] * spread[None], axis=1)
    imag_part = -jnp.sum(sin_table[:, :, None, None] * spread[None], axis=1)
    local_epoch = position * block_len + jnp.arange(block_len, dtype=jnp.int32)
    real_part, imag_part = rotate(real_part, imag_part, index, local_epoch, samples)
    return jnp.stack([real_part, imag_part], axis=1)


def class_spectrum(gathered, samples):
    devices_tm, _, block_len, columns = gathered.shape
    length = devices_tm * block_len
    index = jnp.arange(devices_tm, dtype=jnp.int32)
    cos_table, sin_table = phase_tables(index, index, devices_tm)
    real_in = gathered[:, 0]
    imag_in = gathered[:, 1]
    cos_b = cos_table[:, :, None, None]
    sin_b = sin_table[:, :, None, None]
    real_part = jnp.sum(cos_b * real_in[None] + sin_b * imag_in[None], axis=1)
    imag_part = jnp.sum(cos_b * imag_in[None] - sin_b * real_in[None], axis=1)
    real_part, imag_part = rotate(
        real_part, imag_part, index, jnp.arange(block_len, dtype=jnp.int32), length
    )
    kept = block_len // 2 + 1
    cos_inner, sin_inner = phase_tables(
        jnp.arange(kept, dtype=jnp.int32), jnp.arange(block_len, dtype=jnp.int32), block_len
    )
    dims = (((1,), (1,)), ((), ()))

    def mat(table, value):
        return lax.dot_general(
            table, value, dims, precision=lax.Precision.HIGH,
            preferred_element_type=jnp.float32,
        )

    new_real = mat(cos_inner, real_part) + mat(sin_inner, imag_part)
    new_imag = mat(cos_inner, imag_part) - mat(sin_inner, real_part)
    new_real = (new_real.reshape(kept * devices_tm, columns) / samples).astype(jnp.bfloat16)
    new_imag = (new_imag.reshape(kept * devices_tm, columns) / samples).astype(jnp.bfloat16)
    return jnp.stack([new_real, new_imag])


def swap_blocks(blocks, axis, ordered):
    count = lax.axis_size(axis)
    if count > 8:
        received = lax.all_to_all(blocks, axis, 0, 0, tiled=True)
        if ordered:
            return received, jnp.arange(count, dtype=jnp.int32)
        return jnp.sum(received, axis=0)
    me = lax.axis_index(axis)
    arrived = [lax.dynamic_index_in_dim(blocks, me, 0, keepdims=False)]
    for shift in range(1, count):
        outgoing = lax.dynamic_index_in_dim(blocks, (me + shift) % count, 0, keepdims=False)
        pairs = [(src, (src + shift) % count) for src in range(count)]
        arrived.append(lax.ppermute(outgoing, axis, pairs))
    if not ordered:
        total = arrived[0]
        for part in arrived[1:]:
            total = total + part
        return total
    return jnp.stack(arrived), (me - jnp.arange(count, dtype=jnp.int32)) % count


def packed_partials(real_in, imag_in, position, samples, sources):
    devices_tm, block_len, columns = real_in.shape
    index = jnp.arange(devices_tm, dtype=jnp.int32)
    cos_table, sin_table = phase_tables(index, sources, devices_tm)
    cos_b = cos_table[:, :, None, None]
    sin_b = sin_table[:, :, None, None]
    real_part = jnp.sum(cos_b * real_in[None] + sin_b * imag_in[None], axis=1)
    imag_part = jnp.sum(cos_b * imag_in[None] - sin_b * real_in[None], axis=1)
    local_epoch = position * block_len + jnp.arange(block_len, dtype=jnp.int32)
    real_part, imag_part = rotate(real_part, imag_part, index, local_epoch, samples)
    return jnp.stack([real_part, imag_part], axis=1)


def packed_transform(gathered):
    devices_tm, _, block_len, columns = gathered.shape
    length = devices_tm * block_len
    index = jnp.arange(devices_tm, dtype=jnp.int32)
    cos_table, sin_table = phase_tables(index, index, devices_tm)
    real_in = gathered[:, 0]
    imag_in = gathered[:, 1]
    cos_b = cos_table[:, :, None, None]
    sin_b = sin_table[:, :, None, None]
    real_part = jnp.sum(cos_b * real_in[None] + sin_b * imag_in[None], axis=1)
    imag_part = jnp.sum(cos_b * imag_in[None] - sin_b * real_in[None], axis=1)
    real_part, imag_part = rotate(
        real_part, imag_part, index, jnp.arange(block_len, dtype=jnp.int32), length
    )
    kept = block_len // 2 + 1
    rows = jnp.arange(kept, dtype=jnp.int32)
    cols = jnp.arange(block_len, dtype=jnp.int32)
    cos_own, sin_own = phase_tables(rows, cols, block_len)
    cos_far, sin_far = phase_tables(block_len - 1 - rows, cols, block_len)
    dims = (((1,), (1,)), ((), ()))

    def mat(table, value):
        return lax.dot_general(
            table, value, dims, precision=lax.Precision.HIGH,
            preferred_element_type=jnp.float32,
        )

    def apply(cos_table, sin_table, real_in, imag_in):
        table = jnp.concatenate([cos_table, sin_table], axis=0)
        from_real = mat(table, real_in)
        from_imag = mat(table, imag_in)
        new_real = from_real[:kept] + from_imag[kept:]
        new_imag = from_imag[:kept] - from_real[kept:]
        return jnp.stack([new_real, new_imag]).reshape(2, kept * devices_tm, columns)

    table = jnp.concatenate([cos_own, sin_own, cos_far, sin_far], axis=0)
    from_real = mat(table, real_part)
    from_imag = mat(table, imag_part)
    own_real = from_real[:kept] + from_imag[kept:2 * kept]
    own_imag = from_imag[:kept] - from_real[kept:2 * kept]
    far_real = from_real[2 * kept:3 * kept] + from_imag[3 * kept:]
    far_imag = from_imag[2 * kept:3 * kept] - from_real[3 * kept:]
    own = jnp.stack([own_real, own_imag]).reshape(2, kept * devices_tm, columns)
    far = jnp.stack([far_real, far_imag])[:, :, ::-1].reshape(2, kept * devices_tm, columns)
    return own, far


def unpack_spectra(own, far, position, samples, norm_scale):
    devices_tm = lax.axis_size("tm")
    shifted = jnp.concatenate([own[:, :1], far[:, :-1]], axis=1)
    outgoing = jnp.where(position == 0, shifted, far)
    pairs = [(src, (devices_tm - src) % devices_tm) for src in range(devices_tm)]
    mirror = lax.ppermute(outgoing, "tm", pairs)
    own_real = own[0]
    own_imag = own[1]
    first_real = (own_real + mirror[0]) * 0.5
    first_imag = (own_imag - mirror[1]) * 0.5
    second_real = (own_imag + mirror[1]) * 0.5
    second_imag = (mirror[0] - own_real) * 0.5
    scale = norm_scale[None, :] / samples
    new_real = jnp.concatenate([first_real, second_real], axis=1) * scale
    new_imag = jnp.concatenate([first_imag, second_imag], axis=1) * scale
    return jnp.stack([new_real.astype(jnp.bfloat16), new_imag.astype(jnp.bfloat16)])


def body(orbit_angles, gap_mask, column_index, lat_coeffs, psd_table):
    devices_tm = lax.axis_size("tm")
    panels = lax.axis_size("panel")
    epochs = orbit_angles.shape[1]
    block_len = epochs // devices_tm
    samples = epochs * devices_tm
    columns = lat_coeffs.shape[2]
    coeffs = lat_coeffs[0]
    keep_rows = gap_mask.astype(jnp.float32)
    packed = jnp.concatenate([orbit_angles, keep_rows[None]], axis=0)
    packed = packed.reshape(3, devices_tm, block_len).transpose(1, 0, 2)
    received, sources = swap_blocks(packed, "tm", True)
    flat_orbit = received.transpose(1, 0, 2).reshape(3, devices_tm * block_len)
    spread = synthesize(flat_orbit[0:2], flat_orbit[2], column_index, coeffs).reshape(
        devices_tm, block_len, columns
    )
    position = lax.axis_index("tm")
    half_cols = columns // 2
    twisted = packed_partials(
        spread[..., :half_cols], spread[..., half_cols:], position, samples, sources
    )
    gathered = lax.all_to_all(twisted, "tm", 0, 0, tiled=True)
    own, far = packed_transform(gathered)
    norm_scale = 1.0 / jnp.sqrt(column_index[0].astype(jnp.float32) + 1.0)
    spectra = unpack_spectra(own, far, position, samples, norm_scale)
    inverse_psd, fold = inverse_weights(
        psd_table[0], position, devices_tm, epochs, samples, spectra.shape[1]
    )
    weighted = (spectra.astype(jnp.float32) * inverse_psd[None, :, None]).astype(jnp.bfloat16)
    weighted = weighted * fold[None, :, None].astype(jnp.bfloat16)
    contract = (((0, 1), (0, 1)), ((), ()))
    products = [
        lax.dot_general(block, weighted, contract, preferred_element_type=jnp.float32)
        for block in panel_spectra(spectra)
    ]
    by_shift = jnp.stack(products)
    panel = lax.axis_index("panel")
    rows = panels * columns // devices_tm
    if devices_tm <= 8 and columns % rows == 0:
        per_panel = columns // rows
        grid = by_shift.reshape(panels, per_panel, rows, columns)

        def block(target):
            start = ((panel - target // per_panel) % panels, target % per_panel, 0, 0)
            return lax.dynamic_slice(grid, start, (1, 1, rows, columns))[0, 0]

        total = block(position)
        for shift in range(1, devices_tm):
            pairs = [(src, (src + shift) % devices_tm) for src in range(devices_tm)]
            total = total + lax.ppermute(block((position + shift) % devices_tm), "tm", pairs)
        return comp_sum(total)
    order = (panel - jnp.arange(panels, dtype=jnp.int32)) % panels
    partial_value = jnp.take(by_shift, order, axis=0).reshape(panels * columns, columns)
    return settle_rows(partial_value)


def settle_rows(partial_value):
    devices_tm = lax.axis_size("tm")
    comps = lax.axis_size("comp")
    rows_total, columns = partial_value.shape
    rows = rows_total // devices_tm
    if comps != 2 or columns % 256 != 0 or devices_tm <= 8:
        return comp_sum(swap_blocks(partial_value.reshape(devices_tm, rows, columns), "tm", False))
    half = columns // 2
    comp = lax.axis_index("comp")
    mine = lax.dynamic_slice_in_dim(partial_value, comp * half, half, axis=1)
    theirs = lax.dynamic_slice_in_dim(partial_value, (1 - comp) * half, half, axis=1)
    summed = mine + lax.ppermute(theirs, "comp", [(0, 1), (1, 0)])
    block = swap_blocks(summed.reshape(devices_tm, rows, half), "tm", False)
    other = lax.ppermute(block, "comp", [(0, 1), (1, 0)])
    first = jnp.where(comp == 0, block, other)
    second = jnp.where(comp == 0, other, block)
    return jnp.concatenate([first, second], axis=1)


def solution(mesh):
    return jax.shard_map(
        body,
        mesh=mesh,
        in_specs=(
            P(None, ("groups", "tm")),
            P(("groups", "tm")),
            P(None, "panel"),
            P("comp", None, "panel"),
            P("comp", None),
        ),
        out_specs=P(("groups", "tm"), "panel"),
        check_vma=False,
    )
```

```python
import math

import jax
import jax.numpy as jnp
from jax import lax
from jax.sharding import PartitionSpec as P

SPLIT = 64


def rounding_error(value, factor, product):
    high = lax.reduce_precision(value, exponent_bits=8, mantissa_bits=11)
    low = value - high
    return (product - high * factor) - low * factor


def colatitude_basis(colatitude, terms):
    wavenumbers = jnp.arange(terms, dtype=jnp.float32)
    theta = colatitude[:, None]
    phases = lax.optimization_barrier(theta * wavenumbers[None, :])
    if terms % 16 != 0:
        return jnp.concatenate([jnp.cos(phases), jnp.sin(phases)], axis=1)
    groups = terms // 16
    coarse = jnp.arange(groups, dtype=jnp.float32) * 16.0
    fine = jnp.arange(16, dtype=jnp.float32)
    phase_a = lax.optimization_barrier(theta * coarse[None, :])
    phase_b = lax.optimization_barrier(theta * fine[None, :])
    count = colatitude.shape[0]
    delta = (
        rounding_error(theta, wavenumbers[None, :], phases).reshape(count, groups, 16)
        - rounding_error(theta, coarse[None, :], phase_a)[:, :, None]
        - rounding_error(theta, fine[None, :], phase_b)[:, None, :]
    )
    cos_a = jnp.cos(phase_a)[:, :, None]
    sin_a = jnp.sin(phase_a)[:, :, None]
    cos_b = jnp.cos(phase_b)[:, None, :]
    sin_b = jnp.sin(phase_b)[:, None, :]
    cos_sum = cos_a * cos_b - sin_a * sin_b
    sin_sum = sin_a * cos_b + cos_a * sin_b
    cos_k = (cos_sum - delta * sin_sum).reshape(count, terms)
    sin_k = (sin_sum + delta * cos_sum).reshape(count, terms)
    return jnp.concatenate([cos_k, sin_k], axis=1)


def synthesize(angles, keep_rows, column_index, coeffs):
    terms_lat = coeffs.shape[0] // 2
    colatitude = angles[0]
    longit = angles[1]
    basis_rows = colatitude_basis(colatitude, terms_lat).astype(jnp.bfloat16)
    degree = column_index[0]
    orders = column_index[1]
    levels = jnp.arange(2 * terms_lat, dtype=jnp.int32) % terms_lat
    allowed = levels[:, None] <= degree[None, :]
    masked = jnp.where(allowed, coeffs, jnp.zeros_like(coeffs))
    latitude = jnp.dot(basis_rows, masked, preferred_element_type=jnp.float32)
    lon_phase = longit[:, None] * jnp.abs(orders).astype(jnp.float32)[None, :]
    lon_wave = jnp.where(orders[None, :] >= 0, jnp.cos(lon_phase), jnp.sin(lon_phase))
    return latitude * lon_wave * keep_rows[:, None]


def phase_tables(row_index, col_index, length):
    product = row_index[:, None] * col_index[None, :] % length
    angle_grid = product.astype(jnp.float32) * (2.0 * math.pi / length)
    return (jnp.cos(angle_grid), jnp.sin(angle_grid))


def dft_tables(length):
    indices = jnp.arange(length, dtype=jnp.int32)
    return phase_tables(indices, indices, length)


def rotate(real_part, imag_part, outer_index, inner_index, length):
    index_grid = outer_index[:, None] * inner_index[None, :] % length
    angle_grid = index_grid.astype(jnp.float32) * (2.0 * math.pi / length)
    cosine = jnp.cos(angle_grid)[:, :, None]
    sine_grid = jnp.sin(angle_grid)[:, :, None]
    return (real_part * cosine + imag_part * sine_grid, imag_part * cosine - real_part * sine_grid)


def precise_dot(left_side, right_side):
    return jnp.dot(
        left_side, right_side, precision=lax.Precision.HIGHEST, preferred_element_type=jnp.float32
    )


def transform(cos_table, sin_table, real_part, imag_part):
    new_real = precise_dot(cos_table, real_part) + precise_dot(sin_table, imag_part)
    new_imag = precise_dot(cos_table, imag_part) - precise_dot(sin_table, real_part)
    return (new_real, new_imag)


def four_step(real_in, imag_in, samples):
    length = real_in.shape[0]
    columns = real_in.shape[1]
    outer_count = SPLIT
    inner_count = length // SPLIT
    real_part = real_in.reshape(outer_count, inner_count * columns)
    imag_part = imag_in.reshape(outer_count, inner_count * columns)
    cos_outer, sin_outer = dft_tables(outer_count)
    real_part, imag_part = transform(cos_outer, sin_outer, real_part, imag_part)
    real_part = real_part.reshape(outer_count, inner_count, columns)
    imag_part = imag_part.reshape(outer_count, inner_count, columns)
    real_part, imag_part = rotate(
        real_part,
        imag_part,
        jnp.arange(outer_count, dtype=jnp.int32),
        jnp.arange(inner_count, dtype=jnp.int32),
        length,
    )
    real_part = jnp.transpose(real_part, (1, 0, 2)).reshape(inner_count, outer_count * columns)
    imag_part = jnp.transpose(imag_part, (1, 0, 2)).reshape(inner_count, outer_count * columns)
    cos_inner, sin_inner = dft_tables(inner_count)
    real_part, imag_part = transform(cos_inner, sin_inner, real_part, imag_part)
    return (
        real_part.reshape(length, columns) / samples,
        imag_part.reshape(length, columns) / samples,
    )


def local_transform(received, samples):
    real_part, imag_part = four_step(received[0, 0], received[1, 0], samples)
    return (real_part.astype(jnp.bfloat16), imag_part.astype(jnp.bfloat16))


def inverse_weights(psd_row, position, devices_tm, epochs, samples, count):
    half = samples // 2
    mirrored = jnp.concatenate([psd_row[: half + 1], psd_row[1:half][::-1]])
    picked = lax.dynamic_slice_in_dim(mirrored.reshape(epochs, devices_tm), position, 1, axis=1)
    inverse = 8192.0 / picked[:count, 0].astype(jnp.float32)
    order = jnp.arange(count, dtype=jnp.int32)
    first = jnp.where(position == 0, 1.0, 2.0)
    middle = jnp.where(position == 0, 1.0, 0.0)
    fold = jnp.where(
        order == 0, first, jnp.where(order < epochs // 2, 2.0, jnp.where(order == epochs // 2, middle, 0.0))
    )
    return inverse, fold


def panel_spectra(spectra):
    panels = lax.axis_size("panel")
    blocks = [spectra]
    for shift in range(1, panels):
        pairs = [(src, (src + shift) % panels) for src in range(panels)]
        blocks.append(lax.ppermute(spectra, "panel", pairs))
    return blocks


def comp_sum(value):
    comps = lax.axis_size("comp")
    if comps == 1:
        return value
    if comps != 2:
        return lax.psum(value, "comp")
    other = lax.ppermute(value, "comp", [(0, 1), (1, 0)])
    return value + other


def class_partials(spread, position, samples):
    devices_tm, block_len, columns = spread.shape
    index = jnp.arange(devices_tm, dtype=jnp.int32)
    cos_table, sin_table = phase_tables(index, index, devices_tm)
    real_part = jnp.sum(cos_table[:, :, None, None] * spread[None], axis=1)
    imag_part = -jnp.sum(sin_table[:, :, None, None] * spread[None], axis=1)
    local_epoch = position * block_len + jnp.arange(block_len, dtype=jnp.int32)
    real_part, imag_part = rotate(real_part, imag_part, index, local_epoch, samples)
    return jnp.stack([real_part, imag_part], axis=1)


def class_spectrum(gathered, samples):
    devices_tm, _, block_len, columns = gathered.shape
    length = devices_tm * block_len
    index = jnp.arange(devices_tm, dtype=jnp.int32)
    cos_table, sin_table = phase_tables(index, index, devices_tm)
    real_in = gathered[:, 0]
    imag_in = gathered[:, 1]
    cos_b = cos_table[:, :, None, None]
    sin_b = sin_table[:, :, None, None]
    real_part = jnp.sum(cos_b * real_in[None] + sin_b * imag_in[None], axis=1)
    imag_part = jnp.sum(cos_b * imag_in[None] - sin_b * real_in[None], axis=1)
    real_part, imag_part = rotate(
        real_part, imag_part, index, jnp.arange(block_len, dtype=jnp.int32), length
    )
    kept = block_len // 2 + 1
    cos_inner, sin_inner = phase_tables(
        jnp.arange(kept, dtype=jnp.int32), jnp.arange(block_len, dtype=jnp.int32), block_len
    )
    dims = (((1,), (1,)), ((), ()))

    def mat(table, value):
        return lax.dot_general(
            table, value, dims, precision=lax.Precision.HIGH,
            preferred_element_type=jnp.float32,
        )

    new_real = mat(cos_inner, real_part) + mat(sin_inner, imag_part)
    new_imag = mat(cos_inner, imag_part) - mat(sin_inner, real_part)
    new_real = (new_real.reshape(kept * devices_tm, columns) / samples).astype(jnp.bfloat16)
    new_imag = (new_imag.reshape(kept * devices_tm, columns) / samples).astype(jnp.bfloat16)
    return jnp.stack([new_real, new_imag])


def swap_blocks(blocks, axis, ordered):
    count = lax.axis_size(axis)
    if count > 8:
        received = lax.all_to_all(blocks, axis, 0, 0, tiled=True)
        if ordered:
            return received, jnp.arange(count, dtype=jnp.int32)
        return jnp.sum(received, axis=0)
    me = lax.axis_index(axis)
    arrived = [lax.dynamic_index_in_dim(blocks, me, 0, keepdims=False)]
    for shift in range(1, count):
        outgoing = lax.dynamic_index_in_dim(blocks, (me + shift) % count, 0, keepdims=False)
        pairs = [(src, (src + shift) % count) for src in range(count)]
        arrived.append(lax.ppermute(outgoing, axis, pairs))
    if not ordered:
        total = arrived[0]
        for part in arrived[1:]:
            total = total + part
        return total
    return jnp.stack(arrived), (me - jnp.arange(count, dtype=jnp.int32)) % count


def packed_partials(real_in, imag_in, position, samples, sources):
    devices_tm, block_len, columns = real_in.shape
    index = jnp.arange(devices_tm, dtype=jnp.int32)
    cos_table, sin_table = phase_tables(index, sources, devices_tm)
    cos_b = cos_table[:, :, None, None]
    sin_b = sin_table[:, :, None, None]
    real_part = jnp.sum(cos_b * real_in[None] + sin_b * imag_in[None], axis=1)
    imag_part = jnp.sum(cos_b * imag_in[None] - sin_b * real_in[None], axis=1)
    local_epoch = position * block_len + jnp.arange(block_len, dtype=jnp.int32)
    real_part, imag_part = rotate(real_part, imag_part, index, local_epoch, samples)
    return jnp.concatenate([real_part, imag_part], axis=-1)


def packed_transform(gathered):
    devices_tm, block_len, doubled = gathered.shape
    columns = doubled // 2
    length = devices_tm * block_len
    index = jnp.arange(devices_tm, dtype=jnp.int32)
    cos_table, sin_table = phase_tables(index, index, devices_tm)
    real_in = gathered[..., :columns]
    imag_in = gathered[..., columns:]
    cos_b = cos_table[:, :, None, None]
    sin_b = sin_table[:, :, None, None]
    real_part = jnp.sum(cos_b * real_in[None] + sin_b * imag_in[None], axis=1)
    imag_part = jnp.sum(cos_b * imag_in[None] - sin_b * real_in[None], axis=1)
    real_part, imag_part = rotate(
        real_part, imag_part, index, jnp.arange(block_len, dtype=jnp.int32), length
    )
    kept = block_len // 2 + 1
    rows = jnp.arange(kept, dtype=jnp.int32)
    cols = jnp.arange(block_len, dtype=jnp.int32)
    cos_own, sin_own = phase_tables(rows, cols, block_len)
    cos_far, sin_far = phase_tables(block_len - 1 - rows, cols, block_len)
    dims = (((1,), (1,)), ((), ()))

    def mat(table, value):
        return lax.dot_general(
            table, value, dims, precision=lax.Precision.HIGH,
            preferred_element_type=jnp.float32,
        )

    def apply(cos_table, sin_table, real_in, imag_in):
        table = jnp.concatenate([cos_table, sin_table], axis=0)
        from_real = mat(table, real_in)
        from_imag = mat(table, imag_in)
        new_real = from_real[:kept] + from_imag[kept:]
        new_imag = from_imag[:kept] - from_real[kept:]
        return jnp.stack([new_real, new_imag]).reshape(2, kept * devices_tm, columns)

    table = jnp.concatenate([cos_own, sin_own, cos_far, sin_far], axis=0)
    from_real = mat(table, real_part)
    from_imag = mat(table, imag_part)
    own_real = from_real[:kept] + from_imag[kept:2 * kept]
    own_imag = from_imag[:kept] - from_real[kept:2 * kept]
    far_real = from_real[2 * kept:3 * kept] + from_imag[3 * kept:]
    far_imag = from_imag[2 * kept:3 * kept] - from_real[3 * kept:]
    own = jnp.stack([own_real, own_imag]).reshape(2, kept * devices_tm, columns)
    far = jnp.stack([far_real, far_imag])[:, :, ::-1].reshape(2, kept * devices_tm, columns)
    return own, far


def unpack_spectra(own, far, position, samples, norm_scale):
    devices_tm = lax.axis_size("tm")
    shifted = jnp.concatenate([own[:, :1], far[:, :-1]], axis=1)
    outgoing = jnp.where(position == 0, shifted, far)
    pairs = [(src, (devices_tm - src) % devices_tm) for src in range(devices_tm)]
    mirror = lax.ppermute(outgoing, "tm", pairs)
    own_real = own[0]
    own_imag = own[1]
    first_real = (own_real + mirror[0]) * 0.5
    first_imag = (own_imag - mirror[1]) * 0.5
    second_real = (own_imag + mirror[1]) * 0.5
    second_imag = (mirror[0] - own_real) * 0.5
    scale = norm_scale[None, :] / samples
    new_real = jnp.concatenate([first_real, second_real], axis=1) * scale
    new_imag = jnp.concatenate([first_imag, second_imag], axis=1) * scale
    return jnp.stack([new_real.astype(jnp.bfloat16), new_imag.astype(jnp.bfloat16)])


def body(orbit_angles, gap_mask, column_index, lat_coeffs, psd_table):
    devices_tm = lax.axis_size("tm")
    panels = lax.axis_size("panel")
    epochs = orbit_angles.shape[1]
    block_len = epochs // devices_tm
    samples = epochs * devices_tm
    columns = lat_coeffs.shape[2]
    coeffs = lat_coeffs[0]
    keep_rows = gap_mask.astype(jnp.float32)
    packed = jnp.concatenate([orbit_angles, keep_rows[None]], axis=0)
    packed = packed.reshape(3, devices_tm, block_len).transpose(1, 0, 2)
    received, sources = swap_blocks(packed, "tm", True)
    flat_orbit = received.transpose(1, 0, 2).reshape(3, devices_tm * block_len)
    spread = synthesize(flat_orbit[0:2], flat_orbit[2], column_index, coeffs).reshape(
        devices_tm, block_len, columns
    )
    position = lax.axis_index("tm")
    half_cols = columns // 2
    twisted = packed_partials(
        spread[..., :half_cols], spread[..., half_cols:], position, samples, sources
    )
    gathered = lax.all_to_all(twisted, "tm", 0, 0, tiled=True)
    own, far = packed_transform(gathered)
    norm_scale = 1.0 / jnp.sqrt(column_index[0].astype(jnp.float32) + 1.0)
    spectra = unpack_spectra(own, far, position, samples, norm_scale)
    inverse_psd, fold = inverse_weights(
        psd_table[0], position, devices_tm, epochs, samples, spectra.shape[1]
    )
    weighted = (spectra.astype(jnp.float32) * inverse_psd[None, :, None]).astype(jnp.bfloat16)
    weighted = weighted * fold[None, :, None].astype(jnp.bfloat16)
    contract = (((0, 1), (0, 1)), ((), ()))
    products = [
        lax.dot_general(block, weighted, contract, preferred_element_type=jnp.float32)
        for block in panel_spectra(spectra)
    ]
    by_shift = jnp.stack(products)
    panel = lax.axis_index("panel")
    rows = panels * columns // devices_tm
    if devices_tm <= 8 and columns % rows == 0:
        per_panel = columns // rows
        grid = by_shift.reshape(panels, per_panel, rows, columns)

        def block(target):
            start = ((panel - target // per_panel) % panels, target % per_panel, 0, 0)
            return lax.dynamic_slice(grid, start, (1, 1, rows, columns))[0, 0]

        total = block(position)
        for shift in range(1, devices_tm):
            pairs = [(src, (src + shift) % devices_tm) for src in range(devices_tm)]
            total = total + lax.ppermute(block((position + shift) % devices_tm), "tm", pairs)
        return comp_sum(total)
    order = (panel - jnp.arange(panels, dtype=jnp.int32)) % panels
    partial_value = jnp.take(by_shift, order, axis=0).reshape(panels * columns, columns)
    return settle_rows(partial_value)


def settle_rows(partial_value):
    devices_tm = lax.axis_size("tm")
    comps = lax.axis_size("comp")
    rows_total, columns = partial_value.shape
    rows = rows_total // devices_tm
    if comps != 2 or columns % 256 != 0 or devices_tm <= 8:
        return comp_sum(swap_blocks(partial_value.reshape(devices_tm, rows, columns), "tm", False))
    half = columns // 2
    comp = lax.axis_index("comp")
    mine = lax.dynamic_slice_in_dim(partial_value, comp * half, half, axis=1)
    theirs = lax.dynamic_slice_in_dim(partial_value, (1 - comp) * half, half, axis=1)
    summed = mine + lax.ppermute(theirs, "comp", [(0, 1), (1, 0)])
    block = swap_blocks(summed.reshape(devices_tm, rows, half), "tm", False)
    other = lax.ppermute(block, "comp", [(0, 1), (1, 0)])
    first = jnp.where(comp == 0, block, other)
    second = jnp.where(comp == 0, other, block)
    return jnp.concatenate([first, second], axis=1)


def solution(mesh):
    return jax.shard_map(
        body,
        mesh=mesh,
        in_specs=(
            P(None, ("groups", "tm")),
            P(("groups", "tm")),
            P(None, "panel"),
            P("comp", None, "panel"),
            P("comp", None),
        ),
        out_specs=P(("groups", "tm"), "panel"),
        check_vma=False,
    )
```

```python
import math

import jax
import jax.numpy as jnp
from jax import lax
from jax.sharding import PartitionSpec as P

SPLIT = 64


def rounding_error(value, factor, product):
    high = lax.reduce_precision(value, exponent_bits=8, mantissa_bits=11)
    low = value - high
    return (product - high * factor) - low * factor


def colatitude_basis(colatitude, terms):
    wavenumbers = jnp.arange(terms, dtype=jnp.float32)
    theta = colatitude[:, None]
    phases = lax.optimization_barrier(theta * wavenumbers[None, :])
    if terms % 16 != 0:
        return jnp.concatenate([jnp.cos(phases), jnp.sin(phases)], axis=1)
    groups = terms // 16
    coarse = jnp.arange(groups, dtype=jnp.float32) * 16.0
    fine = jnp.arange(16, dtype=jnp.float32)
    phase_a = lax.optimization_barrier(theta * coarse[None, :])
    phase_b = lax.optimization_barrier(theta * fine[None, :])
    count = colatitude.shape[0]
    delta = (
        rounding_error(theta, wavenumbers[None, :], phases).reshape(count, groups, 16)
        - rounding_error(theta, coarse[None, :], phase_a)[:, :, None]
        - rounding_error(theta, fine[None, :], phase_b)[:, None, :]
    )
    cos_a = jnp.cos(phase_a)[:, :, None]
    sin_a = jnp.sin(phase_a)[:, :, None]
    cos_b = jnp.cos(phase_b)[:, None, :]
    sin_b = jnp.sin(phase_b)[:, None, :]
    cos_sum = cos_a * cos_b - sin_a * sin_b
    sin_sum = sin_a * cos_b + cos_a * sin_b
    cos_k = (cos_sum - delta * sin_sum).reshape(count, terms)
    sin_k = (sin_sum + delta * cos_sum).reshape(count, terms)
    return jnp.concatenate([cos_k, sin_k], axis=1)


def synthesize(angles, keep_rows, column_index, coeffs):
    terms_lat = coeffs.shape[0] // 2
    colatitude = angles[0]
    longit = angles[1]
    basis_rows = colatitude_basis(colatitude, terms_lat).astype(jnp.bfloat16)
    degree = column_index[0]
    orders = column_index[1]
    levels = jnp.arange(2 * terms_lat, dtype=jnp.int32) % terms_lat
    allowed = levels[:, None] <= degree[None, :]
    masked = jnp.where(allowed, coeffs, jnp.zeros_like(coeffs))
    latitude = jnp.dot(basis_rows, masked, preferred_element_type=jnp.float32)
    lon_phase = longit[:, None] * jnp.abs(orders).astype(jnp.float32)[None, :]
    lon_wave = jnp.where(orders[None, :] >= 0, jnp.cos(lon_phase), jnp.sin(lon_phase))
    return latitude * lon_wave * keep_rows[:, None]


def phase_tables(row_index, col_index, length):
    product = row_index[:, None] * col_index[None, :] % length
    angle_grid = product.astype(jnp.float32) * (2.0 * math.pi / length)
    return (jnp.cos(angle_grid), jnp.sin(angle_grid))


def dft_tables(length):
    indices = jnp.arange(length, dtype=jnp.int32)
    return phase_tables(indices, indices, length)


def rotate(real_part, imag_part, outer_index, inner_index, length):
    index_grid = outer_index[:, None] * inner_index[None, :] % length
    angle_grid = index_grid.astype(jnp.float32) * (2.0 * math.pi / length)
    cosine = jnp.cos(angle_grid)[:, :, None]
    sine_grid = jnp.sin(angle_grid)[:, :, None]
    return (real_part * cosine + imag_part * sine_grid, imag_part * cosine - real_part * sine_grid)


def precise_dot(left_side, right_side):
    return jnp.dot(
        left_side, right_side, precision=lax.Precision.HIGHEST, preferred_element_type=jnp.float32
    )


def transform(cos_table, sin_table, real_part, imag_part):
    new_real = precise_dot(cos_table, real_part) + precise_dot(sin_table, imag_part)
    new_imag = precise_dot(cos_table, imag_part) - precise_dot(sin_table, real_part)
    return (new_real, new_imag)


def four_step(real_in, imag_in, samples):
    length = real_in.shape[0]
    columns = real_in.shape[1]
    outer_count = SPLIT
    inner_count = length // SPLIT
    real_part = real_in.reshape(outer_count, inner_count * columns)
    imag_part = imag_in.reshape(outer_count, inner_count * columns)
    cos_outer, sin_outer = dft_tables(outer_count)
    real_part, imag_part = transform(cos_outer, sin_outer, real_part, imag_part)
    real_part = real_part.reshape(outer_count, inner_count, columns)
    imag_part = imag_part.reshape(outer_count, inner_count, columns)
    real_part, imag_part = rotate(
        real_part,
        imag_part,
        jnp.arange(outer_count, dtype=jnp.int32),
        jnp.arange(inner_count, dtype=jnp.int32),
        length,
    )
    real_part = jnp.transpose(real_part, (1, 0, 2)).reshape(inner_count, outer_count * columns)
    imag_part = jnp.transpose(imag_part, (1, 0, 2)).reshape(inner_count, outer_count * columns)
    cos_inner, sin_inner = dft_tables(inner_count)
    real_part, imag_part = transform(cos_inner, sin_inner, real_part, imag_part)
    return (
        real_part.reshape(length, columns) / samples,
        imag_part.reshape(length, columns) / samples,
    )


def local_transform(received, samples):
    real_part, imag_part = four_step(received[0, 0], received[1, 0], samples)
    return (real_part.astype(jnp.bfloat16), imag_part.astype(jnp.bfloat16))


def inverse_weights(psd_row, position, devices_tm, epochs, samples, count):
    half = samples // 2
    mirrored = jnp.concatenate([psd_row[: half + 1], psd_row[1:half][::-1]])
    picked = lax.dynamic_slice_in_dim(mirrored.reshape(epochs, devices_tm), position, 1, axis=1)
    inverse = 8192.0 / picked[:count, 0].astype(jnp.float32)
    order = jnp.arange(count, dtype=jnp.int32)
    first = jnp.where(position == 0, 1.0, 2.0)
    middle = jnp.where(position == 0, 1.0, 0.0)
    fold = jnp.where(
        order == 0, first, jnp.where(order < epochs // 2, 2.0, jnp.where(order == epochs // 2, middle, 0.0))
    )
    return inverse, fold


def panel_spectra(spectra):
    panels = lax.axis_size("panel")
    blocks = [spectra]
    for shift in range(1, panels):
        pairs = [(src, (src + shift) % panels) for src in range(panels)]
        blocks.append(lax.ppermute(spectra, "panel", pairs))
    return blocks


def comp_sum(value):
    comps = lax.axis_size("comp")
    if comps == 1:
        return value
    if comps != 2:
        return lax.psum(value, "comp")
    other = lax.ppermute(value, "comp", [(0, 1), (1, 0)])
    return value + other


def class_partials(spread, position, samples):
    devices_tm, block_len, columns = spread.shape
    index = jnp.arange(devices_tm, dtype=jnp.int32)
    cos_table, sin_table = phase_tables(index, index, devices_tm)
    real_part = jnp.sum(cos_table[:, :, None, None] * spread[None], axis=1)
    imag_part = -jnp.sum(sin_table[:, :, None, None] * spread[None], axis=1)
    local_epoch = position * block_len + jnp.arange(block_len, dtype=jnp.int32)
    real_part, imag_part = rotate(real_part, imag_part, index, local_epoch, samples)
    return jnp.stack([real_part, imag_part], axis=1)


def class_spectrum(gathered, samples):
    devices_tm, _, block_len, columns = gathered.shape
    length = devices_tm * block_len
    index = jnp.arange(devices_tm, dtype=jnp.int32)
    cos_table, sin_table = phase_tables(index, index, devices_tm)
    real_in = gathered[:, 0]
    imag_in = gathered[:, 1]
    cos_b = cos_table[:, :, None, None]
    sin_b = sin_table[:, :, None, None]
    real_part = jnp.sum(cos_b * real_in[None] + sin_b * imag_in[None], axis=1)
    imag_part = jnp.sum(cos_b * imag_in[None] - sin_b * real_in[None], axis=1)
    real_part, imag_part = rotate(
        real_part, imag_part, index, jnp.arange(block_len, dtype=jnp.int32), length
    )
    kept = block_len // 2 + 1
    cos_inner, sin_inner = phase_tables(
        jnp.arange(kept, dtype=jnp.int32), jnp.arange(block_len, dtype=jnp.int32), block_len
    )
    dims = (((1,), (1,)), ((), ()))

    def mat(table, value):
        return lax.dot_general(
            table, value, dims, precision=lax.Precision.HIGH,
            preferred_element_type=jnp.float32,
        )

    new_real = mat(cos_inner, real_part) + mat(sin_inner, imag_part)
    new_imag = mat(cos_inner, imag_part) - mat(sin_inner, real_part)
    new_real = (new_real.reshape(kept * devices_tm, columns) / samples).astype(jnp.bfloat16)
    new_imag = (new_imag.reshape(kept * devices_tm, columns) / samples).astype(jnp.bfloat16)
    return jnp.stack([new_real, new_imag])


def swap_blocks(blocks, axis, ordered):
    count = lax.axis_size(axis)
    if count > 8:
        received = lax.all_to_all(blocks, axis, 0, 0, tiled=True)
        if ordered:
            return received, jnp.arange(count, dtype=jnp.int32)
        return jnp.sum(received, axis=0)
    me = lax.axis_index(axis)
    arrived = [lax.dynamic_index_in_dim(blocks, me, 0, keepdims=False)]
    for shift in range(1, count):
        outgoing = lax.dynamic_index_in_dim(blocks, (me + shift) % count, 0, keepdims=False)
        pairs = [(src, (src + shift) % count) for src in range(count)]
        arrived.append(lax.ppermute(outgoing, axis, pairs))
    if not ordered:
        total = arrived[0]
        for part in arrived[1:]:
            total = total + part
        return total
    return jnp.stack(arrived), (me - jnp.arange(count, dtype=jnp.int32)) % count


def packed_partials(real_in, imag_in, position, samples, sources):
    devices_tm, block_len, columns = real_in.shape
    index = jnp.arange(devices_tm, dtype=jnp.int32)
    cos_table, sin_table = phase_tables(index, sources, devices_tm)
    cos_b = cos_table[:, :, None, None]
    sin_b = sin_table[:, :, None, None]
    real_part = jnp.sum(cos_b * real_in[None] + sin_b * imag_in[None], axis=1)
    imag_part = jnp.sum(cos_b * imag_in[None] - sin_b * real_in[None], axis=1)
    local_epoch = position * block_len + jnp.arange(block_len, dtype=jnp.int32)
    real_part, imag_part = rotate(real_part, imag_part, index, local_epoch, samples)
    return jnp.stack([real_part, imag_part], axis=1)


def packed_transform(gathered):
    devices_tm, _, block_len, columns = gathered.shape
    length = devices_tm * block_len
    index = jnp.arange(devices_tm, dtype=jnp.int32)
    cos_table, sin_table = phase_tables(index, index, devices_tm)
    real_in = gathered[:, 0]
    imag_in = gathered[:, 1]
    cos_b = cos_table[:, :, None, None]
    sin_b = sin_table[:, :, None, None]
    real_part = jnp.sum(cos_b * real_in[None] + sin_b * imag_in[None], axis=1)
    imag_part = jnp.sum(cos_b * imag_in[None] - sin_b * real_in[None], axis=1)
    real_part, imag_part = rotate(
        real_part, imag_part, index, jnp.arange(block_len, dtype=jnp.int32), length
    )
    kept = block_len // 2 + 1
    rows = jnp.arange(kept, dtype=jnp.int32)
    cols = jnp.arange(block_len, dtype=jnp.int32)
    cos_own, sin_own = phase_tables(rows, cols, block_len)
    cos_far, sin_far = phase_tables(block_len - 1 - rows, cols, block_len)
    dims = (((1,), (1,)), ((), ()))

    def mat(table, value):
        return lax.dot_general(
            table, value, dims, precision=lax.Precision.HIGH,
            preferred_element_type=jnp.float32,
        )

    def apply(cos_table, sin_table, real_in, imag_in):
        table = jnp.concatenate([cos_table, sin_table], axis=0)
        from_real = mat(table, real_in)
        from_imag = mat(table, imag_in)
        new_real = from_real[:kept] + from_imag[kept:]
        new_imag = from_imag[:kept] - from_real[kept:]
        return jnp.stack([new_real, new_imag]).reshape(2, kept * devices_tm, columns)

    table = jnp.concatenate([cos_own, sin_own, cos_far, sin_far], axis=0)
    from_real = mat(table, real_part)
    from_imag = mat(table, imag_part)
    own_real = from_real[:kept] + from_imag[kept:2 * kept]
    own_imag = from_imag[:kept] - from_real[kept:2 * kept]
    far_real = from_real[2 * kept:3 * kept] + from_imag[3 * kept:]
    far_imag = from_imag[2 * kept:3 * kept] - from_real[3 * kept:]
    own = jnp.stack([own_real, own_imag]).reshape(2, kept * devices_tm, columns)
    far = jnp.stack([far_real, far_imag])[:, :, ::-1].reshape(2, kept * devices_tm, columns)
    return own, far


def unpack_spectra(own, far, position, samples, norm_scale, start, stop):
    devices_tm = lax.axis_size("tm")
    shifted = jnp.concatenate([own[:, :1], far[:, :-1]], axis=1)
    outgoing = jnp.where(position == 0, shifted, far)
    pairs = [(src, (devices_tm - src) % devices_tm) for src in range(devices_tm)]
    mirror = lax.ppermute(outgoing[:, start:stop], "tm", pairs)
    own_real = own[0, start:stop]
    own_imag = own[1, start:stop]
    first_real = (own_real + mirror[0]) * 0.5
    first_imag = (own_imag - mirror[1]) * 0.5
    second_real = (own_imag + mirror[1]) * 0.5
    second_imag = (mirror[0] - own_real) * 0.5
    scale = norm_scale[None, :] / samples
    new_real = jnp.concatenate([first_real, second_real], axis=1) * scale
    new_imag = jnp.concatenate([first_imag, second_imag], axis=1) * scale
    return jnp.stack([new_real.astype(jnp.bfloat16), new_imag.astype(jnp.bfloat16)])


def body(orbit_angles, gap_mask, column_index, lat_coeffs, psd_table):
    devices_tm = lax.axis_size("tm")
    panels = lax.axis_size("panel")
    epochs = orbit_angles.shape[1]
    block_len = epochs // devices_tm
    samples = epochs * devices_tm
    columns = lat_coeffs.shape[2]
    coeffs = lat_coeffs[0]
    keep_rows = gap_mask.astype(jnp.float32)
    packed = jnp.concatenate([orbit_angles, keep_rows[None]], axis=0)
    packed = packed.reshape(3, devices_tm, block_len).transpose(1, 0, 2)
    received, sources = swap_blocks(packed, "tm", True)
    flat_orbit = received.transpose(1, 0, 2).reshape(3, devices_tm * block_len)
    spread = synthesize(flat_orbit[0:2], flat_orbit[2], column_index, coeffs).reshape(
        devices_tm, block_len, columns
    )
    position = lax.axis_index("tm")
    half_cols = columns // 2
    twisted = packed_partials(
        spread[..., :half_cols], spread[..., half_cols:], position, samples, sources
    )
    gathered = lax.all_to_all(twisted, "tm", 0, 0, tiled=True)
    own, far = packed_transform(gathered)
    norm_scale = 1.0 / jnp.sqrt(column_index[0].astype(jnp.float32) + 1.0)
    count = own.shape[1]
    inverse_psd, fold = inverse_weights(
        psd_table[0], position, devices_tm, epochs, samples, count
    )
    cut = (count // 2) // 16 * 16
    contract = (((0, 1), (0, 1)), ((), ()))
    products = [0.0] * panels
    for start, stop in ((0, cut), (cut, count)):
        spectra = unpack_spectra(own, far, position, samples, norm_scale, start, stop)
        weighted = (
            spectra.astype(jnp.float32) * inverse_psd[None, start:stop, None]
        ).astype(jnp.bfloat16)
        weighted = weighted * fold[None, start:stop, None].astype(jnp.bfloat16)
        for shift, block in enumerate(panel_spectra(spectra)):
            products[shift] = products[shift] + lax.dot_general(
                block, weighted, contract, preferred_element_type=jnp.float32
            )
    by_shift = jnp.stack(products)
    panel = lax.axis_index("panel")
    rows = panels * columns // devices_tm
    if devices_tm <= 8 and columns % rows == 0:
        per_panel = columns // rows
        grid = by_shift.reshape(panels, per_panel, rows, columns)

        def block(target):
            start = ((panel - target // per_panel) % panels, target % per_panel, 0, 0)
            return lax.dynamic_slice(grid, start, (1, 1, rows, columns))[0, 0]

        total = block(position)
        for shift in range(1, devices_tm):
            pairs = [(src, (src + shift) % devices_tm) for src in range(devices_tm)]
            total = total + lax.ppermute(block((position + shift) % devices_tm), "tm", pairs)
        return comp_sum(total)
    order = (panel - jnp.arange(panels, dtype=jnp.int32)) % panels
    partial_value = jnp.take(by_shift, order, axis=0).reshape(panels * columns, columns)
    return settle_rows(partial_value)


def settle_rows(partial_value):
    devices_tm = lax.axis_size("tm")
    comps = lax.axis_size("comp")
    rows_total, columns = partial_value.shape
    rows = rows_total // devices_tm
    if comps != 2 or columns % 256 != 0 or devices_tm <= 8:
        return comp_sum(swap_blocks(partial_value.reshape(devices_tm, rows, columns), "tm", False))
    half = columns // 2
    comp = lax.axis_index("comp")
    mine = lax.dynamic_slice_in_dim(partial_value, comp * half, half, axis=1)
    theirs = lax.dynamic_slice_in_dim(partial_value, (1 - comp) * half, half, axis=1)
    summed = mine + lax.ppermute(theirs, "comp", [(0, 1), (1, 0)])
    block = swap_blocks(summed.reshape(devices_tm, rows, half), "tm", False)
    other = lax.ppermute(block, "comp", [(0, 1), (1, 0)])
    first = jnp.where(comp == 0, block, other)
    second = jnp.where(comp == 0, other, block)
    return jnp.concatenate([first, second], axis=1)


def solution(mesh):
    return jax.shard_map(
        body,
        mesh=mesh,
        in_specs=(
            P(None, ("groups", "tm")),
            P(("groups", "tm")),
            P(None, "panel"),
            P("comp", None, "panel"),
            P("comp", None),
        ),
        out_specs=P(("groups", "tm"), "panel"),
        check_vma=False,
    )
```

```python
import math

import jax
import jax.numpy as jnp
from jax import lax
from jax.sharding import PartitionSpec as P

SPLIT = 64


def rounding_error(value, factor, product):
    high = lax.reduce_precision(value, exponent_bits=8, mantissa_bits=11)
    low = value - high
    return (product - high * factor) - low * factor


def colatitude_basis(colatitude, terms):
    wavenumbers = jnp.arange(terms, dtype=jnp.float32)
    theta = colatitude[:, None]
    phases = lax.optimization_barrier(theta * wavenumbers[None, :])
    if terms % 16 != 0:
        return jnp.concatenate([jnp.cos(phases), jnp.sin(phases)], axis=1)
    groups = terms // 16
    coarse = jnp.arange(groups, dtype=jnp.float32) * 16.0
    fine = jnp.arange(16, dtype=jnp.float32)
    phase_a = lax.optimization_barrier(theta * coarse[None, :])
    phase_b = lax.optimization_barrier(theta * fine[None, :])
    count = colatitude.shape[0]
    delta = (
        rounding_error(theta, wavenumbers[None, :], phases).reshape(count, groups, 16)
        - rounding_error(theta, coarse[None, :], phase_a)[:, :, None]
        - rounding_error(theta, fine[None, :], phase_b)[:, None, :]
    )
    cos_a = jnp.cos(phase_a)[:, :, None]
    sin_a = jnp.sin(phase_a)[:, :, None]
    cos_b = jnp.cos(phase_b)[:, None, :]
    sin_b = jnp.sin(phase_b)[:, None, :]
    cos_sum = cos_a * cos_b - sin_a * sin_b
    sin_sum = sin_a * cos_b + cos_a * sin_b
    cos_k = (cos_sum - delta * sin_sum).reshape(count, terms)
    sin_k = (sin_sum + delta * cos_sum).reshape(count, terms)
    return jnp.concatenate([cos_k, sin_k], axis=1)


def synthesize(angles, keep_rows, column_index, coeffs):
    terms_lat = coeffs.shape[0] // 2
    colatitude = angles[0]
    longit = angles[1]
    basis_rows = colatitude_basis(colatitude, terms_lat).astype(jnp.bfloat16)
    degree = column_index[0]
    orders = column_index[1]
    levels = jnp.arange(2 * terms_lat, dtype=jnp.int32) % terms_lat
    allowed = levels[:, None] <= degree[None, :]
    masked = jnp.where(allowed, coeffs, jnp.zeros_like(coeffs))
    latitude = jnp.dot(basis_rows, masked, preferred_element_type=jnp.float32)
    lon_phase = longit[:, None] * jnp.abs(orders).astype(jnp.float32)[None, :]
    quarter = jnp.where(orders >= 0, 0.0, 0.5 * math.pi).astype(jnp.float32)
    lon_wave = jnp.cos(lon_phase - quarter[None, :])
    return latitude * lon_wave * keep_rows[:, None]


def phase_tables(row_index, col_index, length):
    product = row_index[:, None] * col_index[None, :] % length
    angle_grid = product.astype(jnp.float32) * (2.0 * math.pi / length)
    return (jnp.cos(angle_grid), jnp.sin(angle_grid))


def dft_tables(length):
    indices = jnp.arange(length, dtype=jnp.int32)
    return phase_tables(indices, indices, length)


def rotate(real_part, imag_part, outer_index, inner_index, length):
    index_grid = outer_index[:, None] * inner_index[None, :] % length
    angle_grid = index_grid.astype(jnp.float32) * (2.0 * math.pi / length)
    cosine = jnp.cos(angle_grid)[:, :, None]
    sine_grid = jnp.sin(angle_grid)[:, :, None]
    return (real_part * cosine + imag_part * sine_grid, imag_part * cosine - real_part * sine_grid)


def precise_dot(left_side, right_side):
    return jnp.dot(
        left_side, right_side, precision=lax.Precision.HIGHEST, preferred_element_type=jnp.float32
    )


def transform(cos_table, sin_table, real_part, imag_part):
    new_real = precise_dot(cos_table, real_part) + precise_dot(sin_table, imag_part)
    new_imag = precise_dot(cos_table, imag_part) - precise_dot(sin_table, real_part)
    return (new_real, new_imag)


def four_step(real_in, imag_in, samples):
    length = real_in.shape[0]
    columns = real_in.shape[1]
    outer_count = SPLIT
    inner_count = length // SPLIT
    real_part = real_in.reshape(outer_count, inner_count * columns)
    imag_part = imag_in.reshape(outer_count, inner_count * columns)
    cos_outer, sin_outer = dft_tables(outer_count)
    real_part, imag_part = transform(cos_outer, sin_outer, real_part, imag_part)
    real_part = real_part.reshape(outer_count, inner_count, columns)
    imag_part = imag_part.reshape(outer_count, inner_count, columns)
    real_part, imag_part = rotate(
        real_part,
        imag_part,
        jnp.arange(outer_count, dtype=jnp.int32),
        jnp.arange(inner_count, dtype=jnp.int32),
        length,
    )
    real_part = jnp.transpose(real_part, (1, 0, 2)).reshape(inner_count, outer_count * columns)
    imag_part = jnp.transpose(imag_part, (1, 0, 2)).reshape(inner_count, outer_count * columns)
    cos_inner, sin_inner = dft_tables(inner_count)
    real_part, imag_part = transform(cos_inner, sin_inner, real_part, imag_part)
    return (
        real_part.reshape(length, columns) / samples,
        imag_part.reshape(length, columns) / samples,
    )


def local_transform(received, samples):
    real_part, imag_part = four_step(received[0, 0], received[1, 0], samples)
    return (real_part.astype(jnp.bfloat16), imag_part.astype(jnp.bfloat16))


def inverse_weights(psd_row, position, devices_tm, epochs, samples, count):
    half = samples // 2
    mirrored = jnp.concatenate([psd_row[: half + 1], psd_row[1:half][::-1]])
    picked = lax.dynamic_slice_in_dim(mirrored.reshape(epochs, devices_tm), position, 1, axis=1)
    inverse = 8192.0 / picked[:count, 0].astype(jnp.float32)
    order = jnp.arange(count, dtype=jnp.int32)
    first = jnp.where(position == 0, 1.0, 2.0)
    middle = jnp.where(position == 0, 1.0, 0.0)
    fold = jnp.where(
        order == 0, first, jnp.where(order < epochs // 2, 2.0, jnp.where(order == epochs // 2, middle, 0.0))
    )
    return inverse, fold


def panel_spectra(spectra):
    panels = lax.axis_size("panel")
    blocks = [spectra]
    for shift in range(1, panels):
        pairs = [(src, (src + shift) % panels) for src in range(panels)]
        blocks.append(lax.ppermute(spectra, "panel", pairs))
    return blocks


def comp_sum(value):
    comps = lax.axis_size("comp")
    if comps == 1:
        return value
    if comps != 2:
        return lax.psum(value, "comp")
    other = lax.ppermute(value, "comp", [(0, 1), (1, 0)])
    return value + other


def class_partials(spread, position, samples):
    devices_tm, block_len, columns = spread.shape
    index = jnp.arange(devices_tm, dtype=jnp.int32)
    cos_table, sin_table = phase_tables(index, index, devices_tm)
    real_part = jnp.sum(cos_table[:, :, None, None] * spread[None], axis=1)
    imag_part = -jnp.sum(sin_table[:, :, None, None] * spread[None], axis=1)
    local_epoch = position * block_len + jnp.arange(block_len, dtype=jnp.int32)
    real_part, imag_part = rotate(real_part, imag_part, index, local_epoch, samples)
    return jnp.stack([real_part, imag_part], axis=1)


def class_spectrum(gathered, samples):
    devices_tm, _, block_len, columns = gathered.shape
    length = devices_tm * block_len
    index = jnp.arange(devices_tm, dtype=jnp.int32)
    cos_table, sin_table = phase_tables(index, index, devices_tm)
    real_in = gathered[:, 0]
    imag_in = gathered[:, 1]
    cos_b = cos_table[:, :, None, None]
    sin_b = sin_table[:, :, None, None]
    real_part = jnp.sum(cos_b * real_in[None] + sin_b * imag_in[None], axis=1)
    imag_part = jnp.sum(cos_b * imag_in[None] - sin_b * real_in[None], axis=1)
    real_part, imag_part = rotate(
        real_part, imag_part, index, jnp.arange(block_len, dtype=jnp.int32), length
    )
    kept = block_len // 2 + 1
    cos_inner, sin_inner = phase_tables(
        jnp.arange(kept, dtype=jnp.int32), jnp.arange(block_len, dtype=jnp.int32), block_len
    )
    dims = (((1,), (1,)), ((), ()))

    def mat(table, value):
        return lax.dot_general(
            table, value, dims, precision=lax.Precision.HIGH,
            preferred_element_type=jnp.float32,
        )

    new_real = mat(cos_inner, real_part) + mat(sin_inner, imag_part)
    new_imag = mat(cos_inner, imag_part) - mat(sin_inner, real_part)
    new_real = (new_real.reshape(kept * devices_tm, columns) / samples).astype(jnp.bfloat16)
    new_imag = (new_imag.reshape(kept * devices_tm, columns) / samples).astype(jnp.bfloat16)
    return jnp.stack([new_real, new_imag])


def swap_blocks(blocks, axis, ordered):
    count = lax.axis_size(axis)
    if count > 8:
        received = lax.all_to_all(blocks, axis, 0, 0, tiled=True)
        if ordered:
            return received, jnp.arange(count, dtype=jnp.int32)
        return jnp.sum(received, axis=0)
    me = lax.axis_index(axis)
    arrived = [lax.dynamic_index_in_dim(blocks, me, 0, keepdims=False)]
    for shift in range(1, count):
        outgoing = lax.dynamic_index_in_dim(blocks, (me + shift) % count, 0, keepdims=False)
        pairs = [(src, (src + shift) % count) for src in range(count)]
        arrived.append(lax.ppermute(outgoing, axis, pairs))
    if not ordered:
        total = arrived[0]
        for part in arrived[1:]:
            total = total + part
        return total
    return jnp.stack(arrived), (me - jnp.arange(count, dtype=jnp.int32)) % count


def packed_partials(real_in, imag_in, position, samples, sources):
    devices_tm, block_len, columns = real_in.shape
    index = jnp.arange(devices_tm, dtype=jnp.int32)
    cos_table, sin_table = phase_tables(index, sources, devices_tm)
    cos_b = cos_table[:, :, None, None]
    sin_b = sin_table[:, :, None, None]
    real_part = jnp.sum(cos_b * real_in[None] + sin_b * imag_in[None], axis=1)
    imag_part = jnp.sum(cos_b * imag_in[None] - sin_b * real_in[None], axis=1)
    local_epoch = position * block_len + jnp.arange(block_len, dtype=jnp.int32)
    real_part, imag_part = rotate(real_part, imag_part, index, local_epoch, samples)
    return jnp.stack([real_part, imag_part], axis=1)


def packed_transform(gathered):
    devices_tm, _, block_len, columns = gathered.shape
    length = devices_tm * block_len
    index = jnp.arange(devices_tm, dtype=jnp.int32)
    cos_table, sin_table = phase_tables(index, index, devices_tm)
    real_in = gathered[:, 0]
    imag_in = gathered[:, 1]
    cos_b = cos_table[:, :, None, None]
    sin_b = sin_table[:, :, None, None]
    real_part = jnp.sum(cos_b * real_in[None] + sin_b * imag_in[None], axis=1)
    imag_part = jnp.sum(cos_b * imag_in[None] - sin_b * real_in[None], axis=1)
    real_part, imag_part = rotate(
        real_part, imag_part, index, jnp.arange(block_len, dtype=jnp.int32), length
    )
    kept = block_len // 2 + 1
    rows = jnp.arange(kept, dtype=jnp.int32)
    cols = jnp.arange(block_len, dtype=jnp.int32)
    cos_own, sin_own = phase_tables(rows, cols, block_len)
    cos_far, sin_far = phase_tables(block_len - 1 - rows, cols, block_len)
    dims = (((1,), (1,)), ((), ()))

    def mat(table, value):
        return lax.dot_general(
            table, value, dims, precision=lax.Precision.HIGH,
            preferred_element_type=jnp.float32,
        )

    def apply(cos_table, sin_table, real_in, imag_in):
        table = jnp.concatenate([cos_table, sin_table], axis=0)
        from_real = mat(table, real_in)
        from_imag = mat(table, imag_in)
        new_real = from_real[:kept] + from_imag[kept:]
        new_imag = from_imag[:kept] - from_real[kept:]
        return jnp.stack([new_real, new_imag]).reshape(2, kept * devices_tm, columns)

    table = jnp.concatenate([cos_own, sin_own, cos_far, sin_far], axis=0)
    from_real = mat(table, real_part)
    from_imag = mat(table, imag_part)
    own_real = from_real[:kept] + from_imag[kept:2 * kept]
    own_imag = from_imag[:kept] - from_real[kept:2 * kept]
    far_real = from_real[2 * kept:3 * kept] + from_imag[3 * kept:]
    far_imag = from_imag[2 * kept:3 * kept] - from_real[3 * kept:]
    own = jnp.stack([own_real, own_imag]).reshape(2, kept * devices_tm, columns)
    far = jnp.stack([far_real, far_imag])[:, :, ::-1].reshape(2, kept * devices_tm, columns)
    return own, far


def unpack_spectra(own, far, position, samples, norm_scale):
    devices_tm = lax.axis_size("tm")
    shifted = jnp.concatenate([own[:, :1], far[:, :-1]], axis=1)
    outgoing = jnp.where(position == 0, shifted, far)
    pairs = [(src, (devices_tm - src) % devices_tm) for src in range(devices_tm)]
    mirror = lax.ppermute(outgoing, "tm", pairs)
    own_real = own[0]
    own_imag = own[1]
    first_real = (own_real + mirror[0]) * 0.5
    first_imag = (own_imag - mirror[1]) * 0.5
    second_real = (own_imag + mirror[1]) * 0.5
    second_imag = (mirror[0] - own_real) * 0.5
    scale = norm_scale[None, :] / samples
    new_real = jnp.concatenate([first_real, second_real], axis=1) * scale
    new_imag = jnp.concatenate([first_imag, second_imag], axis=1) * scale
    return jnp.stack([new_real.astype(jnp.bfloat16), new_imag.astype(jnp.bfloat16)])


def body(orbit_angles, gap_mask, column_index, lat_coeffs, psd_table):
    devices_tm = lax.axis_size("tm")
    panels = lax.axis_size("panel")
    epochs = orbit_angles.shape[1]
    block_len = epochs // devices_tm
    samples = epochs * devices_tm
    columns = lat_coeffs.shape[2]
    coeffs = lat_coeffs[0]
    keep_rows = gap_mask.astype(jnp.float32)
    packed = jnp.concatenate([orbit_angles, keep_rows[None]], axis=0)
    packed = packed.reshape(3, devices_tm, block_len).transpose(1, 0, 2)
    received, sources = swap_blocks(packed, "tm", True)
    flat_orbit = received.transpose(1, 0, 2).reshape(3, devices_tm * block_len)
    spread = synthesize(flat_orbit[0:2], flat_orbit[2], column_index, coeffs).reshape(
        devices_tm, block_len, columns
    )
    position = lax.axis_index("tm")
    half_cols = columns // 2
    twisted = packed_partials(
        spread[..., :half_cols], spread[..., half_cols:], position, samples, sources
    )
    gathered = lax.all_to_all(twisted, "tm", 0, 0, tiled=True)
    own, far = packed_transform(gathered)
    norm_scale = 1.0 / jnp.sqrt(column_index[0].astype(jnp.float32) + 1.0)
    spectra = unpack_spectra(own, far, position, samples, norm_scale)
    inverse_psd, fold = inverse_weights(
        psd_table[0], position, devices_tm, epochs, samples, spectra.shape[1]
    )
    weighted = (spectra.astype(jnp.float32) * inverse_psd[None, :, None]).astype(jnp.bfloat16)
    weighted = weighted * fold[None, :, None].astype(jnp.bfloat16)
    contract = (((0, 1), (0, 1)), ((), ()))
    products = [
        lax.dot_general(block, weighted, contract, preferred_element_type=jnp.float32)
        for block in panel_spectra(spectra)
    ]
    by_shift = jnp.stack(products)
    panel = lax.axis_index("panel")
    rows = panels * columns // devices_tm
    if devices_tm <= 8 and columns % rows == 0:
        per_panel = columns // rows
        grid = by_shift.reshape(panels, per_panel, rows, columns)

        def block(target):
            start = ((panel - target // per_panel) % panels, target % per_panel, 0, 0)
            return lax.dynamic_slice(grid, start, (1, 1, rows, columns))[0, 0]

        total = block(position)
        for shift in range(1, devices_tm):
            pairs = [(src, (src + shift) % devices_tm) for src in range(devices_tm)]
            total = total + lax.ppermute(block((position + shift) % devices_tm), "tm", pairs)
        return comp_sum(total)
    order = (panel - jnp.arange(panels, dtype=jnp.int32)) % panels
    partial_value = jnp.take(by_shift, order, axis=0).reshape(panels * columns, columns)
    return settle_rows(partial_value)


def settle_rows(partial_value):
    devices_tm = lax.axis_size("tm")
    comps = lax.axis_size("comp")
    rows_total, columns = partial_value.shape
    rows = rows_total // devices_tm
    if comps != 2 or columns % 256 != 0 or devices_tm <= 8:
        return comp_sum(swap_blocks(partial_value.reshape(devices_tm, rows, columns), "tm", False))
    half = columns // 2
    comp = lax.axis_index("comp")
    mine = lax.dynamic_slice_in_dim(partial_value, comp * half, half, axis=1)
    theirs = lax.dynamic_slice_in_dim(partial_value, (1 - comp) * half, half, axis=1)
    summed = mine + lax.ppermute(theirs, "comp", [(0, 1), (1, 0)])
    block = swap_blocks(summed.reshape(devices_tm, rows, half), "tm", False)
    other = lax.ppermute(block, "comp", [(0, 1), (1, 0)])
    first = jnp.where(comp == 0, block, other)
    second = jnp.where(comp == 0, other, block)
    return jnp.concatenate([first, second], axis=1)


def solution(mesh):
    return jax.shard_map(
        body,
        mesh=mesh,
        in_specs=(
            P(None, ("groups", "tm")),
            P(("groups", "tm")),
            P(None, "panel"),
            P("comp", None, "panel"),
            P("comp", None),
        ),
        out_specs=P(("groups", "tm"), "panel"),
        check_vma=False,
    )
```

```python
import math

import jax
import jax.numpy as jnp
from jax import lax
from jax.sharding import PartitionSpec as P

SPLIT = 64


def rounding_error(value, factor, product):
    high = lax.reduce_precision(value, exponent_bits=8, mantissa_bits=11)
    low = value - high
    return (product - high * factor) - low * factor


def colatitude_basis(colatitude, terms):
    wavenumbers = jnp.arange(terms, dtype=jnp.float32)
    theta = colatitude[:, None]
    phases = lax.optimization_barrier(theta * wavenumbers[None, :])
    if terms % 16 != 0:
        return jnp.concatenate([jnp.cos(phases), jnp.sin(phases)], axis=1)
    groups = terms // 16
    coarse = jnp.arange(groups, dtype=jnp.float32) * 16.0
    fine = jnp.arange(16, dtype=jnp.float32)
    phase_a = lax.optimization_barrier(theta * coarse[None, :])
    phase_b = lax.optimization_barrier(theta * fine[None, :])
    count = colatitude.shape[0]
    delta = (
        rounding_error(theta, wavenumbers[None, :], phases).reshape(count, groups, 16)
        - rounding_error(theta, coarse[None, :], phase_a)[:, :, None]
        - rounding_error(theta, fine[None, :], phase_b)[:, None, :]
    )
    cos_a = jnp.cos(phase_a)[:, :, None]
    sin_a = jnp.sin(phase_a)[:, :, None]
    cos_b = jnp.cos(phase_b)[:, None, :]
    sin_b = jnp.sin(phase_b)[:, None, :]
    cos_sum = cos_a * cos_b - sin_a * sin_b
    sin_sum = sin_a * cos_b + cos_a * sin_b
    cos_k = (cos_sum - delta * sin_sum).reshape(count, terms)
    sin_k = (sin_sum + delta * cos_sum).reshape(count, terms)
    return jnp.concatenate([cos_k, sin_k], axis=1)


def synthesize(angles, keep_rows, column_index, coeffs):
    terms_lat = coeffs.shape[0] // 2
    colatitude = angles[0]
    longit = angles[1]
    basis_rows = colatitude_basis(colatitude, terms_lat).astype(jnp.bfloat16)
    degree = column_index[0]
    orders = column_index[1]
    levels = jnp.arange(2 * terms_lat, dtype=jnp.int32) % terms_lat
    allowed = levels[:, None] <= degree[None, :]
    masked = jnp.where(allowed, coeffs, jnp.zeros_like(coeffs))
    latitude = jnp.dot(basis_rows, masked, preferred_element_type=jnp.float32)
    lon_phase = longit[:, None] * jnp.abs(orders).astype(jnp.float32)[None, :]
    quarter = jnp.where(orders >= 0, 0.0, 0.5 * math.pi).astype(jnp.float32)
    lon_wave = jnp.cos(lon_phase - quarter[None, :])
    return latitude * lon_wave * keep_rows[:, None]


def phase_tables(row_index, col_index, length):
    product = row_index[:, None] * col_index[None, :] % length
    angle_grid = product.astype(jnp.float32) * (2.0 * math.pi / length)
    return (jnp.cos(angle_grid), jnp.sin(angle_grid))


def dft_tables(length):
    indices = jnp.arange(length, dtype=jnp.int32)
    return phase_tables(indices, indices, length)


def rotate(real_part, imag_part, outer_index, inner_index, length):
    index_grid = outer_index[:, None] * inner_index[None, :] % length
    angle_grid = index_grid.astype(jnp.float32) * (2.0 * math.pi / length)
    cosine = jnp.cos(angle_grid)[:, :, None]
    sine_grid = jnp.sin(angle_grid)[:, :, None]
    return (real_part * cosine + imag_part * sine_grid, imag_part * cosine - real_part * sine_grid)


def precise_dot(left_side, right_side):
    return jnp.dot(
        left_side, right_side, precision=lax.Precision.HIGHEST, preferred_element_type=jnp.float32
    )


def transform(cos_table, sin_table, real_part, imag_part):
    new_real = precise_dot(cos_table, real_part) + precise_dot(sin_table, imag_part)
    new_imag = precise_dot(cos_table, imag_part) - precise_dot(sin_table, real_part)
    return (new_real, new_imag)


def four_step(real_in, imag_in, samples):
    length = real_in.shape[0]
    columns = real_in.shape[1]
    outer_count = SPLIT
    inner_count = length // SPLIT
    real_part = real_in.reshape(outer_count, inner_count * columns)
    imag_part = imag_in.reshape(outer_count, inner_count * columns)
    cos_outer, sin_outer = dft_tables(outer_count)
    real_part, imag_part = transform(cos_outer, sin_outer, real_part, imag_part)
    real_part = real_part.reshape(outer_count, inner_count, columns)
    imag_part = imag_part.reshape(outer_count, inner_count, columns)
    real_part, imag_part = rotate(
        real_part,
        imag_part,
        jnp.arange(outer_count, dtype=jnp.int32),
        jnp.arange(inner_count, dtype=jnp.int32),
        length,
    )
    real_part = jnp.transpose(real_part, (1, 0, 2)).reshape(inner_count, outer_count * columns)
    imag_part = jnp.transpose(imag_part, (1, 0, 2)).reshape(inner_count, outer_count * columns)
    cos_inner, sin_inner = dft_tables(inner_count)
    real_part, imag_part = transform(cos_inner, sin_inner, real_part, imag_part)
    return (
        real_part.reshape(length, columns) / samples,
        imag_part.reshape(length, columns) / samples,
    )


def local_transform(received, samples):
    real_part, imag_part = four_step(received[0, 0], received[1, 0], samples)
    return (real_part.astype(jnp.bfloat16), imag_part.astype(jnp.bfloat16))


def inverse_weights(psd_row, position, devices_tm, epochs, samples, count):
    half = samples // 2
    mirrored = jnp.concatenate([psd_row[: half + 1], psd_row[1:half][::-1]])
    picked = lax.dynamic_slice_in_dim(mirrored.reshape(epochs, devices_tm), position, 1, axis=1)
    inverse = 8192.0 / picked[:count, 0].astype(jnp.float32)
    order = jnp.arange(count, dtype=jnp.int32)
    first = jnp.where(position == 0, 1.0, 2.0)
    middle = jnp.where(position == 0, 1.0, 0.0)
    fold = jnp.where(
        order == 0, first, jnp.where(order < epochs // 2, 2.0, jnp.where(order == epochs // 2, middle, 0.0))
    )
    return inverse, fold


def panel_spectra(spectra):
    panels = lax.axis_size("panel")
    blocks = [spectra]
    for shift in range(1, panels):
        pairs = [(src, (src + shift) % panels) for src in range(panels)]
        blocks.append(lax.ppermute(spectra, "panel", pairs))
    return blocks


def comp_sum(value):
    comps = lax.axis_size("comp")
    if comps == 1:
        return value
    if comps != 2:
        return lax.psum(value, "comp")
    other = lax.ppermute(value, "comp", [(0, 1), (1, 0)])
    return value + other


def class_partials(spread, position, samples):
    devices_tm, block_len, columns = spread.shape
    index = jnp.arange(devices_tm, dtype=jnp.int32)
    cos_table, sin_table = phase_tables(index, index, devices_tm)
    real_part = jnp.sum(cos_table[:, :, None, None] * spread[None], axis=1)
    imag_part = -jnp.sum(sin_table[:, :, None, None] * spread[None], axis=1)
    local_epoch = position * block_len + jnp.arange(block_len, dtype=jnp.int32)
    real_part, imag_part = rotate(real_part, imag_part, index, local_epoch, samples)
    return jnp.stack([real_part, imag_part], axis=1)


def class_spectrum(gathered, samples):
    devices_tm, _, block_len, columns = gathered.shape
    length = devices_tm * block_len
    index = jnp.arange(devices_tm, dtype=jnp.int32)
    cos_table, sin_table = phase_tables(index, index, devices_tm)
    real_in = gathered[:, 0]
    imag_in = gathered[:, 1]
    cos_b = cos_table[:, :, None, None]
    sin_b = sin_table[:, :, None, None]
    real_part = jnp.sum(cos_b * real_in[None] + sin_b * imag_in[None], axis=1)
    imag_part = jnp.sum(cos_b * imag_in[None] - sin_b * real_in[None], axis=1)
    real_part, imag_part = rotate(
        real_part, imag_part, index, jnp.arange(block_len, dtype=jnp.int32), length
    )
    kept = block_len // 2 + 1
    cos_inner, sin_inner = phase_tables(
        jnp.arange(kept, dtype=jnp.int32), jnp.arange(block_len, dtype=jnp.int32), block_len
    )
    dims = (((1,), (1,)), ((), ()))

    def mat(table, value):
        return lax.dot_general(
            table, value, dims, precision=lax.Precision.HIGH,
            preferred_element_type=jnp.float32,
        )

    new_real = mat(cos_inner, real_part) + mat(sin_inner, imag_part)
    new_imag = mat(cos_inner, imag_part) - mat(sin_inner, real_part)
    new_real = (new_real.reshape(kept * devices_tm, columns) / samples).astype(jnp.bfloat16)
    new_imag = (new_imag.reshape(kept * devices_tm, columns) / samples).astype(jnp.bfloat16)
    return jnp.stack([new_real, new_imag])


def swap_blocks(blocks, axis, ordered):
    count = lax.axis_size(axis)
    if count > 8:
        received = lax.all_to_all(blocks, axis, 0, 0, tiled=True)
        if ordered:
            return received, jnp.arange(count, dtype=jnp.int32)
        return jnp.sum(received, axis=0)
    me = lax.axis_index(axis)
    arrived = [lax.dynamic_index_in_dim(blocks, me, 0, keepdims=False)]
    for shift in range(1, count):
        outgoing = lax.dynamic_index_in_dim(blocks, (me + shift) % count, 0, keepdims=False)
        pairs = [(src, (src + shift) % count) for src in range(count)]
        arrived.append(lax.ppermute(outgoing, axis, pairs))
    if not ordered:
        total = arrived[0]
        for part in arrived[1:]:
            total = total + part
        return total
    return jnp.stack(arrived), (me - jnp.arange(count, dtype=jnp.int32)) % count


def packed_partials(real_in, imag_in, position, samples, sources):
    devices_tm, block_len, columns = real_in.shape
    index = jnp.arange(devices_tm, dtype=jnp.int32)
    cos_table, sin_table = phase_tables(index, sources, devices_tm)
    cos_b = cos_table[:, :, None, None]
    sin_b = sin_table[:, :, None, None]
    real_part = jnp.sum(cos_b * real_in[None] + sin_b * imag_in[None], axis=1)
    imag_part = jnp.sum(cos_b * imag_in[None] - sin_b * real_in[None], axis=1)
    local_epoch = position * block_len + jnp.arange(block_len, dtype=jnp.int32)
    real_part, imag_part = rotate(real_part, imag_part, index, local_epoch, samples)
    return jnp.concatenate([real_part, imag_part], axis=-1)


def packed_transform(gathered):
    devices_tm, block_len, doubled = gathered.shape
    columns = doubled // 2
    length = devices_tm * block_len
    index = jnp.arange(devices_tm, dtype=jnp.int32)
    cos_table, sin_table = phase_tables(index, index, devices_tm)
    real_in = gathered[..., :columns]
    imag_in = gathered[..., columns:]
    cos_b = cos_table[:, :, None, None]
    sin_b = sin_table[:, :, None, None]
    real_part = jnp.sum(cos_b * real_in[None] + sin_b * imag_in[None], axis=1)
    imag_part = jnp.sum(cos_b * imag_in[None] - sin_b * real_in[None], axis=1)
    real_part, imag_part = rotate(
        real_part, imag_part, index, jnp.arange(block_len, dtype=jnp.int32), length
    )
    kept = block_len // 2 + 1
    rows = jnp.arange(kept, dtype=jnp.int32)
    cols = jnp.arange(block_len, dtype=jnp.int32)
    cos_own, sin_own = phase_tables(rows, cols, block_len)
    cos_far, sin_far = phase_tables(block_len - 1 - rows, cols, block_len)
    dims = (((1,), (1,)), ((), ()))

    def mat(table, value):
        return lax.dot_general(
            table, value, dims, precision=lax.Precision.HIGH,
            preferred_element_type=jnp.float32,
        )

    def apply(cos_table, sin_table, real_in, imag_in):
        table = jnp.concatenate([cos_table, sin_table], axis=0)
        from_real = mat(table, real_in)
        from_imag = mat(table, imag_in)
        new_real = from_real[:kept] + from_imag[kept:]
        new_imag = from_imag[:kept] - from_real[kept:]
        return jnp.stack([new_real, new_imag]).reshape(2, kept * devices_tm, columns)

    table = jnp.concatenate([cos_own, sin_own, cos_far, sin_far], axis=0)
    from_real = mat(table, real_part)
    from_imag = mat(table, imag_part)
    own_real = from_real[:kept] + from_imag[kept:2 * kept]
    own_imag = from_imag[:kept] - from_real[kept:2 * kept]
    far_real = from_real[2 * kept:3 * kept] + from_imag[3 * kept:]
    far_imag = from_imag[2 * kept:3 * kept] - from_real[3 * kept:]
    own = jnp.stack([own_real, own_imag]).reshape(2, kept * devices_tm, columns)
    far = jnp.stack([far_real, far_imag])[:, :, ::-1].reshape(2, kept * devices_tm, columns)
    return own, far


def unpack_spectra(own, far, position, samples, norm_scale):
    devices_tm = lax.axis_size("tm")
    shifted = jnp.concatenate([own[:, :1], far[:, :-1]], axis=1)
    outgoing = jnp.where(position == 0, shifted, far)
    pairs = [(src, (devices_tm - src) % devices_tm) for src in range(devices_tm)]
    mirror = lax.ppermute(outgoing, "tm", pairs)
    own_real = own[0]
    own_imag = own[1]
    first_real = (own_real + mirror[0]) * 0.5
    first_imag = (own_imag - mirror[1]) * 0.5
    second_real = (own_imag + mirror[1]) * 0.5
    second_imag = (mirror[0] - own_real) * 0.5
    scale = norm_scale[None, :] / samples
    new_real = jnp.concatenate([first_real, second_real], axis=1) * scale
    new_imag = jnp.concatenate([first_imag, second_imag], axis=1) * scale
    return jnp.stack([new_real.astype(jnp.bfloat16), new_imag.astype(jnp.bfloat16)])


def body(orbit_angles, gap_mask, column_index, lat_coeffs, psd_table):
    devices_tm = lax.axis_size("tm")
    panels = lax.axis_size("panel")
    epochs = orbit_angles.shape[1]
    block_len = epochs // devices_tm
    samples = epochs * devices_tm
    columns = lat_coeffs.shape[2]
    coeffs = lat_coeffs[0]
    keep_rows = gap_mask.astype(jnp.float32)
    packed = jnp.concatenate([orbit_angles, keep_rows[None]], axis=0)
    packed = packed.reshape(3, devices_tm, block_len).transpose(1, 0, 2)
    received, sources = swap_blocks(packed, "tm", True)
    flat_orbit = received.transpose(1, 0, 2).reshape(3, devices_tm * block_len)
    spread = synthesize(flat_orbit[0:2], flat_orbit[2], column_index, coeffs).reshape(
        devices_tm, block_len, columns
    )
    position = lax.axis_index("tm")
    half_cols = columns // 2
    twisted = packed_partials(
        spread[..., :half_cols], spread[..., half_cols:], position, samples, sources
    )
    gathered = lax.all_to_all(twisted, "tm", 0, 0, tiled=True)
    own, far = packed_transform(gathered)
    norm_scale = 1.0 / jnp.sqrt(column_index[0].astype(jnp.float32) + 1.0)
    spectra = unpack_spectra(own, far, position, samples, norm_scale)
    inverse_psd, fold = inverse_weights(
        psd_table[0], position, devices_tm, epochs, samples, spectra.shape[1]
    )
    weighted = (spectra.astype(jnp.float32) * inverse_psd[None, :, None]).astype(jnp.bfloat16)
    weighted = weighted * fold[None, :, None].astype(jnp.bfloat16)
    contract = (((0, 1), (0, 1)), ((), ()))
    products = [
        lax.dot_general(block, weighted, contract, preferred_element_type=jnp.float32)
        for block in panel_spectra(spectra)
    ]
    by_shift = jnp.stack(products)
    panel = lax.axis_index("panel")
    rows = panels * columns // devices_tm
    if devices_tm <= 8 and columns % rows == 0:
        per_panel = columns // rows
        grid = by_shift.reshape(panels, per_panel, rows, columns)

        def block(target):
            start = ((panel - target // per_panel) % panels, target % per_panel, 0, 0)
            return lax.dynamic_slice(grid, start, (1, 1, rows, columns))[0, 0]

        total = block(position)
        for shift in range(1, devices_tm):
            pairs = [(src, (src + shift) % devices_tm) for src in range(devices_tm)]
            total = total + lax.ppermute(block((position + shift) % devices_tm), "tm", pairs)
        return comp_sum(total)
    order = (panel - jnp.arange(panels, dtype=jnp.int32)) % panels
    partial_value = jnp.take(by_shift, order, axis=0).reshape(panels * columns, columns)
    return settle_rows(partial_value)


def settle_rows(partial_value):
    devices_tm = lax.axis_size("tm")
    comps = lax.axis_size("comp")
    rows_total, columns = partial_value.shape
    rows = rows_total // devices_tm
    if comps != 2 or columns % 256 != 0 or devices_tm <= 8:
        return comp_sum(swap_blocks(partial_value.reshape(devices_tm, rows, columns), "tm", False))
    half = columns // 2
    comp = lax.axis_index("comp")
    mine = lax.dynamic_slice_in_dim(partial_value, comp * half, half, axis=1)
    theirs = lax.dynamic_slice_in_dim(partial_value, (1 - comp) * half, half, axis=1)
    summed = mine + lax.ppermute(theirs, "comp", [(0, 1), (1, 0)])
    block = swap_blocks(summed.reshape(devices_tm, rows, half), "tm", False)
    other = lax.ppermute(block, "comp", [(0, 1), (1, 0)])
    first = jnp.where(comp == 0, block, other)
    second = jnp.where(comp == 0, other, block)
    return jnp.concatenate([first, second], axis=1)


def solution(mesh):
    return jax.shard_map(
        body,
        mesh=mesh,
        in_specs=(
            P(None, ("groups", "tm")),
            P(("groups", "tm")),
            P(None, "panel"),
            P("comp", None, "panel"),
            P("comp", None),
        ),
        out_specs=P(("groups", "tm"), "panel"),
        check_vma=False,
    )
```

```python
import math

import jax
import jax.numpy as jnp
from jax import lax
from jax.sharding import PartitionSpec as P

SPLIT = 64


def rounding_error(value, factor, product):
    high = lax.reduce_precision(value, exponent_bits=8, mantissa_bits=11)
    low = value - high
    return (product - high * factor) - low * factor


def colatitude_basis(colatitude, terms):
    wavenumbers = jnp.arange(terms, dtype=jnp.float32)
    theta = colatitude[:, None]
    phases = lax.optimization_barrier(theta * wavenumbers[None, :])
    if terms % 16 != 0:
        return jnp.concatenate([jnp.cos(phases), jnp.sin(phases)], axis=1)
    groups = terms // 16
    coarse = jnp.arange(groups, dtype=jnp.float32) * 16.0
    fine = jnp.arange(16, dtype=jnp.float32)
    phase_a = lax.optimization_barrier(theta * coarse[None, :])
    phase_b = lax.optimization_barrier(theta * fine[None, :])
    count = colatitude.shape[0]
    delta = (
        rounding_error(theta, wavenumbers[None, :], phases).reshape(count, groups, 16)
        - rounding_error(theta, coarse[None, :], phase_a)[:, :, None]
        - rounding_error(theta, fine[None, :], phase_b)[:, None, :]
    )
    cos_a = jnp.cos(phase_a)[:, :, None]
    sin_a = jnp.sin(phase_a)[:, :, None]
    cos_b = jnp.cos(phase_b)[:, None, :]
    sin_b = jnp.sin(phase_b)[:, None, :]
    cos_sum = cos_a * cos_b - sin_a * sin_b
    sin_sum = sin_a * cos_b + cos_a * sin_b
    cos_k = (cos_sum - delta * sin_sum).reshape(count, terms)
    sin_k = (sin_sum + delta * cos_sum).reshape(count, terms)
    return jnp.concatenate([cos_k, sin_k], axis=1)


def synthesize(angles, keep_rows, column_index, coeffs):
    terms_lat = coeffs.shape[0] // 2
    colatitude = angles[0]
    longit = angles[1]
    basis_rows = colatitude_basis(colatitude, terms_lat).astype(jnp.bfloat16)
    degree = column_index[0]
    orders = column_index[1]
    levels = jnp.arange(2 * terms_lat, dtype=jnp.int32) % terms_lat
    allowed = levels[:, None] <= degree[None, :]
    masked = jnp.where(allowed, coeffs, jnp.zeros_like(coeffs))
    latitude = jnp.dot(basis_rows, masked, preferred_element_type=jnp.float32)
    lon_phase = longit[:, None] * jnp.abs(orders).astype(jnp.float32)[None, :]
    lon_wave = jnp.where(orders[None, :] >= 0, jnp.cos(lon_phase), jnp.sin(lon_phase))
    return latitude * lon_wave * keep_rows[:, None]


def phase_tables(row_index, col_index, length):
    product = row_index[:, None] * col_index[None, :] % length
    angle_grid = product.astype(jnp.float32) * (2.0 * math.pi / length)
    return (jnp.cos(angle_grid), jnp.sin(angle_grid))


def dft_tables(length):
    indices = jnp.arange(length, dtype=jnp.int32)
    return phase_tables(indices, indices, length)


def rotate(real_part, imag_part, outer_index, inner_index, length):
    index_grid = outer_index[:, None] * inner_index[None, :] % length
    angle_grid = index_grid.astype(jnp.float32) * (2.0 * math.pi / length)
    cosine = jnp.cos(angle_grid)[:, :, None]
    sine_grid = jnp.sin(angle_grid)[:, :, None]
    return (real_part * cosine + imag_part * sine_grid, imag_part * cosine - real_part * sine_grid)


def precise_dot(left_side, right_side):
    return jnp.dot(
        left_side, right_side, precision=lax.Precision.HIGHEST, preferred_element_type=jnp.float32
    )


def transform(cos_table, sin_table, real_part, imag_part):
    new_real = precise_dot(cos_table, real_part) + precise_dot(sin_table, imag_part)
    new_imag = precise_dot(cos_table, imag_part) - precise_dot(sin_table, real_part)
    return (new_real, new_imag)


def four_step(real_in, imag_in, samples):
    length = real_in.shape[0]
    columns = real_in.shape[1]
    outer_count = SPLIT
    inner_count = length // SPLIT
    real_part = real_in.reshape(outer_count, inner_count * columns)
    imag_part = imag_in.reshape(outer_count, inner_count * columns)
    cos_outer, sin_outer = dft_tables(outer_count)
    real_part, imag_part = transform(cos_outer, sin_outer, real_part, imag_part)
    real_part = real_part.reshape(outer_count, inner_count, columns)
    imag_part = imag_part.reshape(outer_count, inner_count, columns)
    real_part, imag_part = rotate(
        real_part,
        imag_part,
        jnp.arange(outer_count, dtype=jnp.int32),
        jnp.arange(inner_count, dtype=jnp.int32),
        length,
    )
    real_part = jnp.transpose(real_part, (1, 0, 2)).reshape(inner_count, outer_count * columns)
    imag_part = jnp.transpose(imag_part, (1, 0, 2)).reshape(inner_count, outer_count * columns)
    cos_inner, sin_inner = dft_tables(inner_count)
    real_part, imag_part = transform(cos_inner, sin_inner, real_part, imag_part)
    return (
        real_part.reshape(length, columns) / samples,
        imag_part.reshape(length, columns) / samples,
    )


def local_transform(received, samples):
    real_part, imag_part = four_step(received[0, 0], received[1, 0], samples)
    return (real_part.astype(jnp.bfloat16), imag_part.astype(jnp.bfloat16))


def inverse_weights(psd_row, position, devices_tm, epochs, samples, count):
    half = samples // 2
    mirrored = jnp.concatenate([psd_row[: half + 1], psd_row[1:half][::-1]])
    picked = lax.dynamic_slice_in_dim(mirrored.reshape(epochs, devices_tm), position, 1, axis=1)
    inverse = 8192.0 / picked[:count, 0].astype(jnp.float32)
    order = jnp.arange(count, dtype=jnp.int32)
    first = jnp.where(position == 0, 1.0, 2.0)
    middle = jnp.where(position == 0, 1.0, 0.0)
    fold = jnp.where(
        order == 0, first, jnp.where(order < epochs // 2, 2.0, jnp.where(order == epochs // 2, middle, 0.0))
    )
    return inverse, fold


def panel_spectra(spectra):
    panels = lax.axis_size("panel")
    blocks = [spectra]
    for shift in range(1, panels):
        pairs = [(src, (src + shift) % panels) for src in range(panels)]
        blocks.append(lax.ppermute(spectra, "panel", pairs))
    return blocks


def comp_sum(value):
    comps = lax.axis_size("comp")
    if comps == 1:
        return value
    if comps != 2:
        return lax.psum(value, "comp")
    other = lax.ppermute(value, "comp", [(0, 1), (1, 0)])
    return value + other


def class_partials(spread, position, samples):
    devices_tm, block_len, columns = spread.shape
    index = jnp.arange(devices_tm, dtype=jnp.int32)
    cos_table, sin_table = phase_tables(index, index, devices_tm)
    real_part = jnp.sum(cos_table[:, :, None, None] * spread[None], axis=1)
    imag_part = -jnp.sum(sin_table[:, :, None, None] * spread[None], axis=1)
    local_epoch = position * block_len + jnp.arange(block_len, dtype=jnp.int32)
    real_part, imag_part = rotate(real_part, imag_part, index, local_epoch, samples)
    return jnp.stack([real_part, imag_part], axis=1)


def class_spectrum(gathered, samples):
    devices_tm, _, block_len, columns = gathered.shape
    length = devices_tm * block_len
    index = jnp.arange(devices_tm, dtype=jnp.int32)
    cos_table, sin_table = phase_tables(index, index, devices_tm)
    real_in = gathered[:, 0]
    imag_in = gathered[:, 1]
    cos_b = cos_table[:, :, None, None]
    sin_b = sin_table[:, :, None, None]
    real_part = jnp.sum(cos_b * real_in[None] + sin_b * imag_in[None], axis=1)
    imag_part = jnp.sum(cos_b * imag_in[None] - sin_b * real_in[None], axis=1)
    real_part, imag_part = rotate(
        real_part, imag_part, index, jnp.arange(block_len, dtype=jnp.int32), length
    )
    kept = block_len // 2 + 1
    cos_inner, sin_inner = phase_tables(
        jnp.arange(kept, dtype=jnp.int32), jnp.arange(block_len, dtype=jnp.int32), block_len
    )
    dims = (((1,), (1,)), ((), ()))

    def mat(table, value):
        return lax.dot_general(
            table, value, dims, precision=lax.Precision.HIGH,
            preferred_element_type=jnp.float32,
        )

    new_real = mat(cos_inner, real_part) + mat(sin_inner, imag_part)
    new_imag = mat(cos_inner, imag_part) - mat(sin_inner, real_part)
    new_real = (new_real.reshape(kept * devices_tm, columns) / samples).astype(jnp.bfloat16)
    new_imag = (new_imag.reshape(kept * devices_tm, columns) / samples).astype(jnp.bfloat16)
    return jnp.stack([new_real, new_imag])


def swap_blocks(blocks, axis, ordered):
    count = lax.axis_size(axis)
    if count > 8:
        received = lax.all_to_all(blocks, axis, 0, 0, tiled=True)
        if ordered:
            return received, jnp.arange(count, dtype=jnp.int32)
        return jnp.sum(received, axis=0)
    me = lax.axis_index(axis)
    arrived = [lax.dynamic_index_in_dim(blocks, me, 0, keepdims=False)]
    for shift in range(1, count):
        outgoing = lax.dynamic_index_in_dim(blocks, (me + shift) % count, 0, keepdims=False)
        pairs = [(src, (src + shift) % count) for src in range(count)]
        arrived.append(lax.ppermute(outgoing, axis, pairs))
    if not ordered:
        total = arrived[0]
        for part in arrived[1:]:
            total = total + part
        return total
    return jnp.stack(arrived), (me - jnp.arange(count, dtype=jnp.int32)) % count


def packed_partials(real_in, imag_in, position, samples, sources):
    devices_tm, block_len, columns = real_in.shape
    index = jnp.arange(devices_tm, dtype=jnp.int32)
    cos_table, sin_table = phase_tables(index, sources, devices_tm)
    cos_b = cos_table[:, :, None, None]
    sin_b = sin_table[:, :, None, None]
    real_part = jnp.sum(cos_b * real_in[None] + sin_b * imag_in[None], axis=1)
    imag_part = jnp.sum(cos_b * imag_in[None] - sin_b * real_in[None], axis=1)
    local_epoch = position * block_len + jnp.arange(block_len, dtype=jnp.int32)
    real_part, imag_part = rotate(real_part, imag_part, index, local_epoch, samples)
    return jnp.stack([real_part, imag_part], axis=1)


def packed_transform(gathered):
    devices_tm, _, block_len, columns = gathered.shape
    length = devices_tm * block_len
    index = jnp.arange(devices_tm, dtype=jnp.int32)
    cos_table, sin_table = phase_tables(index, index, devices_tm)
    real_in = gathered[:, 0]
    imag_in = gathered[:, 1]
    cos_b = cos_table[:, :, None, None]
    sin_b = sin_table[:, :, None, None]
    real_part = jnp.sum(cos_b * real_in[None] + sin_b * imag_in[None], axis=1)
    imag_part = jnp.sum(cos_b * imag_in[None] - sin_b * real_in[None], axis=1)
    real_part, imag_part = rotate(
        real_part, imag_part, index, jnp.arange(block_len, dtype=jnp.int32), length
    )
    kept = block_len // 2 + 1
    rows = jnp.arange(kept, dtype=jnp.int32)
    cols = jnp.arange(block_len, dtype=jnp.int32)
    cos_own, sin_own = phase_tables(rows, cols, block_len)
    cos_far, sin_far = phase_tables(block_len - 1 - rows, cols, block_len)
    dims = (((1,), (1,)), ((), ()))

    def mat(table, value):
        return lax.dot_general(
            table, value, dims, precision=lax.Precision.HIGH,
            preferred_element_type=jnp.float32,
        )

    def apply(cos_table, sin_table, real_in, imag_in):
        table = jnp.concatenate([cos_table, sin_table], axis=0)
        from_real = mat(table, real_in)
        from_imag = mat(table, imag_in)
        new_real = from_real[:kept] + from_imag[kept:]
        new_imag = from_imag[:kept] - from_real[kept:]
        return jnp.stack([new_real, new_imag]).reshape(2, kept * devices_tm, columns)

    table = jnp.concatenate([cos_own, sin_own, cos_far, sin_far], axis=0)
    from_real = mat(table, real_part)
    from_imag = mat(table, imag_part)
    own_real = from_real[:kept] + from_imag[kept:2 * kept]
    own_imag = from_imag[:kept] - from_real[kept:2 * kept]
    far_real = from_real[2 * kept:3 * kept] + from_imag[3 * kept:]
    far_imag = from_imag[2 * kept:3 * kept] - from_real[3 * kept:]
    own = jnp.stack([own_real, own_imag]).reshape(2, kept * devices_tm, columns)
    far = jnp.stack([far_real, far_imag])[:, :, ::-1].reshape(2, kept * devices_tm, columns)
    return own, far


def unpack_spectra(own, far, position, samples, norm_scale):
    devices_tm = lax.axis_size("tm")
    shifted = jnp.concatenate([own[:, :1], far[:, :-1]], axis=1)
    outgoing = jnp.where(position == 0, shifted, far)
    pairs = [(src, (devices_tm - src) % devices_tm) for src in range(devices_tm)]
    half = own.shape[1] - devices_tm
    mirror = jnp.concatenate(
        [lax.ppermute(outgoing[:, :half], "tm", pairs), shifted[:, half:]], axis=1
    )
    own_real = own[0]
    own_imag = own[1]
    first_real = (own_real + mirror[0]) * 0.5
    first_imag = (own_imag - mirror[1]) * 0.5
    second_real = (own_imag + mirror[1]) * 0.5
    second_imag = (mirror[0] - own_real) * 0.5
    scale = norm_scale[None, :] / samples
    new_real = jnp.concatenate([first_real, second_real], axis=1) * scale
    new_imag = jnp.concatenate([first_imag, second_imag], axis=1) * scale
    return jnp.stack([new_real.astype(jnp.bfloat16), new_imag.astype(jnp.bfloat16)])


def body(orbit_angles, gap_mask, column_index, lat_coeffs, psd_table):
    devices_tm = lax.axis_size("tm")
    panels = lax.axis_size("panel")
    epochs = orbit_angles.shape[1]
    block_len = epochs // devices_tm
    samples = epochs * devices_tm
    columns = lat_coeffs.shape[2]
    coeffs = lat_coeffs[0]
    keep_rows = gap_mask.astype(jnp.float32)
    packed = jnp.concatenate([orbit_angles, keep_rows[None]], axis=0)
    packed = packed.reshape(3, devices_tm, block_len).transpose(1, 0, 2)
    received, sources = swap_blocks(packed, "tm", True)
    flat_orbit = received.transpose(1, 0, 2).reshape(3, devices_tm * block_len)
    spread = synthesize(flat_orbit[0:2], flat_orbit[2], column_index, coeffs).reshape(
        devices_tm, block_len, columns
    )
    position = lax.axis_index("tm")
    half_cols = columns // 2
    twisted = packed_partials(
        spread[..., :half_cols], spread[..., half_cols:], position, samples, sources
    )
    gathered = lax.all_to_all(twisted, "tm", 0, 0, tiled=True)
    own, far = packed_transform(gathered)
    norm_scale = 1.0 / jnp.sqrt(column_index[0].astype(jnp.float32) + 1.0)
    spectra = unpack_spectra(own, far, position, samples, norm_scale)
    inverse_psd, fold = inverse_weights(
        psd_table[0], position, devices_tm, epochs, samples, spectra.shape[1]
    )
    weighted = (spectra.astype(jnp.float32) * inverse_psd[None, :, None]).astype(jnp.bfloat16)
    weighted = weighted * fold[None, :, None].astype(jnp.bfloat16)
    contract = (((0, 1), (0, 1)), ((), ()))
    products = [
        lax.dot_general(block, weighted, contract, preferred_element_type=jnp.float32)
        for block in panel_spectra(spectra)
    ]
    by_shift = jnp.stack(products)
    panel = lax.axis_index("panel")
    rows = panels * columns // devices_tm
    if devices_tm <= 8 and columns % rows == 0:
        per_panel = columns // rows
        grid = by_shift.reshape(panels, per_panel, rows, columns)

        def block(target):
            start = ((panel - target // per_panel) % panels, target % per_panel, 0, 0)
            return lax.dynamic_slice(grid, start, (1, 1, rows, columns))[0, 0]

        total = block(position)
        for shift in range(1, devices_tm):
            pairs = [(src, (src + shift) % devices_tm) for src in range(devices_tm)]
            total = total + lax.ppermute(block((position + shift) % devices_tm), "tm", pairs)
        return comp_sum(total)
    order = (panel - jnp.arange(panels, dtype=jnp.int32)) % panels
    partial_value = jnp.take(by_shift, order, axis=0).reshape(panels * columns, columns)
    return settle_rows(partial_value)


def settle_rows(partial_value):
    devices_tm = lax.axis_size("tm")
    comps = lax.axis_size("comp")
    rows_total, columns = partial_value.shape
    rows = rows_total // devices_tm
    if comps != 2 or columns % 256 != 0 or devices_tm <= 8:
        return comp_sum(swap_blocks(partial_value.reshape(devices_tm, rows, columns), "tm", False))
    half = columns // 2
    comp = lax.axis_index("comp")
    mine = lax.dynamic_slice_in_dim(partial_value, comp * half, half, axis=1)
    theirs = lax.dynamic_slice_in_dim(partial_value, (1 - comp) * half, half, axis=1)
    summed = mine + lax.ppermute(theirs, "comp", [(0, 1), (1, 0)])
    block = swap_blocks(summed.reshape(devices_tm, rows, half), "tm", False)
    other = lax.ppermute(block, "comp", [(0, 1), (1, 0)])
    first = jnp.where(comp == 0, block, other)
    second = jnp.where(comp == 0, other, block)
    return jnp.concatenate([first, second], axis=1)


def solution(mesh):
    return jax.shard_map(
        body,
        mesh=mesh,
        in_specs=(
            P(None, ("groups", "tm")),
            P(("groups", "tm")),
            P(None, "panel"),
            P("comp", None, "panel"),
            P("comp", None),
        ),
        out_specs=P(("groups", "tm"), "panel"),
        check_vma=False,
    )
```
